32 devices in a mesh: macro: 8 (over y, x, core), work: 4 (over z).
Axes of the slice: x: 2, y: 2, z: 4, core: 2. Of those that a mesh axis runs over, the one named last changes fastest.
Arguments:
- damage: float32 [512, 4096], P(('macro', 'work')), may hold values from 0 to 0.8
- strain: float32 [512, 6, 4096], P(('macro', 'work')), may hold values from -3 to 3
- route: int32 [512], P(('macro', 'work')), may hold values from -1 to 127, as said below
- iters: int32 [512], P(('macro', 'work')), may hold values from 1 to 2
- phase: int32 [4096], replicated, may hold values 0 or 1
- moduli: float32 [2, 2], replicated, may hold values from 0.3 to 3
- tangent_old: float32 [512, 36], P(('macro', 'work')), may hold values from -6 to 6
Outputs:
- tangent: float32 [512, 36], P(('macro', 'work'))
- solved: float32 [128, 36], P(('macro', 'work'))
The draws below stay inside these ranges and needn't reach their ends.
Inputs may be any that keep to these rules, and one draw needn't show every extreme that they name: `route`: an entry is -1 for a point that keeps its tangent, or w * 4 + s for the slot s (s < 4) of the device w (numbered along macro, then work) that solves it; every value of 0 to 127 appears exactly once. For each macro index, the points of one device name at most one slot on the devices with that macro index; some devices name one slot for every macro index. Among the points of the devices with one work index, at most one names a given macro index together with a given slot number s.
All inputs are finite; a program needn't handle non-finite values.
Results may differ from the reference program's by a relative error of at most 0.0003.
Values sent between devices are 32-bit elements; how exact they have to be, the bound alone decides.
No kernel may reach another device: no remote copies, remote signals or barrier semaphores. Data moves between devices by JAX's collectives and lax.ppermute only.
A program may use at most 128 MiB of HBM per device.

```python
import math
import jax
import jax.numpy as jnp
from jax import lax

RES = 16
VOX = 4096
ITERS = 2
ACT_DEV = 4
PTS_DEV = 16
POINTS = 512
ACTIVE = 128
N_MACRO = 8
N_WORK = 4


def draw_route(key, part):
    base = jax.random.fold_in(key, 17)
    key_hot, key_class, key_group, key_local = jax.random.split(base, 4)
    hot_rows = jax.random.permutation(key_hot, N_MACRO)[:ACT_DEV].astype(jnp.int32)
    residue = (jax.random.permutation(key_class, N_MACRO) % ACT_DEV).astype(jnp.int32)
    rotation = jax.random.permutation(key_group, N_WORK).astype(jnp.int32)
    inverse_rotation = jnp.argsort(rotation).astype(jnp.int32)
    hot_ids = jnp.arange(ACT_DEV, dtype=jnp.int32)[:, None, None]
    group_ids = jnp.arange(N_WORK, dtype=jnp.int32)[None, :, None]
    target = jnp.arange(N_MACRO, dtype=jnp.int32)[None, None, :]
    slot_num = (hot_ids - residue[None, None, :]) % ACT_DEV
    worker_group = inverse_rotation[(group_ids - slot_num) % N_WORK]
    value = (target * N_WORK + worker_group) * ACT_DEV + slot_num
    owner = hot_rows[:, None] * N_WORK + jnp.arange(N_WORK, dtype=jnp.int32)[None, :]
    local_keys = jax.random.split(key_local, ACT_DEV * N_WORK)

    def first_rows(single):
        return jax.random.permutation(single, PTS_DEV)[:N_MACRO].astype(jnp.int32)
    local = jax.vmap(first_rows)(local_keys).reshape(ACT_DEV, N_WORK, N_MACRO)
    position = owner[:, :, None] * PTS_DEV + local
    empty = jnp.full((PTS_DEV * N_MACRO * N_WORK,), -1, jnp.int32)
    return empty.at[position.reshape(-1)].set(value.reshape(-1).astype(jnp.int32))


def with_ends(values, own_key, smallest, high):
    dims = values.shape
    index_at = [jax.random.randint(jax.random.fold_in(own_key, axis), (), 0, dims[axis]) for axis in range(len(dims))]
    values = values.at[tuple(index_at)].set(smallest)
    longest = dims.index(max(dims))
    index_at[longest] = (index_at[longest] + 1) % dims[longest]
    return values.at[tuple(index_at)].set(high)


def block_levels(own_key, extent, pieces, least, top_value):
    def one(dim, shards_of):
        heights = jax.random.uniform(jax.random.fold_in(jax.random.fold_in(own_key, 6), dim), (shards_of,), jnp.float32, least / len(pieces), top_value / len(pieces))
        return jnp.repeat(jnp.exp(heights), extent[dim] // shards_of).reshape((-1,) + (1,) * (len(extent) - dim - 1))

    factor_of = one(*pieces[0])
    for cut in pieces[1:]:
        factor_of = factor_of * one(*cut)
    return factor_of


def scatter_about(key, shape, width, most, shards=(), held_as=jnp.bfloat16):
    values = width * jax.random.normal(key, shape, jnp.float32)
    if shards:
        values = values * block_levels(key, shape, shards, -0.22, 0.18)
    return jnp.clip(values, -most, most).astype(held_as)


def setup_inputs(seed: int = 0) -> dict:
    arg_keys = jax.random.split(jax.random.key(seed), 8)
    damage = jnp.clip(0.8 * jax.random.uniform(arg_keys[0], (POINTS, VOX), jnp.float32) ** block_levels(arg_keys[0], (POINTS, VOX), ((0, 32),), -0.2, 0.2), 0.0, 0.8)
    strain = scatter_about(arg_keys[1], (POINTS, 6, VOX), 0.5, 3.0, ((0, 32),), jnp.float32)
    route = draw_route(jax.random.fold_in(arg_keys[7], 71), 0)
    iters = with_ends(jax.random.randint(arg_keys[3], (POINTS,), 1, ITERS + 1), jax.random.fold_in(arg_keys[3], 1), 1, ITERS).astype(jnp.int32)
    phase = with_ends((jax.random.randint(arg_keys[4], (VOX,), 0, 5) < 2).astype(jnp.int32), jax.random.fold_in(arg_keys[4], 1), 0, 1)
    moduli = jnp.clip(jnp.exp(jax.random.uniform(arg_keys[5], (2, 2), jnp.float32, math.log(0.3), math.log(3.0))), 0.3, 3.0)
    tangent_old = scatter_about(arg_keys[6], (POINTS, 36), 1.0, 6.0, ((0, 32),), jnp.float32)
    return {"damage": damage, "strain": strain, "route": route, "iters": iters, "phase": phase, "moduli": moduli, "tangent_old": tangent_old}


def moduli_field(phase, moduli):
    first = jnp.where(phase == 1, moduli[1, 0], moduli[0, 0])
    shear = jnp.where(phase == 1, moduli[1, 1], moduli[0, 1])
    return first, shear


def elastic(field, first, shear):
    trace = field[0] + field[1] + field[2]
    parts = [2.0 * shear * field[c] + first * trace for c in range(3)]
    parts = parts + [2.0 * shear * field[c] for c in range(3, 6)]
    return jnp.stack(parts)


def contract(left, right):
    diagonal = left[0] * right[0] + left[1] * right[1] + left[2] * right[2]
    return diagonal + 2.0 * (left[3] * right[3] + left[4] * right[4] + left[5] * right[5])


def tangent_apply(field, first, shear, keep, state, state_norm):
    weight = keep * shear * contract(field, state) / (1.0 + state_norm)
    return keep * elastic(field, first, shear) - weight * state


def green(part, first0, shear0, wave_a, wave_b, wave_c):
    norm = wave_a * wave_a + wave_b * wave_b + wave_c * wave_c
    safe = jnp.where(norm > 0, norm, 1.0)
    living = jnp.where(norm > 0, 1.0, 0.0)
    force_a = part[0] * wave_a + part[5] * wave_b + part[4] * wave_c
    force_b = part[5] * wave_a + part[1] * wave_b + part[3] * wave_c
    force_c = part[4] * wave_a + part[3] * wave_b + part[2] * wave_c
    kappa = (first0 + shear0) / (shear0 * (first0 + 2.0 * shear0))
    along = (wave_a * force_a + wave_b * force_b + wave_c * force_c) * kappa / (safe * safe)
    factor = 0.5 / (shear0 * safe)
    parts = [
        factor * 2.0 * wave_a * force_a - along * wave_a * wave_a,
        factor * 2.0 * wave_b * force_b - along * wave_b * wave_b,
        factor * 2.0 * wave_c * force_c - along * wave_c * wave_c,
        factor * (wave_c * force_b + wave_b * force_c) - along * wave_b * wave_c,
        factor * (wave_c * force_a + wave_a * force_c) - along * wave_a * wave_c,
        factor * (wave_b * force_a + wave_a * force_b) - along * wave_a * wave_b,
    ]
    return jnp.stack(parts) * living


def signed_waves(edge):
    index = jnp.arange(edge)
    return jnp.where(index < edge // 2, index, index - edge).astype(jnp.float32)


def unit_columns():
    index = jnp.arange(6)
    values = jnp.where(index[:, None] == index[None, :], jnp.where(index[:, None] < 3, 1.0, 0.5), 0.0)
    return values.astype(jnp.float32)


def reference(damage, strain, route, iters, phase, moduli, tangent_old):
    first, shear = moduli_field(phase, moduli)
    first0 = jnp.mean(moduli[:, 0])
    shear0 = jnp.mean(moduli[:, 1])
    waves = signed_waves(RES)
    wave_a = waves[:, None, None]
    wave_b = waves[None, :, None]
    wave_c = waves[None, None, :]
    columns = unit_columns()[:, :, None]
    chosen = jnp.nonzero(route >= 0, size=ACTIVE, fill_value=0)[0].astype(jnp.int32)

    def solve_one(index):
        keep = 1.0 - damage[index]
        state = elastic(strain[index][:, None, :], first, shear)
        state_norm = contract(state, state)
        count = iters[index]
        field = jnp.broadcast_to(columns, (6, 6, VOX)).astype(jnp.float32)
        for step in range(ITERS):
            polar = tangent_apply(field, first, shear, keep, state, state_norm) - elastic(field, first0, shear0)
            spectrum = jnp.fft.fftn(polar.reshape(6, 6, RES, RES, RES), axes=(2, 3, 4))
            real_part = green(spectrum.real, first0, shear0, wave_a, wave_b, wave_c)
            imag_part = green(spectrum.imag, first0, shear0, wave_a, wave_b, wave_c)
            back = jnp.fft.ifftn(real_part + 1j * imag_part, axes=(2, 3, 4)).real.reshape(6, 6, VOX)
            field = jnp.where(step < count, columns - back, field)
        stress = tangent_apply(field, first, shear, keep, state, state_norm)
        return jnp.mean(stress, axis=-1).reshape(36)

    solved = lax.map(solve_one, chosen)
    tangent = tangent_old.at[chosen].set(solved)
    slot_rows = route[chosen].astype(jnp.int32)
    by_slot = jnp.zeros((ACTIVE, 36), solved.dtype).at[slot_rows].set(solved)
    return tangent, by_slot
```

```python
import numpy as np
import jax
import jax.numpy as jnp
from jax import lax
from jax.sharding import PartitionSpec as P

RES = 16
ITERS = 2
ACT_DEV = 4

exact = lax.Precision.HIGHEST
fast = lax.Precision.HIGH


def moduli_field(phase, moduli):
    first = jnp.where(phase == 1, moduli[1, 0], moduli[0, 0])
    shear = jnp.where(phase == 1, moduli[1, 1], moduli[0, 1])
    return (first, shear)


def elastic(field, first, shear):
    trace = field[0] + field[1] + field[2]
    parts = [2.0 * shear * field[c] + first * trace for c in range(3)]
    parts = parts + [2.0 * shear * field[c] for c in range(3, 6)]
    return jnp.stack(parts)


def contract(left, right):
    diagonal = left[0] * right[0] + left[1] * right[1] + left[2] * right[2]
    return diagonal + 2.0 * (left[3] * right[3] + left[4] * right[4] + left[5] * right[5])


def green(part, first0, shear0, wave_a, wave_b, wave_c):
    norm = wave_a * wave_a + wave_b * wave_b + wave_c * wave_c
    safe = jnp.where(norm > 0, norm, 1.0)
    living = jnp.where(norm > 0, 1.0, 0.0)
    force_a = part[0] * wave_a + part[5] * wave_b + part[4] * wave_c
    force_b = part[5] * wave_a + part[1] * wave_b + part[3] * wave_c
    force_c = part[4] * wave_a + part[3] * wave_b + part[2] * wave_c
    kappa = (first0 + shear0) / (shear0 * (first0 + 2.0 * shear0))
    along = (wave_a * force_a + wave_b * force_b + wave_c * force_c) * kappa / (safe * safe)
    factor = 0.5 / (shear0 * safe)
    parts = [
        factor * 2.0 * wave_a * force_a - along * wave_a * wave_a,
        factor * 2.0 * wave_b * force_b - along * wave_b * wave_b,
        factor * 2.0 * wave_c * force_c - along * wave_c * wave_c,
        factor * (wave_c * force_b + wave_b * force_c) - along * wave_b * wave_c,
        factor * (wave_c * force_a + wave_a * force_c) - along * wave_a * wave_c,
        factor * (wave_b * force_a + wave_a * force_b) - along * wave_a * wave_b,
    ]
    return jnp.stack(parts) * living


def fourier_tables(edge):
    line = np.arange(edge)
    angle_one = (np.outer(line, line) % edge) * (2.0 * np.pi / edge)
    flat = np.arange(edge * edge)
    rows, cols = flat // edge, flat % edge
    angle_two = (np.outer(rows, rows) + np.outer(cols, cols)) % edge
    angle_two = angle_two * (2.0 * np.pi / edge)
    volume = float(edge ** 3)
    return dict(
        cos_one=np.cos(angle_one).astype(np.float32),
        sin_one=np.sin(angle_one).astype(np.float32),
        cos_two=np.cos(angle_two).astype(np.float32),
        nsin_two=(-np.sin(angle_two)).astype(np.float32),
        icos_two=(np.cos(angle_two) / volume).astype(np.float32),
        insin_two=(-np.sin(angle_two) / volume).astype(np.float32),
    )


def along_first(mat, x):
    lead = x.shape[0]
    return jnp.matmul(mat, x.reshape(lead, -1), precision=fast).reshape(x.shape)


def forward(x, tables):
    part_re = jnp.matmul(x, tables["cos_two"], precision=fast)
    part_im = jnp.matmul(x, tables["nsin_two"], precision=fast)
    cos_one, sin_one = tables["cos_one"], tables["sin_one"]
    spec_re = along_first(cos_one, part_re) + along_first(sin_one, part_im)
    spec_im = along_first(cos_one, part_im) - along_first(sin_one, part_re)
    return spec_re, spec_im


def inverse_real(spec_re, spec_im, tables):
    cos_one, sin_one = tables["cos_one"], tables["sin_one"]
    part_re = along_first(cos_one, spec_re) - along_first(sin_one, spec_im)
    part_im = along_first(sin_one, spec_re) + along_first(cos_one, spec_im)
    return jnp.matmul(part_re, tables["icos_two"], precision=fast) + jnp.matmul(
        part_im, tables["insin_two"], precision=fast
    )


def pair_index():
    order = {}
    for i in range(6):
        for l in range(i, 6):
            order[(i, l)] = len(order)
    return {(i, l): order[(min(i, l), max(i, l))] for i in range(6) for l in range(6)}


def solve_local(damage_v, strain_v, count_v, phase, moduli):
    edge = RES
    plane = edge * edge
    vols = damage_v.shape[0]
    voxels = edge * plane
    tables = {k: jnp.asarray(v) for k, v in fourier_tables(edge).items()}
    first, shear = moduli_field(phase.reshape(edge, 1, plane), moduli)
    first0 = jnp.mean(moduli[:, 0])
    shear0 = jnp.mean(moduli[:, 1])
    weights = [1.0, 1.0, 1.0, 2.0, 2.0, 2.0]
    unit = [1.0, 1.0, 1.0, 0.5, 0.5, 0.5]
    pairs = pair_index()

    keep = jnp.transpose((1.0 - damage_v).reshape(vols, edge, plane), (1, 0, 2))
    strain_t = jnp.transpose(strain_v.reshape(vols, 6, edge, plane), (1, 2, 0, 3))
    state = elastic(strain_t, first, shear)
    state = jnp.transpose(state, (1, 0, 2, 3))
    s = [state[:, i] for i in range(6)]
    norm = contract(s, s)
    gain = keep * shear / (1.0 + norm)
    kfirst = keep * first
    kshear = keep * shear
    prods = []
    for i in range(6):
        for l in range(i, 6):
            prods.append(gain * s[i] * s[l])
    coef = jnp.stack([kfirst, kshear] + prods, axis=1)
    coef_mean = jnp.sum(coef, axis=(0, 3)) / voxels
    coef_re, coef_im = forward(coef, tables)

    def a_entry(spec, i, l):
        value = -weights[l] * spec[:, 2 + pairs[(i, l)]]
        if i == l:
            value = value + 2.0 * spec[:, 1]
        if i < 3 and l < 3:
            value = value + spec[:, 0]
        return value

    waves = np.where(np.arange(edge) < edge // 2, np.arange(edge), np.arange(edge) - edge).astype(np.float32)
    flat = np.arange(plane)
    wave_a = jnp.asarray(waves.reshape(edge, 1, 1, 1))
    wave_b = jnp.asarray(waves[flat // edge])
    wave_c = jnp.asarray(waves[flat % edge])

    def apply_green(spec):
        parts = [spec[:, c] for c in range(6)]
        out = green(parts, first0, shear0, wave_a, wave_b, wave_c)
        return jnp.transpose(out, (1, 0, 2, 3, 4))

    def tau_zero(spec):
        cols = []
        for c in range(6):
            cols.append(jnp.stack([unit[j] * a_entry(spec, c, j) for j in range(6)], axis=1))
        return jnp.stack(cols, axis=1)

    g1_re = apply_green(tau_zero(coef_re))
    g1_im = apply_green(tau_zero(coef_im))

    h1 = inverse_real(g1_re, g1_im, tables)
    columns = np.zeros((6, 6), np.float32)
    for j in range(6):
        columns[j, j] = unit[j]
    e1 = jnp.asarray(columns).reshape(1, 6, 6, 1, 1) - h1
    e = [e1[:, c] for c in range(6)]
    trace = e[0] + e[1] + e[2]
    dot_se = contract([x[:, None] for x in s], e)
    wk = gain[:, None] * dot_se
    tau1 = []
    for c in range(6):
        value = 2.0 * kshear[:, None] * e[c] - wk * s[c][:, None] - 2.0 * shear0 * e[c]
        if c < 3:
            value = value + (kfirst[:, None] - first0) * trace
        tau1.append(value)
    tau1 = jnp.stack(tau1, axis=1)
    t1_re, t1_im = forward(tau1, tables)
    g2_re = apply_green(t1_re)
    g2_im = apply_green(t1_im)

    count = count_v.reshape(1, 1, 1, vols, 1)
    gf_re = jnp.where(count >= 2, g2_re, jnp.where(count >= 1, g1_re, 0.0))
    gf_im = jnp.where(count >= 2, g2_im, jnp.where(count >= 1, g1_im, 0.0))

    scale = 1.0 / (float(voxels) * float(voxels))
    amat_re = jnp.stack([jnp.stack([a_entry(coef_re, i, l) for l in range(6)], axis=1) for i in range(6)], axis=1)
    amat_im = jnp.stack([jnp.stack([a_entry(coef_im, i, l) for l in range(6)], axis=1) for i in range(6)], axis=1)
    mean_ah = jnp.einsum("kilvn,kljvn->vij", amat_re, gf_re, precision=exact)
    mean_ah = mean_ah + jnp.einsum("kilvn,kljvn->vij", amat_im, gf_im, precision=exact)
    mean_ah = mean_ah * scale

    def mean_entry(i, l):
        value = -weights[l] * coef_mean[2 + pairs[(i, l)]]
        if i == l:
            value = value + 2.0 * coef_mean[1]
        if i < 3 and l < 3:
            value = value + coef_mean[0]
        return value

    mean_a = jnp.stack([jnp.stack([unit[j] * mean_entry(i, j) for j in range(6)], axis=-1) for i in range(6)], axis=-2)
    result = mean_a - mean_ah
    return result.reshape(vols, 36)


def body(damage, strain, route, iters, phase, moduli, tangent_old):
    slots = ACT_DEV
    macro_count = lax.axis_size("macro")
    work_count = lax.axis_size("work")
    me = lax.axis_index("macro") * work_count + lax.axis_index("work")
    points = route.shape[0]
    vols = min(points, macro_count)
    active = route >= 0
    rank = jnp.cumsum(active.astype(jnp.int32)) - 1
    vol_ids = jnp.arange(vols, dtype=jnp.int32)
    select = (active[None, :] & (rank[None, :] == vol_ids[:, None])).astype(jnp.float32)
    damage_v = jnp.dot(select, damage, precision=exact)
    strain_v = jnp.einsum("vp,pcn->vcn", select, strain, precision=exact)
    count_v = jnp.dot(select, iters.astype(jnp.float32), precision=exact)
    route_v = jnp.dot(select, route.astype(jnp.float32) + 1.0, precision=exact) - 1.0
    solved_v = solve_local(damage_v, strain_v, count_v, phase, moduli)
    mine = jnp.dot(select.T, solved_v, precision=exact)
    tangent = jnp.where(active[:, None], mine, tangent_old)
    packed = jnp.concatenate([solved_v, route_v[:, None]], axis=1)
    everyone = lax.all_gather(packed, ("macro", "work"), axis=0, tiled=True)
    wanted = (me * slots + jnp.arange(slots, dtype=jnp.int32)).astype(jnp.float32)
    pick = (everyone[None, :, 36] == wanted[:, None]).astype(jnp.float32)
    solved = jnp.dot(pick, everyone[:, :36], precision=exact)
    return (tangent, solved)


def solution(mesh):
    return jax.shard_map(
        body,
        mesh=mesh,
        in_specs=(
            P(("macro", "work"), None),
            P(("macro", "work"), None, None),
            P(("macro", "work")),
            P(("macro", "work")),
            P(),
            P(),
            P(("macro", "work"), None),
        ),
        out_specs=(P(("macro", "work"), None), P(("macro", "work"), None)),
        check_vma=False,
    )
```

```python
import numpy as np
import jax
import jax.numpy as jnp
from jax import lax
from jax.sharding import PartitionSpec as P

RES = 16
ITERS = 2
ACT_DEV = 4

exact = lax.Precision.HIGHEST
fast = lax.Precision.HIGH


def moduli_field(phase, moduli):
    first = jnp.where(phase == 1, moduli[1, 0], moduli[0, 0])
    shear = jnp.where(phase == 1, moduli[1, 1], moduli[0, 1])
    return (first, shear)


def elastic(field, first, shear):
    trace = field[0] + field[1] + field[2]
    parts = [2.0 * shear * field[c] + first * trace for c in range(3)]
    parts = parts + [2.0 * shear * field[c] for c in range(3, 6)]
    return jnp.stack(parts)


def contract(left, right):
    diagonal = left[0] * right[0] + left[1] * right[1] + left[2] * right[2]
    return diagonal + 2.0 * (left[3] * right[3] + left[4] * right[4] + left[5] * right[5])


def green(part, first0, shear0, wave_a, wave_b, wave_c):
    norm = wave_a * wave_a + wave_b * wave_b + wave_c * wave_c
    safe = jnp.where(norm > 0, norm, 1.0)
    living = jnp.where(norm > 0, 1.0, 0.0)
    force_a = part[0] * wave_a + part[5] * wave_b + part[4] * wave_c
    force_b = part[5] * wave_a + part[1] * wave_b + part[3] * wave_c
    force_c = part[4] * wave_a + part[3] * wave_b + part[2] * wave_c
    kappa = (first0 + shear0) / (shear0 * (first0 + 2.0 * shear0))
    along = (wave_a * force_a + wave_b * force_b + wave_c * force_c) * kappa / (safe * safe)
    factor = 0.5 / (shear0 * safe)
    parts = [
        factor * 2.0 * wave_a * force_a - along * wave_a * wave_a,
        factor * 2.0 * wave_b * force_b - along * wave_b * wave_b,
        factor * 2.0 * wave_c * force_c - along * wave_c * wave_c,
        factor * (wave_c * force_b + wave_b * force_c) - along * wave_b * wave_c,
        factor * (wave_c * force_a + wave_a * force_c) - along * wave_a * wave_c,
        factor * (wave_b * force_a + wave_a * force_b) - along * wave_a * wave_b,
    ]
    return jnp.stack(parts) * living


def fourier_tables(edge):
    line = np.arange(edge)
    angle_one = (np.outer(line, line) % edge) * (2.0 * np.pi / edge)
    flat = np.arange(edge * edge)
    rows, cols = flat // edge, flat % edge
    angle_two = (np.outer(rows, rows) + np.outer(cols, cols)) % edge
    angle_two = angle_two * (2.0 * np.pi / edge)
    volume = float(edge ** 3)
    return dict(
        cos_one=np.cos(angle_one).astype(np.float32),
        sin_one=np.sin(angle_one).astype(np.float32),
        cos_two=np.cos(angle_two).astype(np.float32),
        nsin_two=(-np.sin(angle_two)).astype(np.float32),
        icos_two=(np.cos(angle_two) / volume).astype(np.float32),
        insin_two=(-np.sin(angle_two) / volume).astype(np.float32),
    )


def along_first(mat, x):
    lead = x.shape[0]
    flat = x.reshape(lead, x.shape[1], -1)
    batch = jnp.broadcast_to(mat, (lead,) + mat.shape)
    out = lax.dot_general(batch, flat, (((2,), (1,)), ((0,), (0,))), precision=fast)
    return out.reshape(x.shape)


def forward(x, tables):
    part_re = jnp.matmul(x, tables["cos_two"], precision=fast)
    part_im = jnp.matmul(x, tables["nsin_two"], precision=fast)
    cos_one, sin_one = tables["cos_one"], tables["sin_one"]
    spec_re = along_first(cos_one, part_re) + along_first(sin_one, part_im)
    spec_im = along_first(cos_one, part_im) - along_first(sin_one, part_re)
    return spec_re, spec_im


def inverse_real(spec_re, spec_im, tables):
    cos_one, sin_one = tables["cos_one"], tables["sin_one"]
    part_re = along_first(cos_one, spec_re) - along_first(sin_one, spec_im)
    part_im = along_first(sin_one, spec_re) + along_first(cos_one, spec_im)
    return jnp.matmul(part_re, tables["icos_two"], precision=fast) + jnp.matmul(
        part_im, tables["insin_two"], precision=fast
    )


def tangent_apply(field, first, shear, keep, state, gain):
    weight = gain * contract(field, state)
    return keep * elastic(field, first, shear) - weight * state


def solve_local(damage_v, strain_v, count_v, phase, moduli):
    edge = RES
    plane = edge * edge
    vols = damage_v.shape[0]
    voxels = edge * plane
    tables = {k: jnp.asarray(v) for k, v in fourier_tables(edge).items()}
    first, shear = moduli_field(phase.reshape(edge, 1, 1, plane), moduli)
    first0 = jnp.mean(moduli[:, 0])
    shear0 = jnp.mean(moduli[:, 1])
    keep = jnp.transpose((1.0 - damage_v).reshape(vols, edge, plane), (1, 0, 2))[:, None]
    strain_t = jnp.transpose(strain_v.reshape(vols, 6, edge, plane), (1, 2, 0, 3))[:, :, None]
    state = elastic(strain_t, first, shear)
    gain = keep * shear / (1.0 + contract(state, state))
    waves = np.where(np.arange(edge) < edge // 2, np.arange(edge), np.arange(edge) - edge).astype(np.float32)
    flat = np.arange(plane)
    wave_a = jnp.asarray(waves.reshape(edge, 1, 1, 1))
    wave_b = jnp.asarray(waves[flat // edge])
    wave_c = jnp.asarray(waves[flat % edge])
    unit = np.zeros((6, 1, 6, 1, 1), np.float32)
    for j in range(6):
        unit[j, 0, j] = 1.0 if j < 3 else 0.5
    macro_field = jnp.asarray(unit)
    field = jnp.broadcast_to(macro_field, (6, edge, 6, vols, plane))
    count = count_v.reshape(1, 1, 1, vols, 1)
    for step in range(ITERS):
        polar = tangent_apply(field, first, shear, keep, state, gain) - elastic(field, first0, shear0)
        spec_re, spec_im = forward(polar, tables)
        g_re = green(spec_re, first0, shear0, wave_a, wave_b, wave_c)
        g_im = green(spec_im, first0, shear0, wave_a, wave_b, wave_c)
        back = inverse_real(g_re, g_im, tables)
        field = jnp.where(step < count, macro_field - back, field)
    stress = tangent_apply(field, first, shear, keep, state, gain)
    means = jnp.sum(stress, axis=(1, 4)) / voxels
    return jnp.transpose(means, (2, 0, 1)).reshape(vols, 36)


def body(damage, strain, route, iters, phase, moduli, tangent_old):
    slots = ACT_DEV
    macro_count = lax.axis_size("macro")
    work_count = lax.axis_size("work")
    devices = macro_count * work_count
    points = route.shape[0]
    vols = min(points, macro_count)
    active = route >= 0
    rank = jnp.cumsum(active.astype(jnp.int32)) - 1
    vol_ids = jnp.arange(vols, dtype=jnp.int32)
    select = (active[None, :] & (rank[None, :] == vol_ids[:, None])).astype(jnp.float32)
    damage_v = jnp.dot(select, damage, precision=exact)
    strain_v = jnp.einsum("vp,pcn->vcn", select, strain, precision=exact)
    count_v = jnp.dot(select, iters.astype(jnp.float32), precision=exact)
    route_v = jnp.dot(select, route.astype(jnp.float32) + 1.0, precision=exact) - 1.0
    solved_v = solve_local(damage_v, strain_v, count_v, phase, moduli)
    mine = jnp.dot(select.T, solved_v, precision=exact)
    tangent = jnp.where(active[:, None], mine, tangent_old)
    route_i = route_v.astype(jnp.int32)
    dest_ids = jnp.arange(devices, dtype=jnp.int32)
    to_dest = ((route_i[None, :] >= 0) & (route_i[None, :] // slots == dest_ids[:, None])).astype(jnp.float32)
    slot_tag = jnp.where(route_i >= 0, route_i % slots + 1, 0).astype(jnp.float32)
    packed = jnp.concatenate([solved_v, slot_tag[:, None]], axis=1)
    outgoing = jnp.dot(to_dest, packed, precision=exact)
    arrived = lax.all_to_all(outgoing, ("macro", "work"), 0, 0, tiled=True)
    slot_ids = jnp.arange(slots, dtype=jnp.float32) + 1.0
    pick = (arrived[None, :, 36] == slot_ids[:, None]).astype(jnp.float32)
    solved = jnp.dot(pick, arrived[:, :36], precision=exact)
    return (tangent, solved)


def solution(mesh):
    return jax.shard_map(
        body,
        mesh=mesh,
        in_specs=(
            P(("macro", "work"), None),
            P(("macro", "work"), None, None),
            P(("macro", "work")),
            P(("macro", "work")),
            P(),
            P(),
            P(("macro", "work"), None),
        ),
        out_specs=(P(("macro", "work"), None), P(("macro", "work"), None)),
        check_vma=False,
    )
```

```python
import numpy as np
import jax
import jax.numpy as jnp
from jax import lax
from jax.sharding import PartitionSpec as P

RES = 16
ITERS = 2
ACT_DEV = 4

exact = lax.Precision.HIGHEST
fast = lax.Precision.HIGH


def moduli_field(phase, moduli):
    first = jnp.where(phase == 1, moduli[1, 0], moduli[0, 0])
    shear = jnp.where(phase == 1, moduli[1, 1], moduli[0, 1])
    return (first, shear)


def elastic(field, first, shear):
    trace = field[0] + field[1] + field[2]
    parts = [2.0 * shear * field[c] + first * trace for c in range(3)]
    parts = parts + [2.0 * shear * field[c] for c in range(3, 6)]
    return jnp.stack(parts)


def contract(left, right):
    diagonal = left[0] * right[0] + left[1] * right[1] + left[2] * right[2]
    return diagonal + 2.0 * (left[3] * right[3] + left[4] * right[4] + left[5] * right[5])


def green(part, first0, shear0, wave_a, wave_b, wave_c):
    norm = wave_a * wave_a + wave_b * wave_b + wave_c * wave_c
    safe = jnp.where(norm > 0, norm, 1.0)
    living = jnp.where(norm > 0, 1.0, 0.0)
    force_a = part[0] * wave_a + part[5] * wave_b + part[4] * wave_c
    force_b = part[5] * wave_a + part[1] * wave_b + part[3] * wave_c
    force_c = part[4] * wave_a + part[3] * wave_b + part[2] * wave_c
    kappa = (first0 + shear0) / (shear0 * (first0 + 2.0 * shear0))
    along = (wave_a * force_a + wave_b * force_b + wave_c * force_c) * kappa / (safe * safe)
    factor = 0.5 / (shear0 * safe)
    parts = [
        factor * 2.0 * wave_a * force_a - along * wave_a * wave_a,
        factor * 2.0 * wave_b * force_b - along * wave_b * wave_b,
        factor * 2.0 * wave_c * force_c - along * wave_c * wave_c,
        factor * (wave_c * force_b + wave_b * force_c) - along * wave_b * wave_c,
        factor * (wave_c * force_a + wave_a * force_c) - along * wave_a * wave_c,
        factor * (wave_b * force_a + wave_a * force_b) - along * wave_a * wave_b,
    ]
    return jnp.stack(parts) * living


def fourier_tables(edge):
    line = np.arange(edge)
    angle_one = (np.outer(line, line) % edge) * (2.0 * np.pi / edge)
    flat = np.arange(edge * edge)
    rows, cols = flat // edge, flat % edge
    angle_two = (np.outer(rows, rows) + np.outer(cols, cols)) % edge
    angle_two = angle_two * (2.0 * np.pi / edge)
    volume = float(edge ** 3)
    return dict(
        cos_one=np.cos(angle_one).astype(np.float32),
        sin_one=np.sin(angle_one).astype(np.float32),
        cos_two=np.cos(angle_two).astype(np.float32),
        nsin_two=(-np.sin(angle_two)).astype(np.float32),
        icos_two=(np.cos(angle_two) / volume).astype(np.float32),
        insin_two=(-np.sin(angle_two) / volume).astype(np.float32),
    )


def forward(field, tables):
    cos_one, sin_one, cos_two, nsin_two = tables[:4]
    real_one = jnp.einsum("ka,...al->...kl", cos_one, field, precision=fast)
    imag_one = -jnp.einsum("ka,...al->...kl", sin_one, field, precision=fast)
    real_two = jnp.matmul(real_one, cos_two, precision=fast) - jnp.matmul(
        imag_one, nsin_two, precision=fast
    )
    imag_two = jnp.matmul(imag_one, cos_two, precision=fast) + jnp.matmul(
        real_one, nsin_two, precision=fast
    )
    return (real_two, imag_two)


def inverse(real_two, imag_two, tables):
    cos_one, sin_one, cos_two, nsin_two = tables[:4]
    real_one = jnp.matmul(real_two, cos_two, precision=fast) + jnp.matmul(
        imag_two, nsin_two, precision=fast
    )
    imag_one = jnp.matmul(imag_two, cos_two, precision=fast) - jnp.matmul(
        real_two, nsin_two, precision=fast
    )
    total = jnp.einsum("ka,...kl->...al", cos_one, real_one, precision=fast)
    total = total - jnp.einsum("ka,...kl->...al", sin_one, imag_one, precision=fast)
    return total / (cos_one.shape[0] * cos_two.shape[0])


def tangent_apply(field, first, shear, keep, state, state_norm):
    weight = keep * shear * contract(field, state) / (1.0 + state_norm)
    return keep * elastic(field, first, shear) - weight * state


def signed_waves(index, edge):
    return jnp.where(index < edge // 2, index, index - edge).astype(jnp.float32)


def unit_columns():
    index = jnp.arange(6)
    values = jnp.where(
        index[:, None] == index[None, :], jnp.where(index[:, None] < 3, 1.0, 0.5), 0.0
    )
    return values.astype(jnp.float32)


def solve_slots(held_damage, held_strain, held_count, phase, moduli):
    edge = RES
    plane = edge * edge
    slots = held_damage.shape[0]
    first, shear = moduli_field(phase.reshape(edge, plane), moduli)
    first0 = jnp.mean(moduli[:, 0])
    shear0 = jnp.mean(moduli[:, 1])
    keep = (1.0 - held_damage).reshape(slots, 1, edge, plane)
    state_strain = jnp.transpose(held_strain.reshape(slots, 6, edge, plane), (1, 0, 2, 3))[
        :, :, None
    ]
    state = elastic(state_strain, first, shear)
    state_norm = contract(state, state)
    flat = jnp.arange(plane, dtype=jnp.int32)
    wave_a = signed_waves(jnp.arange(edge, dtype=jnp.int32), edge)[:, None]
    wave_b = signed_waves(flat // edge, edge)[None, :]
    wave_c = signed_waves(flat % edge, edge)[None, :]
    table = fourier_tables(edge)
    tables = tuple(jnp.asarray(table[k]) for k in ("cos_one", "sin_one", "cos_two", "nsin_two"))
    macro_field = unit_columns()[:, None, :, None, None]
    field = jnp.broadcast_to(macro_field, (6, slots, 6, edge, plane))
    count = held_count[:, None, None, None]
    for step in range(ITERS):
        polar = tangent_apply(field, first, shear, keep, state, state_norm) - elastic(
            field, first0, shear0
        )
        real_part, imag_part = forward(polar, tables)
        real_part = green(real_part, first0, shear0, wave_a, wave_b, wave_c)
        imag_part = green(imag_part, first0, shear0, wave_a, wave_b, wave_c)
        back = inverse(real_part, imag_part, tables)
        field = jnp.where(step < count, macro_field - back, field)
    stress = tangent_apply(field, first, shear, keep, state, state_norm)
    means = jnp.sum(stress, axis=(3, 4)) / (edge * plane)
    return jnp.transpose(means, (1, 0, 2)).reshape(slots, 36)


def body(damage, strain, route, iters, phase, moduli, tangent_old):
    slots = ACT_DEV
    macro_count = lax.axis_size("macro")
    work_count = lax.axis_size("work")
    devices = macro_count * work_count
    my_macro = lax.axis_index("macro")
    my_work = lax.axis_index("work")
    points, voxels = damage.shape
    width = 7 * voxels
    active = route >= 0
    dest_macro = jnp.where(active, route // slots // work_count, -1)
    macro_ids = jnp.arange(macro_count, dtype=jnp.int32)
    to_macro = (dest_macro[None, :] == macro_ids[:, None]).astype(jnp.float32)
    meta = jnp.zeros((points, 128), jnp.float32)
    meta = meta.at[:, 0].set(route.astype(jnp.float32) + 1.0)
    meta = meta.at[:, 1].set(iters.astype(jnp.float32))
    meta = meta.at[:, 2].set(jnp.arange(points, dtype=jnp.float32) + 1.0)
    source = jnp.concatenate([damage, strain.reshape(points, 6 * voxels), meta], axis=1)
    outgoing = jnp.dot(to_macro, source, precision=exact)
    arrived = lax.all_to_all(outgoing, "macro", 0, 0, tiled=True)
    valid = arrived[:, width] > 0.5
    rank = jnp.cumsum(valid.astype(jnp.int32)) - 1
    vol_ids = jnp.arange(slots, dtype=jnp.int32)
    select = (valid[None, :] & (rank[None, :] == vol_ids[:, None])).astype(jnp.float32)
    held = jnp.dot(select, arrived, precision=exact)
    held_valid = jnp.sum(select, axis=1) > 0.5
    held_route = (held[:, width] - 1.0).astype(jnp.int32)
    held_count = held[:, width + 1]
    held_row = held[:, width + 2]
    held_from = jnp.dot(select, macro_ids.astype(jnp.float32), precision=exact).astype(jnp.int32)
    tangents = solve_slots(
        held[:, :voxels], held[:, voxels:width].reshape(slots, 6, voxels), held_count, phase, moduli
    )
    dest_ids = jnp.arange(devices, dtype=jnp.int32)
    owner_dev = held_from * work_count + my_work
    to_owner = (held_valid[None, :] & (owner_dev[None, :] == dest_ids[:, None])).astype(jnp.float32)
    owner_part = jnp.dot(
        to_owner, jnp.concatenate([tangents, held_row[:, None]], axis=1), precision=exact
    )
    slot_parts = []
    for s in range(slots):
        hit = held_valid & (held_route == dest_ids[:, None] * slots + s)
        slot_parts.append(jnp.dot(hit.astype(jnp.float32), tangents, precision=exact))
    back = jnp.concatenate([owner_part] + slot_parts, axis=1)
    returned = lax.all_to_all(back, ("macro", "work"), 0, 0, tiled=True)
    row_ids = jnp.arange(points, dtype=jnp.float32) + 1.0
    mine = (returned[None, :, 36] == row_ids[:, None]).astype(jnp.float32)
    chosen = jnp.dot(mine, returned[:, :36], precision=exact)
    tangent = jnp.where(active[:, None], chosen, tangent_old)
    solved = jnp.stack(
        [jnp.sum(returned[:, 37 + 36 * s : 37 + 36 * (s + 1)], axis=0) for s in range(slots)]
    )
    return (tangent, solved)


def solution(mesh):
    return jax.shard_map(
        body,
        mesh=mesh,
        in_specs=(
            P(("macro", "work"), None),
            P(("macro", "work"), None, None),
            P(("macro", "work")),
            P(("macro", "work")),
            P(),
            P(),
            P(("macro", "work"), None),
        ),
        out_specs=(P(("macro", "work"), None), P(("macro", "work"), None)),
        check_vma=False,
    )
```

```python
import numpy as np
import jax
import jax.numpy as jnp
from jax import lax
from jax.sharding import PartitionSpec as P

RES = 16
ITERS = 2
ACT_DEV = 4

exact = lax.Precision.HIGHEST
fast = lax.Precision.HIGH


def moduli_field(phase, moduli):
    first = jnp.where(phase == 1, moduli[1, 0], moduli[0, 0])
    shear = jnp.where(phase == 1, moduli[1, 1], moduli[0, 1])
    return (first, shear)


def elastic(field, first, shear):
    trace = field[0] + field[1] + field[2]
    parts = [2.0 * shear * field[c] + first * trace for c in range(3)]
    parts = parts + [2.0 * shear * field[c] for c in range(3, 6)]
    return jnp.stack(parts)


def contract(left, right):
    diagonal = left[0] * right[0] + left[1] * right[1] + left[2] * right[2]
    return diagonal + 2.0 * (left[3] * right[3] + left[4] * right[4] + left[5] * right[5])


def green(part, first0, shear0, wave_a, wave_b, wave_c):
    norm = wave_a * wave_a + wave_b * wave_b + wave_c * wave_c
    safe = jnp.where(norm > 0, norm, 1.0)
    living = jnp.where(norm > 0, 1.0, 0.0)
    force_a = part[0] * wave_a + part[5] * wave_b + part[4] * wave_c
    force_b = part[5] * wave_a + part[1] * wave_b + part[3] * wave_c
    force_c = part[4] * wave_a + part[3] * wave_b + part[2] * wave_c
    kappa = (first0 + shear0) / (shear0 * (first0 + 2.0 * shear0))
    along = (wave_a * force_a + wave_b * force_b + wave_c * force_c) * kappa / (safe * safe)
    factor = 0.5 / (shear0 * safe)
    parts = [
        factor * 2.0 * wave_a * force_a - along * wave_a * wave_a,
        factor * 2.0 * wave_b * force_b - along * wave_b * wave_b,
        factor * 2.0 * wave_c * force_c - along * wave_c * wave_c,
        factor * (wave_c * force_b + wave_b * force_c) - along * wave_b * wave_c,
        factor * (wave_c * force_a + wave_a * force_c) - along * wave_a * wave_c,
        factor * (wave_b * force_a + wave_a * force_b) - along * wave_a * wave_b,
    ]
    return jnp.stack(parts) * living


def fourier_tables(edge):
    line = np.arange(edge)
    angle_one = (np.outer(line, line) % edge) * (2.0 * np.pi / edge)
    flat = np.arange(edge * edge)
    rows, cols = flat // edge, flat % edge
    angle_two = (np.outer(rows, rows) + np.outer(cols, cols)) % edge
    angle_two = angle_two * (2.0 * np.pi / edge)
    volume = float(edge ** 3)
    return dict(
        cos_one=np.cos(angle_one).astype(np.float32),
        sin_one=np.sin(angle_one).astype(np.float32),
        cos_two=np.cos(angle_two).astype(np.float32),
        nsin_two=(-np.sin(angle_two)).astype(np.float32),
        icos_two=(np.cos(angle_two) / volume).astype(np.float32),
        insin_two=(-np.sin(angle_two) / volume).astype(np.float32),
        plus_two=(np.cos(angle_two) - np.sin(angle_two)).astype(np.float32),
        minus_two=(-np.sin(angle_two) - np.cos(angle_two)).astype(np.float32),
    )


def forward(field, tables):
    cos_one, sin_one, cos_two, nsin_two, plus_two, minus_two = tables
    real_one = jnp.einsum("ka,...al->...kl", cos_one, field, precision=fast)
    imag_one = -jnp.einsum("ka,...al->...kl", sin_one, field, precision=fast)
    both = jnp.matmul(real_one + imag_one, cos_two, precision=fast)
    real_two = both - jnp.matmul(imag_one, plus_two, precision=fast)
    imag_two = both + jnp.matmul(real_one, minus_two, precision=fast)
    return (real_two, imag_two)


def inverse(real_two, imag_two, tables):
    cos_one, sin_one, cos_two, nsin_two, plus_two, minus_two = tables
    both = jnp.matmul(real_two + imag_two, cos_two, precision=fast)
    real_one = both + jnp.matmul(imag_two, minus_two, precision=fast)
    imag_one = both - jnp.matmul(real_two, plus_two, precision=fast)
    total = jnp.einsum("ka,...kl->...al", cos_one, real_one, precision=fast)
    total = total - jnp.einsum("ka,...kl->...al", sin_one, imag_one, precision=fast)
    return total / (cos_one.shape[0] * cos_two.shape[0])


def tangent_apply(field, first, shear, keep, state, state_norm):
    weight = keep * shear * contract(field, state) / (1.0 + state_norm)
    return keep * elastic(field, first, shear) - weight * state


def signed_waves(index, edge):
    return jnp.where(index < edge // 2, index, index - edge).astype(jnp.float32)


def unit_columns():
    index = jnp.arange(6)
    values = jnp.where(
        index[:, None] == index[None, :], jnp.where(index[:, None] < 3, 1.0, 0.5), 0.0
    )
    return values.astype(jnp.float32)


def solve_slots(held_damage, held_strain, held_count, phase, moduli):
    edge = RES
    plane = edge * edge
    slots = held_damage.shape[0]
    first, shear = moduli_field(phase.reshape(edge, plane), moduli)
    first0 = jnp.mean(moduli[:, 0])
    shear0 = jnp.mean(moduli[:, 1])
    keep = (1.0 - held_damage).reshape(slots, 1, edge, plane)
    state_strain = jnp.transpose(held_strain.reshape(slots, 6, edge, plane), (1, 0, 2, 3))[
        :, :, None
    ]
    state = elastic(state_strain, first, shear)
    state_norm = contract(state, state)
    flat = jnp.arange(plane, dtype=jnp.int32)
    wave_a = signed_waves(jnp.arange(edge, dtype=jnp.int32), edge)[:, None]
    wave_b = signed_waves(flat // edge, edge)[None, :]
    wave_c = signed_waves(flat % edge, edge)[None, :]
    table = fourier_tables(edge)
    tables = tuple(jnp.asarray(table[k]) for k in ("cos_one", "sin_one", "cos_two", "nsin_two", "plus_two", "minus_two"))
    macro_field = unit_columns()[:, None, :, None, None]
    field = jnp.broadcast_to(macro_field, (6, slots, 6, edge, plane))
    count = held_count[:, None, None, None]
    for step in range(ITERS):
        polar = tangent_apply(field, first, shear, keep, state, state_norm) - elastic(
            field, first0, shear0
        )
        real_part, imag_part = forward(polar, tables)
        real_part = green(real_part, first0, shear0, wave_a, wave_b, wave_c)
        imag_part = green(imag_part, first0, shear0, wave_a, wave_b, wave_c)
        back = inverse(real_part, imag_part, tables)
        field = jnp.where(step < count, macro_field - back, field)
    stress = tangent_apply(field, first, shear, keep, state, state_norm)
    means = jnp.sum(stress, axis=(3, 4)) / (edge * plane)
    return jnp.transpose(means, (1, 0, 2)).reshape(slots, 36)


def body(damage, strain, route, iters, phase, moduli, tangent_old):
    slots = ACT_DEV
    macro_count = lax.axis_size("macro")
    work_count = lax.axis_size("work")
    devices = macro_count * work_count
    my_macro = lax.axis_index("macro")
    my_work = lax.axis_index("work")
    points, voxels = damage.shape
    width = 7 * voxels
    active = route >= 0
    dest_macro = jnp.where(active, route // slots // work_count, -1)
    macro_ids = jnp.arange(macro_count, dtype=jnp.int32)
    to_macro = dest_macro[None, :] == macro_ids[:, None]
    point_ids = jnp.arange(points, dtype=jnp.int32)
    pick = jnp.max(jnp.where(to_macro, point_ids[None, :], -1), axis=1)
    sending = pick >= 0
    pick = jnp.maximum(pick, 0)
    meta = jnp.stack(
        [route.astype(jnp.float32) + 1.0, iters.astype(jnp.float32), point_ids.astype(jnp.float32) + 1.0]
        + [jnp.zeros((points,), jnp.float32)] * 125,
        axis=1,
    )
    outgoing = jnp.concatenate(
        [damage[pick], strain[pick].reshape(macro_count, 6 * voxels), meta[pick]], axis=1
    )
    outgoing = jnp.where(sending[:, None], outgoing, 0.0)
    arrived = lax.all_to_all(outgoing, "macro", 0, 0, tiled=True)
    valid = arrived[:, width] > 0.5
    rank = jnp.cumsum(valid.astype(jnp.int32)) - 1
    vol_ids = jnp.arange(slots, dtype=jnp.int32)
    select = (valid[None, :] & (rank[None, :] == vol_ids[:, None])).astype(jnp.float32)
    held = jnp.dot(select, arrived, precision=exact)
    held_valid = jnp.sum(select, axis=1) > 0.5
    held_route = (held[:, width] - 1.0).astype(jnp.int32)
    held_count = held[:, width + 1]
    held_row = held[:, width + 2]
    held_from = jnp.dot(select, macro_ids.astype(jnp.float32), precision=exact).astype(jnp.int32)
    tangents = solve_slots(
        held[:, :voxels], held[:, voxels:width].reshape(slots, 6, voxels), held_count, phase, moduli
    )
    dest_ids = jnp.arange(devices, dtype=jnp.int32)
    owner_dev = held_from * work_count + my_work
    to_owner = (held_valid[None, :] & (owner_dev[None, :] == dest_ids[:, None])).astype(jnp.float32)
    owner_part = jnp.dot(
        to_owner, jnp.concatenate([tangents, held_row[:, None]], axis=1), precision=exact
    )
    slot_parts = []
    for s in range(slots):
        hit = held_valid & (held_route == dest_ids[:, None] * slots + s)
        slot_parts.append(jnp.dot(hit.astype(jnp.float32), tangents, precision=exact))
    back = jnp.concatenate([owner_part] + slot_parts, axis=1)
    returned = lax.all_to_all(back, ("macro", "work"), 0, 0, tiled=True)
    row_ids = jnp.arange(points, dtype=jnp.float32) + 1.0
    mine = (returned[None, :, 36] == row_ids[:, None]).astype(jnp.float32)
    chosen = jnp.dot(mine, returned[:, :36], precision=exact)
    tangent = jnp.where(active[:, None], chosen, tangent_old)
    solved = jnp.stack(
        [jnp.sum(returned[:, 37 + 36 * s : 37 + 36 * (s + 1)], axis=0) for s in range(slots)]
    )
    return (tangent, solved)


def solution(mesh):
    return jax.shard_map(
        body,
        mesh=mesh,
        in_specs=(
            P(("macro", "work"), None),
            P(("macro", "work"), None, None),
            P(("macro", "work")),
            P(("macro", "work")),
            P(),
            P(),
            P(("macro", "work"), None),
        ),
        out_specs=(P(("macro", "work"), None), P(("macro", "work"), None)),
        check_vma=False,
    )
```

```python
import numpy as np
import jax
import jax.numpy as jnp
from jax import lax
from jax.sharding import PartitionSpec as P

RES = 16
ITERS = 2
ACT_DEV = 4

exact = lax.Precision.HIGHEST
fast = lax.Precision.HIGH


def moduli_field(phase, moduli):
    first = jnp.where(phase == 1, moduli[1, 0], moduli[0, 0])
    shear = jnp.where(phase == 1, moduli[1, 1], moduli[0, 1])
    return (first, shear)


def elastic(field, first, shear):
    trace = field[0] + field[1] + field[2]
    parts = [2.0 * shear * field[c] + first * trace for c in range(3)]
    parts = parts + [2.0 * shear * field[c] for c in range(3, 6)]
    return jnp.stack(parts)


def contract(left, right):
    diagonal = left[0] * right[0] + left[1] * right[1] + left[2] * right[2]
    return diagonal + 2.0 * (left[3] * right[3] + left[4] * right[4] + left[5] * right[5])


def green(part, first0, shear0, wave_a, wave_b, wave_c):
    norm = wave_a * wave_a + wave_b * wave_b + wave_c * wave_c
    safe = jnp.where(norm > 0, norm, 1.0)
    living = jnp.where(norm > 0, 1.0, 0.0)
    force_a = part[0] * wave_a + part[5] * wave_b + part[4] * wave_c
    force_b = part[5] * wave_a + part[1] * wave_b + part[3] * wave_c
    force_c = part[4] * wave_a + part[3] * wave_b + part[2] * wave_c
    kappa = (first0 + shear0) / (shear0 * (first0 + 2.0 * shear0))
    along = (wave_a * force_a + wave_b * force_b + wave_c * force_c) * kappa / (safe * safe)
    factor = 0.5 / (shear0 * safe)
    parts = [
        factor * 2.0 * wave_a * force_a - along * wave_a * wave_a,
        factor * 2.0 * wave_b * force_b - along * wave_b * wave_b,
        factor * 2.0 * wave_c * force_c - along * wave_c * wave_c,
        factor * (wave_c * force_b + wave_b * force_c) - along * wave_b * wave_c,
        factor * (wave_c * force_a + wave_a * force_c) - along * wave_a * wave_c,
        factor * (wave_b * force_a + wave_a * force_b) - along * wave_a * wave_b,
    ]
    return jnp.stack(parts) * living


def fourier_tables(edge):
    line = np.arange(edge)
    angle_one = (np.outer(line, line) % edge) * (2.0 * np.pi / edge)
    flat = np.arange(edge * edge)
    rows, cols = flat // edge, flat % edge
    angle_two = (np.outer(rows, rows) + np.outer(cols, cols)) % edge
    angle_two = angle_two * (2.0 * np.pi / edge)
    volume = float(edge ** 3)
    return dict(
        cos_one=np.cos(angle_one).astype(np.float32),
        sin_one=np.sin(angle_one).astype(np.float32),
        cos_two=np.cos(angle_two).astype(np.float32),
        nsin_two=(-np.sin(angle_two)).astype(np.float32),
        icos_two=(np.cos(angle_two) / volume).astype(np.float32),
        insin_two=(-np.sin(angle_two) / volume).astype(np.float32),
        plus_two=(np.cos(angle_two) - np.sin(angle_two)).astype(np.float32),
        both_one=np.concatenate([np.cos(angle_one), -np.sin(angle_one)]).astype(np.float32),
        icos_one=(np.cos(angle_one) / volume).astype(np.float32),
        isin_one=(np.sin(angle_one) / volume).astype(np.float32),
        minus_two=(-np.sin(angle_two) - np.cos(angle_two)).astype(np.float32),
    )


def forward(field, tables):
    both_one, cos_two, plus_two, minus_two, icos_one, isin_one = tables
    edge = icos_one.shape[0]
    stacked = jnp.einsum("ka,...al->...kl", both_one, field, precision=fast)
    real_one = stacked[..., :edge, :]
    imag_one = stacked[..., edge:, :]
    both = jnp.matmul(real_one + imag_one, cos_two, precision=fast)
    real_two = both - jnp.matmul(imag_one, plus_two, precision=fast)
    imag_two = both + jnp.matmul(real_one, minus_two, precision=fast)
    return (real_two, imag_two)


def inverse(real_two, imag_two, tables):
    both_one, cos_two, plus_two, minus_two, icos_one, isin_one = tables
    both = jnp.matmul(real_two + imag_two, cos_two, precision=fast)
    real_one = both + jnp.matmul(imag_two, minus_two, precision=fast)
    imag_one = both - jnp.matmul(real_two, plus_two, precision=fast)
    total = jnp.einsum("ka,...kl->...al", icos_one, real_one, precision=fast)
    return total - jnp.einsum("ka,...kl->...al", isin_one, imag_one, precision=fast)


def tangent_apply(field, first, shear, keep, state, state_norm):
    weight = keep * shear * contract(field, state) / (1.0 + state_norm)
    return keep * elastic(field, first, shear) - weight * state


def signed_waves(index, edge):
    return jnp.where(index < edge // 2, index, index - edge).astype(jnp.float32)


def unit_columns():
    index = jnp.arange(6)
    values = jnp.where(
        index[:, None] == index[None, :], jnp.where(index[:, None] < 3, 1.0, 0.5), 0.0
    )
    return values.astype(jnp.float32)


def solve_slots(held_damage, held_strain, held_count, phase, moduli):
    edge = RES
    plane = edge * edge
    slots = held_damage.shape[0]
    first, shear = moduli_field(phase.reshape(edge, plane), moduli)
    first0 = jnp.mean(moduli[:, 0])
    shear0 = jnp.mean(moduli[:, 1])
    keep = (1.0 - held_damage).reshape(slots, 1, edge, plane)
    state_strain = jnp.transpose(held_strain.reshape(slots, 6, edge, plane), (1, 0, 2, 3))[
        :, :, None
    ]
    state = elastic(state_strain, first, shear)
    state_norm = contract(state, state)
    flat = jnp.arange(plane, dtype=jnp.int32)
    wave_a = signed_waves(jnp.arange(edge, dtype=jnp.int32), edge)[:, None]
    wave_b = signed_waves(flat // edge, edge)[None, :]
    wave_c = signed_waves(flat % edge, edge)[None, :]
    table = fourier_tables(edge)
    tables = tuple(jnp.asarray(table[k]) for k in ("both_one", "cos_two", "plus_two", "minus_two", "icos_one", "isin_one"))
    macro_field = unit_columns()[:, None, :, None, None]
    field = jnp.broadcast_to(macro_field, (6, slots, 6, edge, plane))
    count = held_count[:, None, None, None]
    for step in range(ITERS):
        polar = tangent_apply(field, first, shear, keep, state, state_norm) - elastic(
            field, first0, shear0
        )
        polar = lax.optimization_barrier(polar)
        real_part, imag_part = forward(polar, tables)
        real_part = green(real_part, first0, shear0, wave_a, wave_b, wave_c)
        imag_part = green(imag_part, first0, shear0, wave_a, wave_b, wave_c)
        back = inverse(real_part, imag_part, tables)
        field = jnp.where(step < count, macro_field - back, field)
    stress = tangent_apply(field, first, shear, keep, state, state_norm)
    means = jnp.sum(stress, axis=(3, 4)) / (edge * plane)
    return jnp.transpose(means, (1, 0, 2)).reshape(slots, 36)


def body(damage, strain, route, iters, phase, moduli, tangent_old):
    slots = ACT_DEV
    macro_count = lax.axis_size("macro")
    work_count = lax.axis_size("work")
    devices = macro_count * work_count
    my_macro = lax.axis_index("macro")
    my_work = lax.axis_index("work")
    points, voxels = damage.shape
    width = 7 * voxels
    active = route >= 0
    dest_macro = jnp.where(active, route // slots // work_count, -1)
    macro_ids = jnp.arange(macro_count, dtype=jnp.int32)
    to_macro = dest_macro[None, :] == macro_ids[:, None]
    point_ids = jnp.arange(points, dtype=jnp.int32)
    pick = jnp.max(jnp.where(to_macro, point_ids[None, :], -1), axis=1)
    sending = pick >= 0
    pick = jnp.maximum(pick, 0)
    meta = jnp.stack(
        [route.astype(jnp.float32) + 1.0, iters.astype(jnp.float32), point_ids.astype(jnp.float32) + 1.0]
        + [jnp.zeros((points,), jnp.float32)] * 125,
        axis=1,
    )
    outgoing = jnp.concatenate(
        [damage[pick], strain[pick].reshape(macro_count, 6 * voxels), meta[pick]], axis=1
    )
    outgoing = jnp.where(sending[:, None], outgoing, 0.0)
    arrived = lax.all_to_all(outgoing, "macro", 0, 0, tiled=True)
    valid = arrived[:, width] > 0.5
    rank = jnp.cumsum(valid.astype(jnp.int32)) - 1
    vol_ids = jnp.arange(slots, dtype=jnp.int32)
    select = (valid[None, :] & (rank[None, :] == vol_ids[:, None])).astype(jnp.float32)
    held = jnp.dot(select, arrived, precision=exact)
    held_valid = jnp.sum(select, axis=1) > 0.5
    held_route = (held[:, width] - 1.0).astype(jnp.int32)
    held_count = held[:, width + 1]
    held_row = held[:, width + 2]
    held_from = jnp.dot(select, macro_ids.astype(jnp.float32), precision=exact).astype(jnp.int32)
    tangents = solve_slots(
        held[:, :voxels], held[:, voxels:width].reshape(slots, 6, voxels), held_count, phase, moduli
    )
    dest_ids = jnp.arange(devices, dtype=jnp.int32)
    owner_dev = held_from * work_count + my_work
    to_owner = (held_valid[None, :] & (owner_dev[None, :] == dest_ids[:, None])).astype(jnp.float32)
    owner_part = jnp.dot(
        to_owner, jnp.concatenate([tangents, held_row[:, None]], axis=1), precision=exact
    )
    slot_parts = []
    for s in range(slots):
        hit = held_valid & (held_route == dest_ids[:, None] * slots + s)
        slot_parts.append(jnp.dot(hit.astype(jnp.float32), tangents, precision=exact))
    back = jnp.concatenate([owner_part] + slot_parts, axis=1)
    returned = lax.all_to_all(back, ("macro", "work"), 0, 0, tiled=True)
    row_ids = jnp.arange(points, dtype=jnp.float32) + 1.0
    mine = (returned[None, :, 36] == row_ids[:, None]).astype(jnp.float32)
    chosen = jnp.dot(mine, returned[:, :36], precision=exact)
    tangent = jnp.where(active[:, None], chosen, tangent_old)
    solved = jnp.stack(
        [jnp.sum(returned[:, 37 + 36 * s : 37 + 36 * (s + 1)], axis=0) for s in range(slots)]
    )
    return (tangent, solved)


def solution(mesh):
    return jax.shard_map(
        body,
        mesh=mesh,
        in_specs=(
            P(("macro", "work"), None),
            P(("macro", "work"), None, None),
            P(("macro", "work")),
            P(("macro", "work")),
            P(),
            P(),
            P(("macro", "work"), None),
        ),
        out_specs=(P(("macro", "work"), None), P(("macro", "work"), None)),
        check_vma=False,
    )
```

```python
import numpy as np
import jax
import jax.numpy as jnp
from jax import lax
from jax.sharding import PartitionSpec as P

RES = 16
ITERS = 2
ACT_DEV = 4

exact = lax.Precision.HIGHEST
fast = lax.Precision.HIGH


def moduli_field(phase, moduli):
    first = jnp.where(phase == 1, moduli[1, 0], moduli[0, 0])
    shear = jnp.where(phase == 1, moduli[1, 1], moduli[0, 1])
    return (first, shear)


def elastic(field, first, shear):
    trace = field[0] + field[1] + field[2]
    parts = [2.0 * shear * field[c] + first * trace for c in range(3)]
    parts = parts + [2.0 * shear * field[c] for c in range(3, 6)]
    return jnp.stack(parts)


def contract(left, right):
    diagonal = left[0] * right[0] + left[1] * right[1] + left[2] * right[2]
    return diagonal + 2.0 * (left[3] * right[3] + left[4] * right[4] + left[5] * right[5])


def green(part, first0, shear0, wave_a, wave_b, wave_c):
    norm = wave_a * wave_a + wave_b * wave_b + wave_c * wave_c
    safe = jnp.where(norm > 0, norm, 1.0)
    living = jnp.where(norm > 0, 1.0, 0.0)
    force_a = part[0] * wave_a + part[5] * wave_b + part[4] * wave_c
    force_b = part[5] * wave_a + part[1] * wave_b + part[3] * wave_c
    force_c = part[4] * wave_a + part[3] * wave_b + part[2] * wave_c
    kappa = (first0 + shear0) / (shear0 * (first0 + 2.0 * shear0))
    along = (wave_a * force_a + wave_b * force_b + wave_c * force_c) * kappa / (safe * safe)
    factor = 0.5 / (shear0 * safe)
    parts = [
        factor * 2.0 * wave_a * force_a - along * wave_a * wave_a,
        factor * 2.0 * wave_b * force_b - along * wave_b * wave_b,
        factor * 2.0 * wave_c * force_c - along * wave_c * wave_c,
        factor * (wave_c * force_b + wave_b * force_c) - along * wave_b * wave_c,
        factor * (wave_c * force_a + wave_a * force_c) - along * wave_a * wave_c,
        factor * (wave_b * force_a + wave_a * force_b) - along * wave_a * wave_b,
    ]
    return jnp.stack(parts) * living


def fourier_tables(edge):
    line = np.arange(edge)
    angle_one = (np.outer(line, line) % edge) * (2.0 * np.pi / edge)
    flat = np.arange(edge * edge)
    rows, cols = flat // edge, flat % edge
    angle_two = (np.outer(rows, rows) + np.outer(cols, cols)) % edge
    angle_two = angle_two * (2.0 * np.pi / edge)
    volume = float(edge ** 3)
    return dict(
        cos_one=np.cos(angle_one).astype(np.float32),
        sin_one=np.sin(angle_one).astype(np.float32),
        cos_two=np.cos(angle_two).astype(np.float32),
        nsin_two=(-np.sin(angle_two)).astype(np.float32),
        icos_two=(np.cos(angle_two) / volume).astype(np.float32),
        insin_two=(-np.sin(angle_two) / volume).astype(np.float32),
        plus_two=(np.cos(angle_two) - np.sin(angle_two)).astype(np.float32),
        both_one=np.concatenate([np.cos(angle_one), -np.sin(angle_one)]).astype(np.float32),
        icos_one=(np.cos(angle_one) / volume).astype(np.float32),
        isin_one=(np.sin(angle_one) / volume).astype(np.float32),
        minus_two=(-np.sin(angle_two) - np.cos(angle_two)).astype(np.float32),
    )


def forward(field, tables):
    both_one, cos_two, plus_two, minus_two, icos_one, isin_one = tables
    edge = icos_one.shape[0]
    stacked = jnp.einsum("ka,...al->...kl", both_one, field, precision=fast)
    real_one = stacked[..., :edge, :]
    imag_one = stacked[..., edge:, :]
    both = jnp.matmul(real_one + imag_one, cos_two, precision=fast)
    real_two = both - jnp.matmul(imag_one, plus_two, precision=fast)
    imag_two = both + jnp.matmul(real_one, minus_two, precision=fast)
    return (real_two, imag_two)


def inverse(real_two, imag_two, tables):
    both_one, cos_two, plus_two, minus_two, icos_one, isin_one = tables
    both = jnp.matmul(real_two + imag_two, cos_two, precision=fast)
    real_one = both + jnp.matmul(imag_two, minus_two, precision=fast)
    imag_one = both - jnp.matmul(real_two, plus_two, precision=fast)
    total = jnp.einsum("ka,...kl->...al", icos_one, real_one, precision=fast)
    return total - jnp.einsum("ka,...kl->...al", isin_one, imag_one, precision=fast)


DIAGONAL = np.array([1.0, 1.0, 1.0, 0.0, 0.0, 0.0], np.float32)
DOUBLED = np.array([1.0, 1.0, 1.0, 2.0, 2.0, 2.0], np.float32)
FIRST_AXIS = [0, 1, 2, 1, 0, 0]
SECOND_AXIS = [0, 1, 2, 2, 2, 1]


def lead(values, ndim):
    return jnp.asarray(np.asarray(values, np.float32).reshape((-1,) + (1,) * (ndim - 1)))


def elastic_wide(field, first, shear):
    trace = field[0] + field[1] + field[2]
    return 2.0 * shear * field + first * trace * lead(DIAGONAL, field.ndim)


def contract_wide(left, right):
    return jnp.sum(lead(DOUBLED, left.ndim) * left * right, axis=0)


def tangent_wide(field, first, shear, keep, state, gain):
    weight = gain * contract_wide(field, state)
    return keep * elastic_wide(field, first, shear) - weight * state


def green_wide(part, first0, shear0, wave_a, wave_b, wave_c):
    norm = wave_a * wave_a + wave_b * wave_b + wave_c * wave_c
    safe = jnp.where(norm > 0, norm, 1.0)
    living = jnp.where(norm > 0, 1.0, 0.0)
    force_a = part[0] * wave_a + part[5] * wave_b + part[4] * wave_c
    force_b = part[5] * wave_a + part[1] * wave_b + part[3] * wave_c
    force_c = part[4] * wave_a + part[3] * wave_b + part[2] * wave_c
    kappa = (first0 + shear0) / (shear0 * (first0 + 2.0 * shear0))
    along = (wave_a * force_a + wave_b * force_b + wave_c * force_c) * kappa / (safe * safe)
    factor = 0.5 / (shear0 * safe)
    waves = (wave_a, wave_b, wave_c)
    forces = (force_a, force_b, force_c)
    ndim = part.ndim

    def pick(table, axes):
        total = None
        for d in range(3):
            mask = lead([1.0 if axes[c] == d else 0.0 for c in range(6)], ndim)
            term = mask * table[d]
            total = term if total is None else total + term
        return total

    wave_one, wave_two = pick(waves, FIRST_AXIS), pick(waves, SECOND_AXIS)
    force_one, force_two = pick(forces, FIRST_AXIS), pick(forces, SECOND_AXIS)
    out = factor * (wave_one * force_two + wave_two * force_one) - along * wave_one * wave_two
    return out * living


def signed_waves(index, edge):
    return jnp.where(index < edge // 2, index, index - edge).astype(jnp.float32)


def unit_columns():
    index = jnp.arange(6)
    values = jnp.where(
        index[:, None] == index[None, :], jnp.where(index[:, None] < 3, 1.0, 0.5), 0.0
    )
    return values.astype(jnp.float32)


def solve_slots(held_damage, held_strain, held_count, phase, moduli):
    edge = RES
    plane = edge * edge
    slots = held_damage.shape[0]
    first, shear = moduli_field(phase.reshape(edge, plane), moduli)
    first0 = jnp.mean(moduli[:, 0])
    shear0 = jnp.mean(moduli[:, 1])
    keep = (1.0 - held_damage).reshape(slots, 1, edge, plane)
    state_strain = jnp.transpose(held_strain.reshape(slots, 6, edge, plane), (1, 0, 2, 3))[
        :, :, None
    ]
    state = elastic_wide(state_strain, first, shear)
    gain = keep * shear / (1.0 + contract_wide(state, state))
    flat = jnp.arange(plane, dtype=jnp.int32)
    wave_a = signed_waves(jnp.arange(edge, dtype=jnp.int32), edge)[:, None]
    wave_b = signed_waves(flat // edge, edge)[None, :]
    wave_c = signed_waves(flat % edge, edge)[None, :]
    table = fourier_tables(edge)
    tables = tuple(jnp.asarray(table[k]) for k in ("both_one", "cos_two", "plus_two", "minus_two", "icos_one", "isin_one"))
    macro_field = unit_columns()[:, None, :, None, None]
    field = jnp.broadcast_to(macro_field, (6, slots, 6, edge, plane))
    count = held_count[:, None, None, None]
    for step in range(ITERS):
        polar = tangent_wide(field, first, shear, keep, state, gain) - elastic_wide(field, first0, shear0)
        polar = lax.optimization_barrier(polar)
        real_part, imag_part = forward(polar, tables)
        real_part = green_wide(real_part, first0, shear0, wave_a, wave_b, wave_c)
        imag_part = green_wide(imag_part, first0, shear0, wave_a, wave_b, wave_c)
        back = inverse(real_part, imag_part, tables)
        field = jnp.where(step < count, macro_field - back, field)
    stress = tangent_wide(field, first, shear, keep, state, gain)
    means = jnp.sum(stress, axis=(3, 4)) / (edge * plane)
    return jnp.transpose(means, (1, 0, 2)).reshape(slots, 36)


def body(damage, strain, route, iters, phase, moduli, tangent_old):
    slots = ACT_DEV
    macro_count = lax.axis_size("macro")
    work_count = lax.axis_size("work")
    devices = macro_count * work_count
    my_macro = lax.axis_index("macro")
    my_work = lax.axis_index("work")
    points, voxels = damage.shape
    width = 7 * voxels
    active = route >= 0
    dest_macro = jnp.where(active, route // slots // work_count, -1)
    macro_ids = jnp.arange(macro_count, dtype=jnp.int32)
    to_macro = dest_macro[None, :] == macro_ids[:, None]
    point_ids = jnp.arange(points, dtype=jnp.int32)
    pick = jnp.max(jnp.where(to_macro, point_ids[None, :], -1), axis=1)
    sending = pick >= 0
    pick = jnp.maximum(pick, 0)
    meta = jnp.stack(
        [route.astype(jnp.float32) + 1.0, iters.astype(jnp.float32), point_ids.astype(jnp.float32) + 1.0]
        + [jnp.zeros((points,), jnp.float32)] * 125,
        axis=1,
    )
    outgoing = jnp.concatenate(
        [damage[pick], strain[pick].reshape(macro_count, 6 * voxels), meta[pick]], axis=1
    )
    outgoing = jnp.where(sending[:, None], outgoing, 0.0)
    arrived = lax.all_to_all(outgoing, "macro", 0, 0, tiled=True)
    valid = arrived[:, width] > 0.5
    rank = jnp.cumsum(valid.astype(jnp.int32)) - 1
    vol_ids = jnp.arange(slots, dtype=jnp.int32)
    select = (valid[None, :] & (rank[None, :] == vol_ids[:, None])).astype(jnp.float32)
    held = jnp.dot(select, arrived, precision=exact)
    held_valid = jnp.sum(select, axis=1) > 0.5
    held_route = (held[:, width] - 1.0).astype(jnp.int32)
    held_count = held[:, width + 1]
    held_row = held[:, width + 2]
    held_from = jnp.dot(select, macro_ids.astype(jnp.float32), precision=exact).astype(jnp.int32)
    tangents = solve_slots(
        held[:, :voxels], held[:, voxels:width].reshape(slots, 6, voxels), held_count, phase, moduli
    )
    dest_ids = jnp.arange(devices, dtype=jnp.int32)
    owner_dev = held_from * work_count + my_work
    to_owner = (held_valid[None, :] & (owner_dev[None, :] == dest_ids[:, None])).astype(jnp.float32)
    owner_part = jnp.dot(
        to_owner, jnp.concatenate([tangents, held_row[:, None]], axis=1), precision=exact
    )
    slot_parts = []
    for s in range(slots):
        hit = held_valid & (held_route == dest_ids[:, None] * slots + s)
        slot_parts.append(jnp.dot(hit.astype(jnp.float32), tangents, precision=exact))
    back = jnp.concatenate([owner_part] + slot_parts, axis=1)
    returned = lax.all_to_all(back, ("macro", "work"), 0, 0, tiled=True)
    row_ids = jnp.arange(points, dtype=jnp.float32) + 1.0
    mine = (returned[None, :, 36] == row_ids[:, None]).astype(jnp.float32)
    chosen = jnp.dot(mine, returned[:, :36], precision=exact)
    tangent = jnp.where(active[:, None], chosen, tangent_old)
    solved = jnp.stack(
        [jnp.sum(returned[:, 37 + 36 * s : 37 + 36 * (s + 1)], axis=0) for s in range(slots)]
    )
    return (tangent, solved)


def solution(mesh):
    return jax.shard_map(
        body,
        mesh=mesh,
        in_specs=(
            P(("macro", "work"), None),
            P(("macro", "work"), None, None),
            P(("macro", "work")),
            P(("macro", "work")),
            P(),
            P(),
            P(("macro", "work"), None),
        ),
        out_specs=(P(("macro", "work"), None), P(("macro", "work"), None)),
        check_vma=False,
    )
```

```python
import numpy as np
import jax
import jax.numpy as jnp
from jax import lax
from jax.sharding import PartitionSpec as P

RES = 16
ITERS = 2
ACT_DEV = 4

exact = lax.Precision.HIGHEST
fast = lax.Precision.HIGH


def moduli_field(phase, moduli):
    first = jnp.where(phase == 1, moduli[1, 0], moduli[0, 0])
    shear = jnp.where(phase == 1, moduli[1, 1], moduli[0, 1])
    return (first, shear)


def elastic(field, first, shear):
    trace = field[0] + field[1] + field[2]
    parts = [2.0 * shear * field[c] + first * trace for c in range(3)]
    parts = parts + [2.0 * shear * field[c] for c in range(3, 6)]
    return jnp.stack(parts)


def contract(left, right):
    diagonal = left[0] * right[0] + left[1] * right[1] + left[2] * right[2]
    return diagonal + 2.0 * (left[3] * right[3] + left[4] * right[4] + left[5] * right[5])


def green(part, first0, shear0, wave_a, wave_b, wave_c):
    norm = wave_a * wave_a + wave_b * wave_b + wave_c * wave_c
    safe = jnp.where(norm > 0, norm, 1.0)
    living = jnp.where(norm > 0, 1.0, 0.0)
    force_a = part[0] * wave_a + part[5] * wave_b + part[4] * wave_c
    force_b = part[5] * wave_a + part[1] * wave_b + part[3] * wave_c
    force_c = part[4] * wave_a + part[3] * wave_b + part[2] * wave_c
    kappa = (first0 + shear0) / (shear0 * (first0 + 2.0 * shear0))
    along = (wave_a * force_a + wave_b * force_b + wave_c * force_c) * kappa / (safe * safe)
    factor = 0.5 / (shear0 * safe)
    parts = [
        factor * 2.0 * wave_a * force_a - along * wave_a * wave_a,
        factor * 2.0 * wave_b * force_b - along * wave_b * wave_b,
        factor * 2.0 * wave_c * force_c - along * wave_c * wave_c,
        factor * (wave_c * force_b + wave_b * force_c) - along * wave_b * wave_c,
        factor * (wave_c * force_a + wave_a * force_c) - along * wave_a * wave_c,
        factor * (wave_b * force_a + wave_a * force_b) - along * wave_a * wave_b,
    ]
    return jnp.stack(parts) * living


def fourier_tables(edge):
    line = np.arange(edge)
    angle_one = (np.outer(line, line) % edge) * (2.0 * np.pi / edge)
    flat = np.arange(edge * edge)
    rows, cols = flat // edge, flat % edge
    angle_two = (np.outer(rows, rows) + np.outer(cols, cols)) % edge
    angle_two = angle_two * (2.0 * np.pi / edge)
    volume = float(edge ** 3)
    return dict(
        cos_one=np.cos(angle_one).astype(np.float32),
        sin_one=np.sin(angle_one).astype(np.float32),
        cos_two=np.cos(angle_two).astype(np.float32),
        nsin_two=(-np.sin(angle_two)).astype(np.float32),
        icos_two=(np.cos(angle_two) / volume).astype(np.float32),
        insin_two=(-np.sin(angle_two) / volume).astype(np.float32),
        plus_two=(np.cos(angle_two) - np.sin(angle_two)).astype(np.float32),
        both_one=np.concatenate([np.cos(angle_one), -np.sin(angle_one)]).astype(np.float32),
        icos_one=(np.cos(angle_one) / volume).astype(np.float32),
        isin_one=(np.sin(angle_one) / volume).astype(np.float32),
        minus_two=(-np.sin(angle_two) - np.cos(angle_two)).astype(np.float32),
    )


def forward(field, tables):
    both_one, cos_two, plus_two, minus_two, icos_one, isin_one = tables
    edge = icos_one.shape[0]
    stacked = jnp.einsum("ka,...al->...kl", both_one, field, precision=fast)
    real_one = stacked[..., :edge, :]
    imag_one = stacked[..., edge:, :]
    both = jnp.matmul(real_one + imag_one, cos_two, precision=fast)
    real_two = both - jnp.matmul(imag_one, plus_two, precision=fast)
    imag_two = both + jnp.matmul(real_one, minus_two, precision=fast)
    return (real_two, imag_two)


def inverse(real_two, imag_two, tables):
    both_one, cos_two, plus_two, minus_two, icos_one, isin_one = tables
    both = jnp.matmul(real_two + imag_two, cos_two, precision=fast)
    real_one = both + jnp.matmul(imag_two, minus_two, precision=fast)
    imag_one = both - jnp.matmul(real_two, plus_two, precision=fast)
    total = jnp.einsum("ka,...kl->...al", icos_one, real_one, precision=fast)
    return total - jnp.einsum("ka,...kl->...al", isin_one, imag_one, precision=fast)


DIAGONAL = np.array([1.0, 1.0, 1.0, 0.0, 0.0, 0.0], np.float32)
DOUBLED = np.array([1.0, 1.0, 1.0, 2.0, 2.0, 2.0], np.float32)
FIRST_AXIS = [0, 1, 2, 1, 0, 0]
SECOND_AXIS = [0, 1, 2, 2, 2, 1]


def lead(values, ndim):
    return jnp.asarray(np.asarray(values, np.float32).reshape((-1,) + (1,) * (ndim - 1)))


def elastic_wide(field, first, shear):
    trace = field[0] + field[1] + field[2]
    return 2.0 * shear * field + first * trace * lead(DIAGONAL, field.ndim)


def contract_wide(left, right):
    return jnp.sum(lead(DOUBLED, left.ndim) * left * right, axis=0)


def tangent_wide(field, first, shear, keep, state, gain):
    weight = gain * contract_wide(field, state)
    return keep * elastic_wide(field, first, shear) - weight * state


def green_wide(part, first0, shear0, wave_a, wave_b, wave_c):
    norm = wave_a * wave_a + wave_b * wave_b + wave_c * wave_c
    safe = jnp.where(norm > 0, norm, 1.0)
    living = jnp.where(norm > 0, 1.0, 0.0)
    force_a = part[0] * wave_a + part[5] * wave_b + part[4] * wave_c
    force_b = part[5] * wave_a + part[1] * wave_b + part[3] * wave_c
    force_c = part[4] * wave_a + part[3] * wave_b + part[2] * wave_c
    kappa = (first0 + shear0) / (shear0 * (first0 + 2.0 * shear0))
    along = (wave_a * force_a + wave_b * force_b + wave_c * force_c) * kappa / (safe * safe)
    factor = 0.5 / (shear0 * safe)
    waves = (wave_a, wave_b, wave_c)
    forces = (force_a, force_b, force_c)
    ndim = part.ndim

    def pick(table, axes):
        total = None
        for d in range(3):
            mask = lead([1.0 if axes[c] == d else 0.0 for c in range(6)], ndim)
            term = mask * table[d]
            total = term if total is None else total + term
        return total

    wave_one, wave_two = pick(waves, FIRST_AXIS), pick(waves, SECOND_AXIS)
    force_one, force_two = pick(forces, FIRST_AXIS), pick(forces, SECOND_AXIS)
    out = factor * (wave_one * force_two + wave_two * force_one) - along * wave_one * wave_two
    return out * living


def signed_waves(index, edge):
    return jnp.where(index < edge // 2, index, index - edge).astype(jnp.float32)


def unit_columns():
    index = jnp.arange(6)
    values = jnp.where(
        index[:, None] == index[None, :], jnp.where(index[:, None] < 3, 1.0, 0.5), 0.0
    )
    return values.astype(jnp.float32)


def solve_slots(held_damage, held_strain, held_count, phase, moduli):
    edge = RES
    plane = edge * edge
    slots = held_damage.shape[0]
    first, shear = moduli_field(phase.reshape(edge, plane), moduli)
    first0 = jnp.mean(moduli[:, 0])
    shear0 = jnp.mean(moduli[:, 1])
    keep = (1.0 - held_damage).reshape(slots, 1, edge, plane)
    state_strain = jnp.transpose(held_strain.reshape(slots, 6, edge, plane), (1, 0, 2, 3))[
        :, :, None
    ]
    state = elastic_wide(state_strain, first, shear)
    gain = keep * shear / (1.0 + contract_wide(state, state))
    flat = jnp.arange(plane, dtype=jnp.int32)
    wave_a = signed_waves(jnp.arange(edge, dtype=jnp.int32), edge)[:, None]
    wave_b = signed_waves(flat // edge, edge)[None, :]
    wave_c = signed_waves(flat % edge, edge)[None, :]
    table = fourier_tables(edge)
    tables = tuple(jnp.asarray(table[k]) for k in ("both_one", "cos_two", "plus_two", "minus_two", "icos_one", "isin_one"))
    macro_field = unit_columns()[:, None, :, None, None]
    field = jnp.broadcast_to(macro_field, (6, slots, 6, edge, plane))
    count = held_count[:, None, None, None]
    for step in range(ITERS):
        polar = tangent_wide(field, first, shear, keep, state, gain) - elastic_wide(field, first0, shear0)
        polar = lax.optimization_barrier(polar)
        real_part, imag_part = forward(polar, tables)
        real_part = green_wide(real_part, first0, shear0, wave_a, wave_b, wave_c)
        imag_part = green_wide(imag_part, first0, shear0, wave_a, wave_b, wave_c)
        real_part, imag_part = lax.optimization_barrier((real_part, imag_part))
        back = inverse(real_part, imag_part, tables)
        field = jnp.where(step < count, macro_field - back, field)
    stress = tangent_wide(field, first, shear, keep, state, gain)
    means = jnp.sum(stress, axis=(3, 4)) / (edge * plane)
    return jnp.transpose(means, (1, 0, 2)).reshape(slots, 36)


def body(damage, strain, route, iters, phase, moduli, tangent_old):
    slots = ACT_DEV
    macro_count = lax.axis_size("macro")
    work_count = lax.axis_size("work")
    devices = macro_count * work_count
    my_macro = lax.axis_index("macro")
    my_work = lax.axis_index("work")
    points, voxels = damage.shape
    width = 7 * voxels
    active = route >= 0
    dest_macro = jnp.where(active, route // slots // work_count, -1)
    macro_ids = jnp.arange(macro_count, dtype=jnp.int32)
    to_macro = dest_macro[None, :] == macro_ids[:, None]
    point_ids = jnp.arange(points, dtype=jnp.int32)
    pick = jnp.max(jnp.where(to_macro, point_ids[None, :], -1), axis=1)
    sending = pick >= 0
    pick = jnp.maximum(pick, 0)
    meta = jnp.stack(
        [route.astype(jnp.float32) + 1.0, iters.astype(jnp.float32), point_ids.astype(jnp.float32) + 1.0]
        + [jnp.zeros((points,), jnp.float32)] * 125,
        axis=1,
    )
    outgoing = jnp.concatenate(
        [damage[pick], strain[pick].reshape(macro_count, 6 * voxels), meta[pick]], axis=1
    )
    outgoing = jnp.where(sending[:, None], outgoing, 0.0)
    arrived = lax.all_to_all(outgoing, "macro", 0, 0, tiled=True)
    valid = arrived[:, width] > 0.5
    rank = jnp.cumsum(valid.astype(jnp.int32)) - 1
    vol_ids = jnp.arange(slots, dtype=jnp.int32)
    select = (valid[None, :] & (rank[None, :] == vol_ids[:, None])).astype(jnp.float32)
    held = jnp.dot(select, arrived, precision=exact)
    held_valid = jnp.sum(select, axis=1) > 0.5
    held_route = (held[:, width] - 1.0).astype(jnp.int32)
    held_count = held[:, width + 1]
    held_row = held[:, width + 2]
    held_from = jnp.dot(select, macro_ids.astype(jnp.float32), precision=exact).astype(jnp.int32)
    tangents = solve_slots(
        held[:, :voxels], held[:, voxels:width].reshape(slots, 6, voxels), held_count, phase, moduli
    )
    dest_ids = jnp.arange(devices, dtype=jnp.int32)
    owner_dev = held_from * work_count + my_work
    to_owner = (held_valid[None, :] & (owner_dev[None, :] == dest_ids[:, None])).astype(jnp.float32)
    owner_part = jnp.dot(
        to_owner, jnp.concatenate([tangents, held_row[:, None]], axis=1), precision=exact
    )
    slot_parts = []
    for s in range(slots):
        hit = held_valid & (held_route == dest_ids[:, None] * slots + s)
        slot_parts.append(jnp.dot(hit.astype(jnp.float32), tangents, precision=exact))
    back = jnp.concatenate([owner_part] + slot_parts, axis=1)
    returned = lax.all_to_all(back, ("macro", "work"), 0, 0, tiled=True)
    row_ids = jnp.arange(points, dtype=jnp.float32) + 1.0
    mine = (returned[None, :, 36] == row_ids[:, None]).astype(jnp.float32)
    chosen = jnp.dot(mine, returned[:, :36], precision=exact)
    tangent = jnp.where(active[:, None], chosen, tangent_old)
    solved = jnp.stack(
        [jnp.sum(returned[:, 37 + 36 * s : 37 + 36 * (s + 1)], axis=0) for s in range(slots)]
    )
    return (tangent, solved)


def solution(mesh):
    return jax.shard_map(
        body,
        mesh=mesh,
        in_specs=(
            P(("macro", "work"), None),
            P(("macro", "work"), None, None),
            P(("macro", "work")),
            P(("macro", "work")),
            P(),
            P(),
            P(("macro", "work"), None),
        ),
        out_specs=(P(("macro", "work"), None), P(("macro", "work"), None)),
        check_vma=False,
    )
```

```python
import numpy as np
import jax
import jax.numpy as jnp
from jax import lax
from jax.sharding import PartitionSpec as P

RES = 16
ITERS = 2
ACT_DEV = 4

exact = lax.Precision.HIGHEST
fast = lax.Precision.HIGH


def moduli_field(phase, moduli):
    first = jnp.where(phase == 1, moduli[1, 0], moduli[0, 0])
    shear = jnp.where(phase == 1, moduli[1, 1], moduli[0, 1])
    return (first, shear)


def elastic(field, first, shear):
    trace = field[0] + field[1] + field[2]
    parts = [2.0 * shear * field[c] + first * trace for c in range(3)]
    parts = parts + [2.0 * shear * field[c] for c in range(3, 6)]
    return jnp.stack(parts)


def contract(left, right):
    diagonal = left[0] * right[0] + left[1] * right[1] + left[2] * right[2]
    return diagonal + 2.0 * (left[3] * right[3] + left[4] * right[4] + left[5] * right[5])


def green(part, first0, shear0, wave_a, wave_b, wave_c):
    norm = wave_a * wave_a + wave_b * wave_b + wave_c * wave_c
    safe = jnp.where(norm > 0, norm, 1.0)
    living = jnp.where(norm > 0, 1.0, 0.0)
    force_a = part[0] * wave_a + part[5] * wave_b + part[4] * wave_c
    force_b = part[5] * wave_a + part[1] * wave_b + part[3] * wave_c
    force_c = part[4] * wave_a + part[3] * wave_b + part[2] * wave_c
    kappa = (first0 + shear0) / (shear0 * (first0 + 2.0 * shear0))
    along = (wave_a * force_a + wave_b * force_b + wave_c * force_c) * kappa / (safe * safe)
    factor = 0.5 / (shear0 * safe)
    parts = [
        factor * 2.0 * wave_a * force_a - along * wave_a * wave_a,
        factor * 2.0 * wave_b * force_b - along * wave_b * wave_b,
        factor * 2.0 * wave_c * force_c - along * wave_c * wave_c,
        factor * (wave_c * force_b + wave_b * force_c) - along * wave_b * wave_c,
        factor * (wave_c * force_a + wave_a * force_c) - along * wave_a * wave_c,
        factor * (wave_b * force_a + wave_a * force_b) - along * wave_a * wave_b,
    ]
    return jnp.stack(parts) * living


def fourier_tables(edge):
    line = np.arange(edge)
    angle_one = (np.outer(line, line) % edge) * (2.0 * np.pi / edge)
    flat = np.arange(edge * edge)
    rows, cols = flat // edge, flat % edge
    angle_two = (np.outer(rows, rows) + np.outer(cols, cols)) % edge
    angle_two = angle_two * (2.0 * np.pi / edge)
    volume = float(edge ** 3)
    return dict(
        cos_one=np.cos(angle_one).astype(np.float32),
        sin_one=np.sin(angle_one).astype(np.float32),
        cos_two=np.cos(angle_two).astype(np.float32),
        nsin_two=(-np.sin(angle_two)).astype(np.float32),
        icos_two=(np.cos(angle_two) / volume).astype(np.float32),
        insin_two=(-np.sin(angle_two) / volume).astype(np.float32),
        plus_two=(np.cos(angle_two) - np.sin(angle_two)).astype(np.float32),
        both_one=np.concatenate([np.cos(angle_one), -np.sin(angle_one)]).astype(np.float32),
        icos_one=(np.cos(angle_one) / volume).astype(np.float32),
        isin_one=(np.sin(angle_one) / volume).astype(np.float32),
        minus_two=(-np.sin(angle_two) - np.cos(angle_two)).astype(np.float32),
    )


def forward(field, tables):
    both_one, cos_two, plus_two, minus_two, icos_one, isin_one = tables
    edge = icos_one.shape[0]
    stacked = jnp.einsum("ka,...al->...kl", both_one, field, precision=fast)
    real_one = stacked[..., :edge, :]
    imag_one = stacked[..., edge:, :]
    both = jnp.matmul(real_one + imag_one, cos_two, precision=fast)
    real_two = both - jnp.matmul(imag_one, plus_two, precision=fast)
    imag_two = both + jnp.matmul(real_one, minus_two, precision=fast)
    return (real_two, imag_two)


def inverse(real_two, imag_two, tables):
    both_one, cos_two, plus_two, minus_two, icos_one, isin_one = tables
    both = jnp.matmul(real_two + imag_two, cos_two, precision=fast)
    real_one = both + jnp.matmul(imag_two, minus_two, precision=fast)
    imag_one = both - jnp.matmul(real_two, plus_two, precision=fast)
    total = jnp.einsum("ka,...kl->...al", icos_one, real_one, precision=fast)
    return total - jnp.einsum("ka,...kl->...al", isin_one, imag_one, precision=fast)


DIAGONAL = np.array([1.0, 1.0, 1.0, 0.0, 0.0, 0.0], np.float32)
DOUBLED = np.array([1.0, 1.0, 1.0, 2.0, 2.0, 2.0], np.float32)
FIRST_AXIS = [0, 1, 2, 1, 0, 0]
SECOND_AXIS = [0, 1, 2, 2, 2, 1]


def lead(values, ndim):
    return jnp.asarray(np.asarray(values, np.float32).reshape((-1,) + (1,) * (ndim - 1)))


def elastic_wide(field, first, shear):
    trace = field[0] + field[1] + field[2]
    return 2.0 * shear * field + first * trace * lead(DIAGONAL, field.ndim)


def contract_wide(left, right):
    return jnp.sum(lead(DOUBLED, left.ndim) * left * right, axis=0)


def tangent_wide(field, first, shear, keep, state, gain):
    weight = gain * contract_wide(field, state)
    return keep * elastic_wide(field, first, shear) - weight * state


def green_wide(part, first0, shear0, wave_a, wave_b, wave_c):
    norm = wave_a * wave_a + wave_b * wave_b + wave_c * wave_c
    safe = jnp.where(norm > 0, norm, 1.0)
    living = jnp.where(norm > 0, 1.0, 0.0)
    force_a = part[0] * wave_a + part[5] * wave_b + part[4] * wave_c
    force_b = part[5] * wave_a + part[1] * wave_b + part[3] * wave_c
    force_c = part[4] * wave_a + part[3] * wave_b + part[2] * wave_c
    kappa = (first0 + shear0) / (shear0 * (first0 + 2.0 * shear0))
    along = (wave_a * force_a + wave_b * force_b + wave_c * force_c) * kappa / (safe * safe)
    factor = 0.5 / (shear0 * safe)
    waves = (wave_a, wave_b, wave_c)
    forces = (force_a, force_b, force_c)
    ndim = part.ndim

    def pick(table, axes):
        total = None
        for d in range(3):
            mask = lead([1.0 if axes[c] == d else 0.0 for c in range(6)], ndim)
            term = mask * table[d]
            total = term if total is None else total + term
        return total

    wave_one, wave_two = pick(waves, FIRST_AXIS), pick(waves, SECOND_AXIS)
    force_one, force_two = pick(forces, FIRST_AXIS), pick(forces, SECOND_AXIS)
    out = factor * (wave_one * force_two + wave_two * force_one) - along * wave_one * wave_two
    return out * living


def signed_waves(index, edge):
    return jnp.where(index < edge // 2, index, index - edge).astype(jnp.float32)


def unit_columns():
    index = jnp.arange(6)
    values = jnp.where(
        index[:, None] == index[None, :], jnp.where(index[:, None] < 3, 1.0, 0.5), 0.0
    )
    return values.astype(jnp.float32)


def solve_slots(held_damage, held_strain, held_count, phase, moduli):
    edge = RES
    plane = edge * edge
    slots = held_damage.shape[0]
    first, shear = moduli_field(phase.reshape(edge, plane), moduli)
    first0 = jnp.mean(moduli[:, 0])
    shear0 = jnp.mean(moduli[:, 1])
    keep = (1.0 - held_damage).reshape(slots, 1, edge, plane)
    state_strain = jnp.transpose(held_strain.reshape(slots, 6, edge, plane), (1, 0, 2, 3))[
        :, :, None
    ]
    state = elastic_wide(state_strain, first, shear)
    gain = keep * shear / (1.0 + contract_wide(state, state))
    flat = jnp.arange(plane, dtype=jnp.int32)
    wave_a = signed_waves(jnp.arange(edge, dtype=jnp.int32), edge)[:, None]
    wave_b = signed_waves(flat // edge, edge)[None, :]
    wave_c = signed_waves(flat % edge, edge)[None, :]
    table = fourier_tables(edge)
    tables = tuple(jnp.asarray(table[k]) for k in ("both_one", "cos_two", "plus_two", "minus_two", "icos_one", "isin_one"))
    macro_field = unit_columns()[:, None, :, None, None]
    field = jnp.broadcast_to(macro_field, (6, slots, 6, edge, plane))
    count = held_count[:, None, None, None]
    for step in range(ITERS):
        polar = tangent_wide(field, first, shear, keep, state, gain) - elastic_wide(field, first0, shear0)
        polar = lax.optimization_barrier(polar)
        real_part, imag_part = forward(polar, tables)
        real_part = green_wide(real_part, first0, shear0, wave_a, wave_b, wave_c)
        imag_part = green_wide(imag_part, first0, shear0, wave_a, wave_b, wave_c)
        real_part, imag_part = lax.optimization_barrier((real_part, imag_part))
        back = inverse(real_part, imag_part, tables)
        field = jnp.where(step < count, macro_field - back, field)
    stress = tangent_wide(field, first, shear, keep, state, gain)
    means = jnp.sum(stress, axis=(3, 4)) / (edge * plane)
    return jnp.transpose(means, (1, 0, 2)).reshape(slots, 36)


def body(damage, strain, route, iters, phase, moduli, tangent_old):
    slots = ACT_DEV
    macro_count = lax.axis_size("macro")
    work_count = lax.axis_size("work")
    devices = macro_count * work_count
    my_macro = lax.axis_index("macro")
    my_work = lax.axis_index("work")
    points, voxels = damage.shape
    active = route >= 0
    dest_macro = jnp.where(active, route // slots // work_count, -1)
    macro_ids = jnp.arange(macro_count, dtype=jnp.int32)
    to_macro = dest_macro[None, :] == macro_ids[:, None]
    point_ids = jnp.arange(points, dtype=jnp.int32)
    pick = jnp.max(jnp.where(to_macro, point_ids[None, :], -1), axis=1)
    sending = pick >= 0
    pick = jnp.maximum(pick, 0)
    lane = jnp.arange(voxels, dtype=jnp.int32)[None, :]
    meta = jnp.where(lane == 0, route.astype(jnp.float32)[:, None] + 1.0, 0.0)
    meta = jnp.where(lane == 1, iters.astype(jnp.float32)[:, None], meta)
    meta = jnp.where(lane == 2, point_ids.astype(jnp.float32)[:, None] + 1.0, meta)
    source = jnp.concatenate([strain, damage[:, None, :], meta[:, None, :]], axis=1)
    outgoing = jnp.where(sending[:, None, None], source[pick], 0.0)
    arrived = lax.all_to_all(outgoing, "macro", 0, 0, tiled=True)
    valid = arrived[:, 7, 0] > 0.5
    rank = jnp.cumsum(valid.astype(jnp.int32)) - 1
    vol_ids = jnp.arange(slots, dtype=jnp.int32)
    select = valid[None, :] & (rank[None, :] == vol_ids[:, None])
    held_valid = jnp.any(select, axis=1)
    held_from = jnp.max(jnp.where(select, macro_ids[None, :], 0), axis=1)
    held = jnp.where(held_valid[:, None, None], arrived[held_from], 0.0)
    held_route = (held[:, 7, 0] - 1.0).astype(jnp.int32)
    held_count = held[:, 7, 1]
    held_row = held[:, 7, 2]
    tangents = solve_slots(held[:, 6], held[:, :6], held_count, phase, moduli)
    dest_ids = jnp.arange(devices, dtype=jnp.int32)
    owner_dev = held_from * work_count + my_work
    to_owner = (held_valid[None, :] & (owner_dev[None, :] == dest_ids[:, None])).astype(jnp.float32)
    owner_part = jnp.dot(
        to_owner, jnp.concatenate([tangents, held_row[:, None]], axis=1), precision=exact
    )
    slot_parts = []
    for s in range(slots):
        hit = held_valid & (held_route == dest_ids[:, None] * slots + s)
        slot_parts.append(jnp.dot(hit.astype(jnp.float32), tangents, precision=exact))
    back = jnp.concatenate([owner_part] + slot_parts, axis=1)
    returned = lax.all_to_all(back, ("macro", "work"), 0, 0, tiled=True)
    row_ids = jnp.arange(points, dtype=jnp.float32) + 1.0
    mine = (returned[None, :, 36] == row_ids[:, None]).astype(jnp.float32)
    chosen = jnp.dot(mine, returned[:, :36], precision=exact)
    tangent = jnp.where(active[:, None], chosen, tangent_old)
    solved = jnp.stack(
        [jnp.sum(returned[:, 37 + 36 * s : 37 + 36 * (s + 1)], axis=0) for s in range(slots)]
    )
    return (tangent, solved)


def solution(mesh):
    return jax.shard_map(
        body,
        mesh=mesh,
        in_specs=(
            P(("macro", "work"), None),
            P(("macro", "work"), None, None),
            P(("macro", "work")),
            P(("macro", "work")),
            P(),
            P(),
            P(("macro", "work"), None),
        ),
        out_specs=(P(("macro", "work"), None), P(("macro", "work"), None)),
        check_vma=False,
    )
```

```python
import numpy as np
import jax
import jax.numpy as jnp
from jax import lax
from jax.sharding import PartitionSpec as P

RES = 16
ITERS = 2
ACT_DEV = 4

exact = lax.Precision.HIGHEST
fast = lax.Precision.HIGH


def moduli_field(phase, moduli):
    first = jnp.where(phase == 1, moduli[1, 0], moduli[0, 0])
    shear = jnp.where(phase == 1, moduli[1, 1], moduli[0, 1])
    return (first, shear)


def elastic(field, first, shear):
    trace = field[0] + field[1] + field[2]
    parts = [2.0 * shear * field[c] + first * trace for c in range(3)]
    parts = parts + [2.0 * shear * field[c] for c in range(3, 6)]
    return jnp.stack(parts)


def contract(left, right):
    diagonal = left[0] * right[0] + left[1] * right[1] + left[2] * right[2]
    return diagonal + 2.0 * (left[3] * right[3] + left[4] * right[4] + left[5] * right[5])


def green(part, first0, shear0, wave_a, wave_b, wave_c):
    norm = wave_a * wave_a + wave_b * wave_b + wave_c * wave_c
    safe = jnp.where(norm > 0, norm, 1.0)
    living = jnp.where(norm > 0, 1.0, 0.0)
    force_a = part[0] * wave_a + part[5] * wave_b + part[4] * wave_c
    force_b = part[5] * wave_a + part[1] * wave_b + part[3] * wave_c
    force_c = part[4] * wave_a + part[3] * wave_b + part[2] * wave_c
    kappa = (first0 + shear0) / (shear0 * (first0 + 2.0 * shear0))
    along = (wave_a * force_a + wave_b * force_b + wave_c * force_c) * kappa / (safe * safe)
    factor = 0.5 / (shear0 * safe)
    parts = [
        factor * 2.0 * wave_a * force_a - along * wave_a * wave_a,
        factor * 2.0 * wave_b * force_b - along * wave_b * wave_b,
        factor * 2.0 * wave_c * force_c - along * wave_c * wave_c,
        factor * (wave_c * force_b + wave_b * force_c) - along * wave_b * wave_c,
        factor * (wave_c * force_a + wave_a * force_c) - along * wave_a * wave_c,
        factor * (wave_b * force_a + wave_a * force_b) - along * wave_a * wave_b,
    ]
    return jnp.stack(parts) * living


def fourier_tables(edge):
    line = np.arange(edge)
    angle_one = (np.outer(line, line) % edge) * (2.0 * np.pi / edge)
    flat = np.arange(edge * edge)
    rows, cols = flat // edge, flat % edge
    angle_two = (np.outer(rows, rows) + np.outer(cols, cols)) % edge
    angle_two = angle_two * (2.0 * np.pi / edge)
    volume = float(edge ** 3)
    return dict(
        cos_one=np.cos(angle_one).astype(np.float32),
        sin_one=np.sin(angle_one).astype(np.float32),
        cos_two=np.cos(angle_two).astype(np.float32),
        nsin_two=(-np.sin(angle_two)).astype(np.float32),
        icos_two=(np.cos(angle_two) / volume).astype(np.float32),
        insin_two=(-np.sin(angle_two) / volume).astype(np.float32),
        plus_two=(np.cos(angle_two) - np.sin(angle_two)).astype(np.float32),
        both_one=np.concatenate([np.cos(angle_one), -np.sin(angle_one)]).astype(np.float32),
        icos_one=(np.cos(angle_one) / volume).astype(np.float32),
        isin_one=(np.sin(angle_one) / volume).astype(np.float32),
        minus_two=(-np.sin(angle_two) - np.cos(angle_two)).astype(np.float32),
    )


def forward(field, tables):
    both_one, cos_two, plus_two, minus_two, icos_one, isin_one = tables
    edge = icos_one.shape[0]
    stacked = jnp.einsum("ka,...al->...kl", both_one, field, precision=fast)
    real_one = stacked[..., :edge, :]
    imag_one = stacked[..., edge:, :]
    both = jnp.matmul(real_one + imag_one, cos_two, precision=fast)
    real_two = both - jnp.matmul(imag_one, plus_two, precision=fast)
    imag_two = both + jnp.matmul(real_one, minus_two, precision=fast)
    return (real_two, imag_two)


def inverse(real_two, imag_two, tables):
    both_one, cos_two, plus_two, minus_two, icos_one, isin_one = tables
    both = jnp.matmul(real_two + imag_two, cos_two, precision=fast)
    real_one = both + jnp.matmul(imag_two, minus_two, precision=fast)
    imag_one = both - jnp.matmul(real_two, plus_two, precision=fast)
    total = jnp.einsum("ka,...kl->...al", icos_one, real_one, precision=fast)
    return total - jnp.einsum("ka,...kl->...al", isin_one, imag_one, precision=fast)


DIAGONAL = np.array([1.0, 1.0, 1.0, 0.0, 0.0, 0.0], np.float32)
DOUBLED = np.array([1.0, 1.0, 1.0, 2.0, 2.0, 2.0], np.float32)
FIRST_AXIS = [0, 1, 2, 1, 0, 0]
SECOND_AXIS = [0, 1, 2, 2, 2, 1]


def lead(values, ndim):
    return jnp.asarray(np.asarray(values, np.float32).reshape((-1,) + (1,) * (ndim - 1)))


def elastic_wide(field, first, shear):
    trace = field[0] + field[1] + field[2]
    return 2.0 * shear * field + first * trace * lead(DIAGONAL, field.ndim)


def contract_wide(left, right):
    return jnp.sum(lead(DOUBLED, left.ndim) * left * right, axis=0)


def tangent_wide(field, first, shear, keep, state, gain):
    weight = gain * contract_wide(field, state)
    return keep * elastic_wide(field, first, shear) - weight * state


def green_wide(part, first0, shear0, wave_a, wave_b, wave_c):
    norm = wave_a * wave_a + wave_b * wave_b + wave_c * wave_c
    safe = jnp.where(norm > 0, norm, 1.0)
    living = jnp.where(norm > 0, 1.0, 0.0)
    force_a = part[0] * wave_a + part[5] * wave_b + part[4] * wave_c
    force_b = part[5] * wave_a + part[1] * wave_b + part[3] * wave_c
    force_c = part[4] * wave_a + part[3] * wave_b + part[2] * wave_c
    kappa = (first0 + shear0) / (shear0 * (first0 + 2.0 * shear0))
    along = (wave_a * force_a + wave_b * force_b + wave_c * force_c) * kappa / (safe * safe)
    factor = 0.5 / (shear0 * safe)
    waves = (wave_a, wave_b, wave_c)
    forces = (force_a, force_b, force_c)
    ndim = part.ndim

    def pick(table, axes):
        total = None
        for d in range(3):
            mask = lead([1.0 if axes[c] == d else 0.0 for c in range(6)], ndim)
            term = mask * table[d]
            total = term if total is None else total + term
        return total

    wave_one, wave_two = pick(waves, FIRST_AXIS), pick(waves, SECOND_AXIS)
    force_one, force_two = pick(forces, FIRST_AXIS), pick(forces, SECOND_AXIS)
    out = factor * (wave_one * force_two + wave_two * force_one) - along * wave_one * wave_two
    return out * living


def signed_waves(index, edge):
    return jnp.where(index < edge // 2, index, index - edge).astype(jnp.float32)


def unit_columns():
    index = jnp.arange(6)
    values = jnp.where(
        index[:, None] == index[None, :], jnp.where(index[:, None] < 3, 1.0, 0.5), 0.0
    )
    return values.astype(jnp.float32)


def solve_slots(held_damage, held_strain, held_count, phase, moduli):
    edge = RES
    plane = edge * edge
    slots = held_damage.shape[0]
    first, shear = moduli_field(phase.reshape(edge, plane), moduli)
    first0 = jnp.mean(moduli[:, 0])
    shear0 = jnp.mean(moduli[:, 1])
    keep = (1.0 - held_damage).reshape(slots, 1, edge, plane)
    state_strain = jnp.transpose(held_strain.reshape(slots, 6, edge, plane), (1, 0, 2, 3))[
        :, :, None
    ]
    state = elastic_wide(state_strain, first, shear)
    gain = keep * shear / (1.0 + contract_wide(state, state))
    flat = jnp.arange(plane, dtype=jnp.int32)
    wave_a = signed_waves(jnp.arange(edge, dtype=jnp.int32), edge)[:, None]
    wave_b = signed_waves(flat // edge, edge)[None, :]
    wave_c = signed_waves(flat % edge, edge)[None, :]
    table = fourier_tables(edge)
    tables = tuple(jnp.asarray(table[k]) for k in ("both_one", "cos_two", "plus_two", "minus_two", "icos_one", "isin_one"))
    macro_field = unit_columns()[:, None, :, None, None]
    field = jnp.broadcast_to(macro_field, (6, slots, 6, edge, plane))
    count = held_count[:, None, None, None]
    def iteration(step, field):
        polar = tangent_wide(field, first, shear, keep, state, gain) - elastic_wide(field, first0, shear0)
        polar = lax.optimization_barrier(polar)
        real_part, imag_part = forward(polar, tables)
        real_part = green_wide(real_part, first0, shear0, wave_a, wave_b, wave_c)
        imag_part = green_wide(imag_part, first0, shear0, wave_a, wave_b, wave_c)
        real_part, imag_part = lax.optimization_barrier((real_part, imag_part))
        back = inverse(real_part, imag_part, tables)
        return jnp.where(step < count, macro_field - back, field)

    field = lax.fori_loop(0, ITERS, iteration, field)
    stress = tangent_wide(field, first, shear, keep, state, gain)
    means = jnp.sum(stress, axis=(3, 4)) / (edge * plane)
    return jnp.transpose(means, (1, 0, 2)).reshape(slots, 36)


def body(damage, strain, route, iters, phase, moduli, tangent_old):
    slots = ACT_DEV
    macro_count = lax.axis_size("macro")
    work_count = lax.axis_size("work")
    devices = macro_count * work_count
    my_macro = lax.axis_index("macro")
    my_work = lax.axis_index("work")
    points, voxels = damage.shape
    width = 7 * voxels
    active = route >= 0
    dest_macro = jnp.where(active, route // slots // work_count, -1)
    macro_ids = jnp.arange(macro_count, dtype=jnp.int32)
    to_macro = dest_macro[None, :] == macro_ids[:, None]
    point_ids = jnp.arange(points, dtype=jnp.int32)
    pick = jnp.max(jnp.where(to_macro, point_ids[None, :], -1), axis=1)
    sending = pick >= 0
    pick = jnp.maximum(pick, 0)
    meta = jnp.stack(
        [route.astype(jnp.float32) + 1.0, iters.astype(jnp.float32), point_ids.astype(jnp.float32) + 1.0]
        + [jnp.zeros((points,), jnp.float32)] * 125,
        axis=1,
    )
    outgoing = jnp.concatenate(
        [damage[pick], strain[pick].reshape(macro_count, 6 * voxels), meta[pick]], axis=1
    )
    outgoing = jnp.where(sending[:, None], outgoing, 0.0)
    arrived = lax.all_to_all(outgoing, "macro", 0, 0, tiled=True)
    valid = arrived[:, width] > 0.5
    rank = jnp.cumsum(valid.astype(jnp.int32)) - 1
    vol_ids = jnp.arange(slots, dtype=jnp.int32)
    select = (valid[None, :] & (rank[None, :] == vol_ids[:, None])).astype(jnp.float32)
    held = jnp.dot(select, arrived, precision=exact)
    held_valid = jnp.sum(select, axis=1) > 0.5
    held_route = (held[:, width] - 1.0).astype(jnp.int32)
    held_count = held[:, width + 1]
    held_row = held[:, width + 2]
    held_from = jnp.dot(select, macro_ids.astype(jnp.float32), precision=exact).astype(jnp.int32)
    tangents = solve_slots(
        held[:, :voxels], held[:, voxels:width].reshape(slots, 6, voxels), held_count, phase, moduli
    )
    dest_ids = jnp.arange(devices, dtype=jnp.int32)
    owner_dev = held_from * work_count + my_work
    to_owner = (held_valid[None, :] & (owner_dev[None, :] == dest_ids[:, None])).astype(jnp.float32)
    owner_part = jnp.dot(
        to_owner, jnp.concatenate([tangents, held_row[:, None]], axis=1), precision=exact
    )
    slot_parts = []
    for s in range(slots):
        hit = held_valid & (held_route == dest_ids[:, None] * slots + s)
        slot_parts.append(jnp.dot(hit.astype(jnp.float32), tangents, precision=exact))
    back = jnp.concatenate([owner_part] + slot_parts, axis=1)
    returned = lax.all_to_all(back, ("macro", "work"), 0, 0, tiled=True)
    row_ids = jnp.arange(points, dtype=jnp.float32) + 1.0
    mine = (returned[None, :, 36] == row_ids[:, None]).astype(jnp.float32)
    chosen = jnp.dot(mine, returned[:, :36], precision=exact)
    tangent = jnp.where(active[:, None], chosen, tangent_old)
    solved = jnp.stack(
        [jnp.sum(returned[:, 37 + 36 * s : 37 + 36 * (s + 1)], axis=0) for s in range(slots)]
    )
    return (tangent, solved)


def solution(mesh):
    return jax.shard_map(
        body,
        mesh=mesh,
        in_specs=(
            P(("macro", "work"), None),
            P(("macro", "work"), None, None),
            P(("macro", "work")),
            P(("macro", "work")),
            P(),
            P(),
            P(("macro", "work"), None),
        ),
        out_specs=(P(("macro", "work"), None), P(("macro", "work"), None)),
        check_vma=False,
    )
```

```python
import numpy as np
import jax
import jax.numpy as jnp
from jax import lax
from jax.sharding import PartitionSpec as P

RES = 16
ITERS = 2
ACT_DEV = 4

exact = lax.Precision.HIGHEST
fast = lax.Precision.HIGH


def moduli_field(phase, moduli):
    first = jnp.where(phase == 1, moduli[1, 0], moduli[0, 0])
    shear = jnp.where(phase == 1, moduli[1, 1], moduli[0, 1])
    return (first, shear)


def elastic(field, first, shear):
    trace = field[0] + field[1] + field[2]
    parts = [2.0 * shear * field[c] + first * trace for c in range(3)]
    parts = parts + [2.0 * shear * field[c] for c in range(3, 6)]
    return jnp.stack(parts)


def contract(left, right):
    diagonal = left[0] * right[0] + left[1] * right[1] + left[2] * right[2]
    return diagonal + 2.0 * (left[3] * right[3] + left[4] * right[4] + left[5] * right[5])


def green(part, first0, shear0, wave_a, wave_b, wave_c):
    norm = wave_a * wave_a + wave_b * wave_b + wave_c * wave_c
    safe = jnp.where(norm > 0, norm, 1.0)
    living = jnp.where(norm > 0, 1.0, 0.0)
    force_a = part[0] * wave_a + part[5] * wave_b + part[4] * wave_c
    force_b = part[5] * wave_a + part[1] * wave_b + part[3] * wave_c
    force_c = part[4] * wave_a + part[3] * wave_b + part[2] * wave_c
    kappa = (first0 + shear0) / (shear0 * (first0 + 2.0 * shear0))
    along = (wave_a * force_a + wave_b * force_b + wave_c * force_c) * kappa / (safe * safe)
    factor = 0.5 / (shear0 * safe)
    parts = [
        factor * 2.0 * wave_a * force_a - along * wave_a * wave_a,
        factor * 2.0 * wave_b * force_b - along * wave_b * wave_b,
        factor * 2.0 * wave_c * force_c - along * wave_c * wave_c,
        factor * (wave_c * force_b + wave_b * force_c) - along * wave_b * wave_c,
        factor * (wave_c * force_a + wave_a * force_c) - along * wave_a * wave_c,
        factor * (wave_b * force_a + wave_a * force_b) - along * wave_a * wave_b,
    ]
    return jnp.stack(parts) * living


def fourier_tables(edge):
    line = np.arange(edge)
    angle_one = (np.outer(line, line) % edge) * (2.0 * np.pi / edge)
    flat = np.arange(edge * edge)
    rows, cols = flat // edge, flat % edge
    angle_two = (np.outer(rows, rows) + np.outer(cols, cols)) % edge
    angle_two = angle_two * (2.0 * np.pi / edge)
    volume = float(edge ** 3)
    return dict(
        cos_one=np.cos(angle_one).astype(np.float32),
        sin_one=np.sin(angle_one).astype(np.float32),
        cos_two=np.cos(angle_two).astype(np.float32),
        nsin_two=(-np.sin(angle_two)).astype(np.float32),
        icos_two=(np.cos(angle_two) / volume).astype(np.float32),
        insin_two=(-np.sin(angle_two) / volume).astype(np.float32),
        plus_two=(np.cos(angle_two) - np.sin(angle_two)).astype(np.float32),
        both_one=np.concatenate([np.cos(angle_one), -np.sin(angle_one)]).astype(np.float32),
        icos_one=(np.cos(angle_one) / volume).astype(np.float32),
        isin_one=(np.sin(angle_one) / volume).astype(np.float32),
        minus_two=(-np.sin(angle_two) - np.cos(angle_two)).astype(np.float32),
    )


def forward(field, tables):
    both_one, cos_two, plus_two, minus_two, icos_one, isin_one = tables
    edge = icos_one.shape[0]
    stacked = jnp.einsum("ka,...al->...kl", both_one, field, precision=fast)
    real_one = stacked[..., :edge, :]
    imag_one = stacked[..., edge:, :]
    both = jnp.matmul(real_one + imag_one, cos_two, precision=fast)
    real_two = both - jnp.matmul(imag_one, plus_two, precision=fast)
    imag_two = both + jnp.matmul(real_one, minus_two, precision=fast)
    return (real_two, imag_two)


def inverse(real_two, imag_two, tables):
    both_one, cos_two, plus_two, minus_two, icos_one, isin_one = tables
    both = jnp.matmul(real_two + imag_two, cos_two, precision=fast)
    real_one = both + jnp.matmul(imag_two, minus_two, precision=fast)
    imag_one = both - jnp.matmul(real_two, plus_two, precision=fast)
    total = jnp.einsum("ka,...kl->...al", icos_one, real_one, precision=fast)
    return total - jnp.einsum("ka,...kl->...al", isin_one, imag_one, precision=fast)


DIAGONAL = np.array([1.0, 1.0, 1.0, 0.0, 0.0, 0.0], np.float32)
DOUBLED = np.array([1.0, 1.0, 1.0, 2.0, 2.0, 2.0], np.float32)
FIRST_AXIS = [0, 1, 2, 1, 0, 0]
SECOND_AXIS = [0, 1, 2, 2, 2, 1]


def lead(values, ndim):
    return jnp.asarray(np.asarray(values, np.float32).reshape((-1,) + (1,) * (ndim - 1)))


def elastic_wide(field, first, shear):
    trace = field[0] + field[1] + field[2]
    return 2.0 * shear * field + first * trace * lead(DIAGONAL, field.ndim)


def contract_wide(left, right):
    return jnp.sum(lead(DOUBLED, left.ndim) * left * right, axis=0)


def tangent_wide(field, first, shear, keep, state, gain):
    weight = gain * contract_wide(field, state)
    return keep * elastic_wide(field, first, shear) - weight * state


def green_wide(part, first0, shear0, wave_a, wave_b, wave_c):
    norm = wave_a * wave_a + wave_b * wave_b + wave_c * wave_c
    safe = jnp.where(norm > 0, norm, 1.0)
    living = jnp.where(norm > 0, 1.0, 0.0)
    force_a = part[0] * wave_a + part[5] * wave_b + part[4] * wave_c
    force_b = part[5] * wave_a + part[1] * wave_b + part[3] * wave_c
    force_c = part[4] * wave_a + part[3] * wave_b + part[2] * wave_c
    kappa = (first0 + shear0) / (shear0 * (first0 + 2.0 * shear0))
    along = (wave_a * force_a + wave_b * force_b + wave_c * force_c) * kappa / (safe * safe)
    factor = 0.5 / (shear0 * safe)
    waves = (wave_a, wave_b, wave_c)
    forces = (force_a, force_b, force_c)
    ndim = part.ndim

    def pick(table, axes):
        total = None
        for d in range(3):
            mask = lead([1.0 if axes[c] == d else 0.0 for c in range(6)], ndim)
            term = mask * table[d]
            total = term if total is None else total + term
        return total

    wave_one, wave_two = pick(waves, FIRST_AXIS), pick(waves, SECOND_AXIS)
    force_one, force_two = pick(forces, FIRST_AXIS), pick(forces, SECOND_AXIS)
    out = factor * (wave_one * force_two + wave_two * force_one) - along * wave_one * wave_two
    return out * living


def signed_waves(index, edge):
    return jnp.where(index < edge // 2, index, index - edge).astype(jnp.float32)


def unit_columns():
    index = jnp.arange(6)
    values = jnp.where(
        index[:, None] == index[None, :], jnp.where(index[:, None] < 3, 1.0, 0.5), 0.0
    )
    return values.astype(jnp.float32)


def solve_slots(held_damage, held_strain, held_count, phase, moduli):
    edge = RES
    plane = edge * edge
    slots = held_damage.shape[0]
    first, shear = moduli_field(phase.reshape(edge, plane), moduli)
    first0 = jnp.mean(moduli[:, 0])
    shear0 = jnp.mean(moduli[:, 1])
    keep = (1.0 - held_damage).reshape(slots, 1, edge, plane)
    state_strain = jnp.transpose(held_strain.reshape(slots, 6, edge, plane), (1, 0, 2, 3))[
        :, :, None
    ]
    state = elastic_wide(state_strain, first, shear)
    gain = keep * shear / (1.0 + contract_wide(state, state))
    flat = jnp.arange(plane, dtype=jnp.int32)
    wave_a = signed_waves(jnp.arange(edge, dtype=jnp.int32), edge)[:, None]
    wave_b = signed_waves(flat // edge, edge)[None, :]
    wave_c = signed_waves(flat % edge, edge)[None, :]
    table = fourier_tables(edge)
    tables = tuple(jnp.asarray(table[k]) for k in ("both_one", "cos_two", "plus_two", "minus_two", "icos_one", "isin_one"))
    macro_field = unit_columns()[:, None, :, None, None]
    field = jnp.broadcast_to(macro_field, (6, slots, 6, edge, plane))
    count = held_count[:, None, None, None]
    polar = tangent_wide(field, first, shear, keep, state, gain) - elastic_wide(field, first0, shear0)
    polar = lax.optimization_barrier(polar)
    spec0_re, spec0_im = forward(polar, tables)
    g1_re = green_wide(spec0_re, first0, shear0, wave_a, wave_b, wave_c)
    g1_im = green_wide(spec0_im, first0, shear0, wave_a, wave_b, wave_c)
    g1_re, g1_im = lax.optimization_barrier((g1_re, g1_im))
    back = inverse(g1_re, g1_im, tables)
    field = jnp.where(0 < count, macro_field - back, field)
    polar = tangent_wide(field, first, shear, keep, state, gain) - elastic_wide(field, first0, shear0)
    polar = lax.optimization_barrier(polar)
    spec1_re, spec1_im = forward(polar, tables)
    g2_re = green_wide(spec1_re, first0, shear0, wave_a, wave_b, wave_c)
    g2_im = green_wide(spec1_im, first0, shear0, wave_a, wave_b, wave_c)
    gf_re = jnp.where(count >= 2, g2_re, jnp.where(count >= 1, g1_re, 0.0))
    gf_im = jnp.where(count >= 2, g2_im, jnp.where(count >= 1, g1_im, 0.0))
    voxels = edge * plane
    inv_unit = np.array([1.0, 1.0, 1.0, 2.0, 2.0, 2.0], np.float32) / float(voxels * voxels)
    acc = None
    for l in range(6):
        term = inv_unit[l] * (
            spec0_re[:, :, l, None] * gf_re[l][None] + spec0_im[:, :, l, None] * gf_im[l][None]
        )
        acc = term if acc is None else acc + term
    coupled = jnp.sum(acc, axis=(3, 4))
    dc = spec0_re[:, :, :, 0, 0] / float(voxels)
    base = np.zeros((2, 6, 6), np.float32)
    for i in range(6):
        for j in range(6):
            base[0, i, j] = 1.0 if (i < 3 and j < 3) else 0.0
            base[1, i, j] = (2.0 * (1.0 if j < 3 else 0.5)) if i == j else 0.0
    c0e = first0 * jnp.asarray(base[0]) + shear0 * jnp.asarray(base[1])
    means = dc + c0e[:, None, :] - coupled
    return jnp.transpose(means, (1, 0, 2)).reshape(slots, 36)


def body(damage, strain, route, iters, phase, moduli, tangent_old):
    slots = ACT_DEV
    macro_count = lax.axis_size("macro")
    work_count = lax.axis_size("work")
    devices = macro_count * work_count
    my_macro = lax.axis_index("macro")
    my_work = lax.axis_index("work")
    points, voxels = damage.shape
    width = 7 * voxels
    active = route >= 0
    dest_macro = jnp.where(active, route // slots // work_count, -1)
    macro_ids = jnp.arange(macro_count, dtype=jnp.int32)
    to_macro = dest_macro[None, :] == macro_ids[:, None]
    point_ids = jnp.arange(points, dtype=jnp.int32)
    pick = jnp.max(jnp.where(to_macro, point_ids[None, :], -1), axis=1)
    sending = pick >= 0
    pick = jnp.maximum(pick, 0)
    meta = jnp.stack(
        [route.astype(jnp.float32) + 1.0, iters.astype(jnp.float32), point_ids.astype(jnp.float32) + 1.0]
        + [jnp.zeros((points,), jnp.float32)] * 125,
        axis=1,
    )
    outgoing = jnp.concatenate(
        [damage[pick], strain[pick].reshape(macro_count, 6 * voxels), meta[pick]], axis=1
    )
    outgoing = jnp.where(sending[:, None], outgoing, 0.0)
    arrived = lax.all_to_all(outgoing, "macro", 0, 0, tiled=True)
    valid = arrived[:, width] > 0.5
    rank = jnp.cumsum(valid.astype(jnp.int32)) - 1
    vol_ids = jnp.arange(slots, dtype=jnp.int32)
    select = (valid[None, :] & (rank[None, :] == vol_ids[:, None])).astype(jnp.float32)
    held = jnp.dot(select, arrived, precision=exact)
    held_valid = jnp.sum(select, axis=1) > 0.5
    held_route = (held[:, width] - 1.0).astype(jnp.int32)
    held_count = held[:, width + 1]
    held_row = held[:, width + 2]
    held_from = jnp.dot(select, macro_ids.astype(jnp.float32), precision=exact).astype(jnp.int32)
    tangents = solve_slots(
        held[:, :voxels], held[:, voxels:width].reshape(slots, 6, voxels), held_count, phase, moduli
    )
    dest_ids = jnp.arange(devices, dtype=jnp.int32)
    owner_dev = held_from * work_count + my_work
    to_owner = (held_valid[None, :] & (owner_dev[None, :] == dest_ids[:, None])).astype(jnp.float32)
    owner_part = jnp.dot(
        to_owner, jnp.concatenate([tangents, held_row[:, None]], axis=1), precision=exact
    )
    slot_parts = []
    for s in range(slots):
        hit = held_valid & (held_route == dest_ids[:, None] * slots + s)
        slot_parts.append(jnp.dot(hit.astype(jnp.float32), tangents, precision=exact))
    back = jnp.concatenate([owner_part] + slot_parts, axis=1)
    returned = lax.all_to_all(back, ("macro", "work"), 0, 0, tiled=True)
    row_ids = jnp.arange(points, dtype=jnp.float32) + 1.0
    mine = (returned[None, :, 36] == row_ids[:, None]).astype(jnp.float32)
    chosen = jnp.dot(mine, returned[:, :36], precision=exact)
    tangent = jnp.where(active[:, None], chosen, tangent_old)
    solved = jnp.stack(
        [jnp.sum(returned[:, 37 + 36 * s : 37 + 36 * (s + 1)], axis=0) for s in range(slots)]
    )
    return (tangent, solved)


def solution(mesh):
    return jax.shard_map(
        body,
        mesh=mesh,
        in_specs=(
            P(("macro", "work"), None),
            P(("macro", "work"), None, None),
            P(("macro", "work")),
            P(("macro", "work")),
            P(),
            P(),
            P(("macro", "work"), None),
        ),
        out_specs=(P(("macro", "work"), None), P(("macro", "work"), None)),
        check_vma=False,
    )
```

```python
import numpy as np
import jax
import jax.numpy as jnp
from jax import lax
from jax.sharding import PartitionSpec as P

RES = 16
ITERS = 2
ACT_DEV = 4

exact = lax.Precision.HIGHEST
fast = lax.Precision.HIGH


def moduli_field(phase, moduli):
    first = jnp.where(phase == 1, moduli[1, 0], moduli[0, 0])
    shear = jnp.where(phase == 1, moduli[1, 1], moduli[0, 1])
    return (first, shear)


def elastic(field, first, shear):
    trace = field[0] + field[1] + field[2]
    parts = [2.0 * shear * field[c] + first * trace for c in range(3)]
    parts = parts + [2.0 * shear * field[c] for c in range(3, 6)]
    return jnp.stack(parts)


def contract(left, right):
    diagonal = left[0] * right[0] + left[1] * right[1] + left[2] * right[2]
    return diagonal + 2.0 * (left[3] * right[3] + left[4] * right[4] + left[5] * right[5])


def green(part, first0, shear0, wave_a, wave_b, wave_c):
    norm = wave_a * wave_a + wave_b * wave_b + wave_c * wave_c
    safe = jnp.where(norm > 0, norm, 1.0)
    living = jnp.where(norm > 0, 1.0, 0.0)
    force_a = part[0] * wave_a + part[5] * wave_b + part[4] * wave_c
    force_b = part[5] * wave_a + part[1] * wave_b + part[3] * wave_c
    force_c = part[4] * wave_a + part[3] * wave_b + part[2] * wave_c
    kappa = (first0 + shear0) / (shear0 * (first0 + 2.0 * shear0))
    along = (wave_a * force_a + wave_b * force_b + wave_c * force_c) * kappa / (safe * safe)
    factor = 0.5 / (shear0 * safe)
    parts = [
        factor * 2.0 * wave_a * force_a - along * wave_a * wave_a,
        factor * 2.0 * wave_b * force_b - along * wave_b * wave_b,
        factor * 2.0 * wave_c * force_c - along * wave_c * wave_c,
        factor * (wave_c * force_b + wave_b * force_c) - along * wave_b * wave_c,
        factor * (wave_c * force_a + wave_a * force_c) - along * wave_a * wave_c,
        factor * (wave_b * force_a + wave_a * force_b) - along * wave_a * wave_b,
    ]
    return jnp.stack(parts) * living


def fourier_tables(edge):
    line = np.arange(edge)
    angle_one = (np.outer(line, line) % edge) * (2.0 * np.pi / edge)
    flat = np.arange(edge * edge)
    rows, cols = flat // edge, flat % edge
    angle_two = (np.outer(rows, rows) + np.outer(cols, cols)) % edge
    angle_two = angle_two * (2.0 * np.pi / edge)
    volume = float(edge ** 3)
    return dict(
        cos_one=np.cos(angle_one).astype(np.float32),
        sin_one=np.sin(angle_one).astype(np.float32),
        cos_two=np.cos(angle_two).astype(np.float32),
        nsin_two=(-np.sin(angle_two)).astype(np.float32),
        icos_two=(np.cos(angle_two) / volume).astype(np.float32),
        insin_two=(-np.sin(angle_two) / volume).astype(np.float32),
        plus_two=(np.cos(angle_two) - np.sin(angle_two)).astype(np.float32),
        both_one=np.concatenate([np.cos(angle_one), -np.sin(angle_one)]).astype(np.float32),
        icos_one=(np.cos(angle_one) / volume).astype(np.float32),
        isin_one=(np.sin(angle_one) / volume).astype(np.float32),
        minus_two=(-np.sin(angle_two) - np.cos(angle_two)).astype(np.float32),
    )


def forward(field, tables):
    both_one, cos_two, plus_two, minus_two, icos_one, isin_one = tables
    edge = icos_one.shape[0]
    stacked = jnp.einsum("ka,...al->...kl", both_one, field, precision=fast)
    real_one = stacked[..., :edge, :]
    imag_one = stacked[..., edge:, :]
    both = jnp.matmul(real_one + imag_one, cos_two, precision=fast)
    real_two = both - jnp.matmul(imag_one, plus_two, precision=fast)
    imag_two = both + jnp.matmul(real_one, minus_two, precision=fast)
    return (real_two, imag_two)


def inverse(real_two, imag_two, tables):
    both_one, cos_two, plus_two, minus_two, icos_one, isin_one = tables
    both = jnp.matmul(real_two + imag_two, cos_two, precision=fast)
    real_one = both + jnp.matmul(imag_two, minus_two, precision=fast)
    imag_one = both - jnp.matmul(real_two, plus_two, precision=fast)
    total = jnp.einsum("ka,...kl->...al", icos_one, real_one, precision=fast)
    return total - jnp.einsum("ka,...kl->...al", isin_one, imag_one, precision=fast)


DIAGONAL = np.array([1.0, 1.0, 1.0, 0.0, 0.0, 0.0], np.float32)
DOUBLED = np.array([1.0, 1.0, 1.0, 2.0, 2.0, 2.0], np.float32)
FIRST_AXIS = [0, 1, 2, 1, 0, 0]
SECOND_AXIS = [0, 1, 2, 2, 2, 1]


def lead(values, ndim):
    return jnp.asarray(np.asarray(values, np.float32).reshape((-1,) + (1,) * (ndim - 1)))


def elastic_wide(field, first, shear):
    trace = field[0] + field[1] + field[2]
    return 2.0 * shear * field + first * trace * lead(DIAGONAL, field.ndim)


def contract_wide(left, right):
    return jnp.sum(lead(DOUBLED, left.ndim) * left * right, axis=0)


def tangent_wide(field, first, shear, keep, state, gain):
    weight = gain * contract_wide(field, state)
    return keep * elastic_wide(field, first, shear) - weight * state


def green_wide(part, first0, shear0, wave_a, wave_b, wave_c):
    norm = wave_a * wave_a + wave_b * wave_b + wave_c * wave_c
    safe = jnp.where(norm > 0, norm, 1.0)
    living = jnp.where(norm > 0, 1.0, 0.0)
    force_a = part[0] * wave_a + part[5] * wave_b + part[4] * wave_c
    force_b = part[5] * wave_a + part[1] * wave_b + part[3] * wave_c
    force_c = part[4] * wave_a + part[3] * wave_b + part[2] * wave_c
    kappa = (first0 + shear0) / (shear0 * (first0 + 2.0 * shear0))
    along = (wave_a * force_a + wave_b * force_b + wave_c * force_c) * kappa / (safe * safe)
    factor = 0.5 / (shear0 * safe)
    waves = (wave_a, wave_b, wave_c)
    forces = (force_a, force_b, force_c)
    ndim = part.ndim

    def pick(table, axes):
        total = None
        for d in range(3):
            mask = lead([1.0 if axes[c] == d else 0.0 for c in range(6)], ndim)
            term = mask * table[d]
            total = term if total is None else total + term
        return total

    wave_one, wave_two = pick(waves, FIRST_AXIS), pick(waves, SECOND_AXIS)
    force_one, force_two = pick(forces, FIRST_AXIS), pick(forces, SECOND_AXIS)
    out = factor * (wave_one * force_two + wave_two * force_one) - along * wave_one * wave_two
    return out * living


def signed_waves(index, edge):
    return jnp.where(index < edge // 2, index, index - edge).astype(jnp.float32)


def unit_columns():
    index = jnp.arange(6)
    values = jnp.where(
        index[:, None] == index[None, :], jnp.where(index[:, None] < 3, 1.0, 0.5), 0.0
    )
    return values.astype(jnp.float32)


def solve_slots(held_damage, held_strain, held_count, phase, moduli):
    edge = RES
    plane = edge * edge
    slots = held_damage.shape[0]
    first, shear = moduli_field(phase.reshape(edge, plane), moduli)
    first0 = jnp.mean(moduli[:, 0])
    shear0 = jnp.mean(moduli[:, 1])
    keep = (1.0 - held_damage).reshape(slots, 1, edge, plane)
    state_strain = jnp.transpose(held_strain.reshape(slots, 6, edge, plane), (1, 0, 2, 3))[
        :, :, None
    ]
    state = elastic_wide(state_strain, first, shear)
    gain = keep * shear / (1.0 + contract_wide(state, state))
    flat = jnp.arange(plane, dtype=jnp.int32)
    wave_a = signed_waves(jnp.arange(edge, dtype=jnp.int32), edge)[:, None]
    wave_b = signed_waves(flat // edge, edge)[None, :]
    wave_c = signed_waves(flat % edge, edge)[None, :]
    table = fourier_tables(edge)
    tables = tuple(jnp.asarray(table[k]) for k in ("both_one", "cos_two", "plus_two", "minus_two", "icos_one", "isin_one"))
    macro_field = unit_columns()[:, None, :, None, None]
    field = jnp.broadcast_to(macro_field, (6, slots, 6, edge, plane))
    count = held_count[:, None, None, None]
    for step in range(ITERS):
        polar = tangent_wide(field, first, shear, keep, state, gain) - elastic_wide(field, first0, shear0)
        polar = lax.optimization_barrier(polar)
        real_part, imag_part = forward(polar, tables)
        real_part = green_wide(real_part, first0, shear0, wave_a, wave_b, wave_c)
        imag_part = green_wide(imag_part, first0, shear0, wave_a, wave_b, wave_c)
        real_part, imag_part = lax.optimization_barrier((real_part, imag_part))
        back = inverse(real_part, imag_part, tables)
        field = jnp.where(step < count, macro_field - back, field)
    stress = tangent_wide(field, first, shear, keep, state, gain)
    means = jnp.sum(stress, axis=(3, 4)) / (edge * plane)
    return jnp.transpose(means, (1, 0, 2)).reshape(slots, 36)


def body(damage, strain, route, iters, phase, moduli, tangent_old):
    slots = ACT_DEV
    macro_count = lax.axis_size("macro")
    work_count = lax.axis_size("work")
    devices = macro_count * work_count
    my_macro = lax.axis_index("macro")
    my_work = lax.axis_index("work")
    points, voxels = damage.shape
    width = 7 * voxels
    active = route >= 0
    dest_macro = jnp.where(active, route // slots // work_count, -1)
    macro_ids = jnp.arange(macro_count, dtype=jnp.int32)
    to_macro = dest_macro[None, :] == macro_ids[:, None]
    point_ids = jnp.arange(points, dtype=jnp.int32)
    pick = jnp.max(jnp.where(to_macro, point_ids[None, :], -1), axis=1)
    sending = pick >= 0
    pick = jnp.maximum(pick, 0)
    meta = jnp.stack(
        [route.astype(jnp.float32) + 1.0, iters.astype(jnp.float32), point_ids.astype(jnp.float32) + 1.0]
        + [jnp.zeros((points,), jnp.float32)] * 125,
        axis=1,
    )
    outgoing = jnp.concatenate(
        [damage[pick], strain[pick].reshape(macro_count, 6 * voxels), meta[pick]], axis=1
    )
    outgoing = jnp.where(sending[:, None], outgoing, 0.0)
    arrived = lax.all_to_all(outgoing, "macro", 0, 0, tiled=True)
    valid = arrived[:, width] > 0.5
    rank = jnp.cumsum(valid.astype(jnp.int32)) - 1
    vol_ids = jnp.arange(slots, dtype=jnp.int32)
    select = valid[None, :] & (rank[None, :] == vol_ids[:, None])
    held_valid = jnp.any(select, axis=1)
    held_at = jnp.max(jnp.where(select, macro_ids[None, :], 0), axis=1)
    held = jnp.where(held_valid[:, None], arrived[held_at], 0.0)
    held_route = (held[:, width] - 1.0).astype(jnp.int32)
    held_count = held[:, width + 1]
    held_row = held[:, width + 2]
    held_from = held_at
    tangents = solve_slots(
        held[:, :voxels], held[:, voxels:width].reshape(slots, 6, voxels), held_count, phase, moduli
    )
    dest_ids = jnp.arange(devices, dtype=jnp.int32)
    owner_dev = held_from * work_count + my_work
    to_owner = held_valid[None, :] & (owner_dev[None, :] == dest_ids[:, None])
    owner_rows = jnp.concatenate([tangents, held_row[:, None]], axis=1)
    owner_part = jnp.sum(jnp.where(to_owner[:, :, None], owner_rows[None], 0.0), axis=1)
    slot_parts = []
    for s in range(slots):
        hit = held_valid & (held_route == dest_ids[:, None] * slots + s)
        slot_parts.append(jnp.sum(jnp.where(hit[:, :, None], tangents[None], 0.0), axis=1))
    back = jnp.concatenate([owner_part] + slot_parts, axis=1)
    returned = lax.all_to_all(back, ("macro", "work"), 0, 0, tiled=True)
    row_ids = jnp.arange(points, dtype=jnp.float32) + 1.0
    mine = returned[None, :, 36] == row_ids[:, None]
    chosen = jnp.sum(jnp.where(mine[:, :, None], returned[None, :, :36], 0.0), axis=1)
    tangent = jnp.where(active[:, None], chosen, tangent_old)
    solved = jnp.stack(
        [jnp.sum(returned[:, 37 + 36 * s : 37 + 36 * (s + 1)], axis=0) for s in range(slots)]
    )
    return (tangent, solved)


def solution(mesh):
    return jax.shard_map(
        body,
        mesh=mesh,
        in_specs=(
            P(("macro", "work"), None),
            P(("macro", "work"), None, None),
            P(("macro", "work")),
            P(("macro", "work")),
            P(),
            P(),
            P(("macro", "work"), None),
        ),
        out_specs=(P(("macro", "work"), None), P(("macro", "work"), None)),
        check_vma=False,
    )
```

```python
import numpy as np
import jax
import jax.numpy as jnp
from jax import lax
from jax.sharding import PartitionSpec as P

RES = 16
ITERS = 2
ACT_DEV = 4

exact = lax.Precision.HIGHEST
fast = lax.Precision.HIGH


def moduli_field(phase, moduli):
    first = jnp.where(phase == 1, moduli[1, 0], moduli[0, 0])
    shear = jnp.where(phase == 1, moduli[1, 1], moduli[0, 1])
    return (first, shear)


def elastic(field, first, shear):
    trace = field[0] + field[1] + field[2]
    parts = [2.0 * shear * field[c] + first * trace for c in range(3)]
    parts = parts + [2.0 * shear * field[c] for c in range(3, 6)]
    return jnp.stack(parts)


def contract(left, right):
    diagonal = left[0] * right[0] + left[1] * right[1] + left[2] * right[2]
    return diagonal + 2.0 * (left[3] * right[3] + left[4] * right[4] + left[5] * right[5])


def green(part, first0, shear0, wave_a, wave_b, wave_c):
    norm = wave_a * wave_a + wave_b * wave_b + wave_c * wave_c
    safe = jnp.where(norm > 0, norm, 1.0)
    living = jnp.where(norm > 0, 1.0, 0.0)
    force_a = part[0] * wave_a + part[5] * wave_b + part[4] * wave_c
    force_b = part[5] * wave_a + part[1] * wave_b + part[3] * wave_c
    force_c = part[4] * wave_a + part[3] * wave_b + part[2] * wave_c
    kappa = (first0 + shear0) / (shear0 * (first0 + 2.0 * shear0))
    along = (wave_a * force_a + wave_b * force_b + wave_c * force_c) * kappa / (safe * safe)
    factor = 0.5 / (shear0 * safe)
    parts = [
        factor * 2.0 * wave_a * force_a - along * wave_a * wave_a,
        factor * 2.0 * wave_b * force_b - along * wave_b * wave_b,
        factor * 2.0 * wave_c * force_c - along * wave_c * wave_c,
        factor * (wave_c * force_b + wave_b * force_c) - along * wave_b * wave_c,
        factor * (wave_c * force_a + wave_a * force_c) - along * wave_a * wave_c,
        factor * (wave_b * force_a + wave_a * force_b) - along * wave_a * wave_b,
    ]
    return jnp.stack(parts) * living


def fourier_tables(edge):
    line = np.arange(edge)
    angle_one = (np.outer(line, line) % edge) * (2.0 * np.pi / edge)
    flat = np.arange(edge * edge)
    rows, cols = flat // edge, flat % edge
    angle_two = (np.outer(rows, rows) + np.outer(cols, cols)) % edge
    angle_two = angle_two * (2.0 * np.pi / edge)
    volume = float(edge ** 3)
    return dict(
        cos_one=np.cos(angle_one).astype(np.float32),
        sin_one=np.sin(angle_one).astype(np.float32),
        cos_two=np.cos(angle_two).astype(np.float32),
        nsin_two=(-np.sin(angle_two)).astype(np.float32),
        icos_two=(np.cos(angle_two) / volume).astype(np.float32),
        insin_two=(-np.sin(angle_two) / volume).astype(np.float32),
        plus_two=(np.cos(angle_two) - np.sin(angle_two)).astype(np.float32),
        both_one=np.concatenate([np.cos(angle_one), -np.sin(angle_one)]).astype(np.float32),
        icos_one=(np.cos(angle_one) / volume).astype(np.float32),
        isin_one=(np.sin(angle_one) / volume).astype(np.float32),
        minus_two=(-np.sin(angle_two) - np.cos(angle_two)).astype(np.float32),
    )


def forward(field, tables):
    both_one, cos_two, plus_two, minus_two, icos_one, isin_one = tables
    edge = icos_one.shape[0]
    stacked = jnp.einsum("ka,...al->...kl", both_one, field, precision=fast)
    real_one = stacked[..., :edge, :]
    imag_one = stacked[..., edge:, :]
    both = jnp.matmul(real_one + imag_one, cos_two, precision=fast)
    real_two = both - jnp.matmul(imag_one, plus_two, precision=fast)
    imag_two = both + jnp.matmul(real_one, minus_two, precision=fast)
    return (real_two, imag_two)


def inverse(real_two, imag_two, tables):
    both_one, cos_two, plus_two, minus_two, icos_one, isin_one = tables
    both = jnp.matmul(real_two + imag_two, cos_two, precision=fast)
    real_one = both + jnp.matmul(imag_two, minus_two, precision=fast)
    imag_one = both - jnp.matmul(real_two, plus_two, precision=fast)
    total = jnp.einsum("ka,...kl->...al", icos_one, real_one, precision=fast)
    return total - jnp.einsum("ka,...kl->...al", isin_one, imag_one, precision=fast)


DIAGONAL = np.array([1.0, 1.0, 1.0, 0.0, 0.0, 0.0], np.float32)
DOUBLED = np.array([1.0, 1.0, 1.0, 2.0, 2.0, 2.0], np.float32)
FIRST_AXIS = [0, 1, 2, 1, 0, 0]
SECOND_AXIS = [0, 1, 2, 2, 2, 1]


def lead(values, ndim):
    return jnp.asarray(np.asarray(values, np.float32).reshape((-1,) + (1,) * (ndim - 1)))


def elastic_wide(field, first, shear):
    trace = field[0] + field[1] + field[2]
    return 2.0 * shear * field + first * trace * lead(DIAGONAL, field.ndim)


def contract_wide(left, right):
    return jnp.sum(lead(DOUBLED, left.ndim) * left * right, axis=0)


def tangent_wide(field, first, shear, keep, state, gain):
    weight = gain * contract_wide(field, state)
    return keep * elastic_wide(field, first, shear) - weight * state


def green_wide(part, first0, shear0, wave_a, wave_b, wave_c):
    norm = wave_a * wave_a + wave_b * wave_b + wave_c * wave_c
    safe = jnp.where(norm > 0, norm, 1.0)
    living = jnp.where(norm > 0, 1.0, 0.0)
    force_a = part[0] * wave_a + part[5] * wave_b + part[4] * wave_c
    force_b = part[5] * wave_a + part[1] * wave_b + part[3] * wave_c
    force_c = part[4] * wave_a + part[3] * wave_b + part[2] * wave_c
    kappa = (first0 + shear0) / (shear0 * (first0 + 2.0 * shear0))
    along = (wave_a * force_a + wave_b * force_b + wave_c * force_c) * kappa / (safe * safe)
    factor = 0.5 / (shear0 * safe)
    waves = (wave_a, wave_b, wave_c)
    forces = (force_a, force_b, force_c)
    ndim = part.ndim

    def pick(table, axes):
        total = None
        for d in range(3):
            mask = lead([1.0 if axes[c] == d else 0.0 for c in range(6)], ndim)
            term = mask * table[d]
            total = term if total is None else total + term
        return total

    wave_one, wave_two = pick(waves, FIRST_AXIS), pick(waves, SECOND_AXIS)
    force_one, force_two = pick(forces, FIRST_AXIS), pick(forces, SECOND_AXIS)
    out = factor * (wave_one * force_two + wave_two * force_one) - along * wave_one * wave_two
    return out * living


def signed_waves(index, edge):
    return jnp.where(index < edge // 2, index, index - edge).astype(jnp.float32)


def unit_columns():
    index = jnp.arange(6)
    values = jnp.where(
        index[:, None] == index[None, :], jnp.where(index[:, None] < 3, 1.0, 0.5), 0.0
    )
    return values.astype(jnp.float32)


def solve_slots(held_damage, held_strain, held_count, phase, moduli):
    edge = RES
    plane = edge * edge
    slots = held_damage.shape[0]
    first, shear = moduli_field(phase.reshape(edge, plane), moduli)
    first0 = jnp.mean(moduli[:, 0])
    shear0 = jnp.mean(moduli[:, 1])
    keep = (1.0 - held_damage).reshape(slots, 1, edge, plane)
    state_strain = jnp.transpose(held_strain.reshape(slots, 6, edge, plane), (1, 0, 2, 3))[
        :, :, None
    ]
    state = elastic_wide(state_strain, first, shear)
    gain = keep * shear / (1.0 + contract_wide(state, state))
    flat = jnp.arange(plane, dtype=jnp.int32)
    wave_a = signed_waves(jnp.arange(edge, dtype=jnp.int32), edge)[:, None]
    wave_b = signed_waves(flat // edge, edge)[None, :]
    wave_c = signed_waves(flat % edge, edge)[None, :]
    table = fourier_tables(edge)
    tables = tuple(jnp.asarray(table[k]) for k in ("both_one", "cos_two", "plus_two", "minus_two", "icos_one", "isin_one"))
    macro_field = unit_columns()[:, None, :, None, None]
    field = jnp.broadcast_to(macro_field, (6, slots, 6, edge, plane))
    count = held_count[:, None, None, None]
    for step in range(ITERS):
        polar = tangent_wide(field, first, shear, keep, state, gain) - elastic_wide(field, first0, shear0)
        if step == 0:
            polar = lax.optimization_barrier(polar)
        real_part, imag_part = forward(polar, tables)
        real_part = green_wide(real_part, first0, shear0, wave_a, wave_b, wave_c)
        imag_part = green_wide(imag_part, first0, shear0, wave_a, wave_b, wave_c)
        real_part, imag_part = lax.optimization_barrier((real_part, imag_part))
        back = inverse(real_part, imag_part, tables)
        field = jnp.where(step < count, macro_field - back, field)
    stress = tangent_wide(field, first, shear, keep, state, gain)
    means = jnp.sum(stress, axis=(3, 4)) / (edge * plane)
    return jnp.transpose(means, (1, 0, 2)).reshape(slots, 36)


def body(damage, strain, route, iters, phase, moduli, tangent_old):
    slots = ACT_DEV
    macro_count = lax.axis_size("macro")
    work_count = lax.axis_size("work")
    devices = macro_count * work_count
    my_macro = lax.axis_index("macro")
    my_work = lax.axis_index("work")
    points, voxels = damage.shape
    width = 7 * voxels
    active = route >= 0
    dest_macro = jnp.where(active, route // slots // work_count, -1)
    macro_ids = jnp.arange(macro_count, dtype=jnp.int32)
    to_macro = dest_macro[None, :] == macro_ids[:, None]
    point_ids = jnp.arange(points, dtype=jnp.int32)
    pick = jnp.max(jnp.where(to_macro, point_ids[None, :], -1), axis=1)
    sending = pick >= 0
    pick = jnp.maximum(pick, 0)
    meta = jnp.stack(
        [route.astype(jnp.float32) + 1.0, iters.astype(jnp.float32), point_ids.astype(jnp.float32) + 1.0]
        + [jnp.zeros((points,), jnp.float32)] * 125,
        axis=1,
    )
    outgoing = jnp.concatenate(
        [damage[pick], strain[pick].reshape(macro_count, 6 * voxels), meta[pick]], axis=1
    )
    outgoing = jnp.where(sending[:, None], outgoing, 0.0)
    arrived = lax.all_to_all(outgoing, "macro", 0, 0, tiled=True)
    valid = arrived[:, width] > 0.5
    rank = jnp.cumsum(valid.astype(jnp.int32)) - 1
    vol_ids = jnp.arange(slots, dtype=jnp.int32)
    select = (valid[None, :] & (rank[None, :] == vol_ids[:, None])).astype(jnp.float32)
    held = jnp.dot(select, arrived, precision=exact)
    held_valid = jnp.sum(select, axis=1) > 0.5
    held_route = (held[:, width] - 1.0).astype(jnp.int32)
    held_count = held[:, width + 1]
    held_row = held[:, width + 2]
    held_from = jnp.dot(select, macro_ids.astype(jnp.float32), precision=exact).astype(jnp.int32)
    tangents = solve_slots(
        held[:, :voxels], held[:, voxels:width].reshape(slots, 6, voxels), held_count, phase, moduli
    )
    dest_ids = jnp.arange(devices, dtype=jnp.int32)
    owner_dev = held_from * work_count + my_work
    to_owner = (held_valid[None, :] & (owner_dev[None, :] == dest_ids[:, None])).astype(jnp.float32)
    owner_part = jnp.dot(
        to_owner, jnp.concatenate([tangents, held_row[:, None]], axis=1), precision=exact
    )
    slot_parts = []
    for s in range(slots):
        hit = held_valid & (held_route == dest_ids[:, None] * slots + s)
        slot_parts.append(jnp.dot(hit.astype(jnp.float32), tangents, precision=exact))
    back = jnp.concatenate([owner_part] + slot_parts, axis=1)
    returned = lax.all_to_all(back, ("macro", "work"), 0, 0, tiled=True)
    row_ids = jnp.arange(points, dtype=jnp.float32) + 1.0
    mine = (returned[None, :, 36] == row_ids[:, None]).astype(jnp.float32)
    chosen = jnp.dot(mine, returned[:, :36], precision=exact)
    tangent = jnp.where(active[:, None], chosen, tangent_old)
    solved = jnp.stack(
        [jnp.sum(returned[:, 37 + 36 * s : 37 + 36 * (s + 1)], axis=0) for s in range(slots)]
    )
    return (tangent, solved)


def solution(mesh):
    return jax.shard_map(
        body,
        mesh=mesh,
        in_specs=(
            P(("macro", "work"), None),
            P(("macro", "work"), None, None),
            P(("macro", "work")),
            P(("macro", "work")),
            P(),
            P(),
            P(("macro", "work"), None),
        ),
        out_specs=(P(("macro", "work"), None), P(("macro", "work"), None)),
        check_vma=False,
    )
```

```python
import numpy as np
import jax
import jax.numpy as jnp
from jax import lax
from jax.sharding import PartitionSpec as P

RES = 16
ITERS = 2
ACT_DEV = 4

exact = lax.Precision.HIGHEST
fast = lax.Precision.HIGH


def moduli_field(phase, moduli):
    first = jnp.where(phase == 1, moduli[1, 0], moduli[0, 0])
    shear = jnp.where(phase == 1, moduli[1, 1], moduli[0, 1])
    return (first, shear)


def elastic(field, first, shear):
    trace = field[0] + field[1] + field[2]
    parts = [2.0 * shear * field[c] + first * trace for c in range(3)]
    parts = parts + [2.0 * shear * field[c] for c in range(3, 6)]
    return jnp.stack(parts)


def contract(left, right):
    diagonal = left[0] * right[0] + left[1] * right[1] + left[2] * right[2]
    return diagonal + 2.0 * (left[3] * right[3] + left[4] * right[4] + left[5] * right[5])


def green(part, first0, shear0, wave_a, wave_b, wave_c):
    norm = wave_a * wave_a + wave_b * wave_b + wave_c * wave_c
    safe = jnp.where(norm > 0, norm, 1.0)
    living = jnp.where(norm > 0, 1.0, 0.0)
    force_a = part[0] * wave_a + part[5] * wave_b + part[4] * wave_c
    force_b = part[5] * wave_a + part[1] * wave_b + part[3] * wave_c
    force_c = part[4] * wave_a + part[3] * wave_b + part[2] * wave_c
    kappa = (first0 + shear0) / (shear0 * (first0 + 2.0 * shear0))
    along = (wave_a * force_a + wave_b * force_b + wave_c * force_c) * kappa / (safe * safe)
    factor = 0.5 / (shear0 * safe)
    parts = [
        factor * 2.0 * wave_a * force_a - along * wave_a * wave_a,
        factor * 2.0 * wave_b * force_b - along * wave_b * wave_b,
        factor * 2.0 * wave_c * force_c - along * wave_c * wave_c,
        factor * (wave_c * force_b + wave_b * force_c) - along * wave_b * wave_c,
        factor * (wave_c * force_a + wave_a * force_c) - along * wave_a * wave_c,
        factor * (wave_b * force_a + wave_a * force_b) - along * wave_a * wave_b,
    ]
    return jnp.stack(parts) * living


def fourier_tables(edge):
    line = np.arange(edge)
    angle_one = (np.outer(line, line) % edge) * (2.0 * np.pi / edge)
    flat = np.arange(edge * edge)
    rows, cols = flat // edge, flat % edge
    angle_two = (np.outer(rows, rows) + np.outer(cols, cols)) % edge
    angle_two = angle_two * (2.0 * np.pi / edge)
    volume = float(edge ** 3)
    return dict(
        cos_one=np.cos(angle_one).astype(np.float32),
        sin_one=np.sin(angle_one).astype(np.float32),
        cos_two=np.cos(angle_two).astype(np.float32),
        nsin_two=(-np.sin(angle_two)).astype(np.float32),
        icos_two=(np.cos(angle_two) / volume).astype(np.float32),
        insin_two=(-np.sin(angle_two) / volume).astype(np.float32),
        plus_two=(np.cos(angle_two) - np.sin(angle_two)).astype(np.float32),
        both_one=np.concatenate([np.cos(angle_one), -np.sin(angle_one)]).astype(np.float32),
        icos_one=(np.cos(angle_one) / volume).astype(np.float32),
        isin_one=(np.sin(angle_one) / volume).astype(np.float32),
        minus_two=(-np.sin(angle_two) - np.cos(angle_two)).astype(np.float32),
    )


def forward(field, tables):
    both_one, cos_two, plus_two, minus_two, icos_one, isin_one = tables
    edge = icos_one.shape[0]
    stacked = jnp.einsum("ka,...al->...kl", both_one, field, precision=fast)
    real_one = stacked[..., :edge, :]
    imag_one = stacked[..., edge:, :]
    both = jnp.matmul(real_one + imag_one, cos_two, precision=fast)
    real_two = both - jnp.matmul(imag_one, plus_two, precision=fast)
    imag_two = both + jnp.matmul(real_one, minus_two, precision=fast)
    return (real_two, imag_two)


def inverse(real_two, imag_two, tables):
    both_one, cos_two, plus_two, minus_two, icos_one, isin_one = tables
    both = jnp.matmul(real_two + imag_two, cos_two, precision=fast)
    real_one = both + jnp.matmul(imag_two, minus_two, precision=fast)
    imag_one = both - jnp.matmul(real_two, plus_two, precision=fast)
    total = jnp.einsum("ka,...kl->...al", icos_one, real_one, precision=fast)
    return total - jnp.einsum("ka,...kl->...al", isin_one, imag_one, precision=fast)


DIAGONAL = np.array([1.0, 1.0, 1.0, 0.0, 0.0, 0.0], np.float32)
DOUBLED = np.array([1.0, 1.0, 1.0, 2.0, 2.0, 2.0], np.float32)
FIRST_AXIS = [0, 1, 2, 1, 0, 0]
SECOND_AXIS = [0, 1, 2, 2, 2, 1]


def lead(values, ndim):
    return jnp.asarray(np.asarray(values, np.float32).reshape((-1,) + (1,) * (ndim - 1)))


def elastic_wide(field, first, shear):
    trace = field[0] + field[1] + field[2]
    return 2.0 * shear * field + first * trace * lead(DIAGONAL, field.ndim)


def contract_wide(left, right):
    return jnp.sum(lead(DOUBLED, left.ndim) * left * right, axis=0)


def tangent_wide(field, first, shear, keep, state, gain):
    weight = gain * contract_wide(field, state)
    return keep * elastic_wide(field, first, shear) - weight * state


def green_wide(part, first0, shear0, wave_a, wave_b, wave_c):
    norm = wave_a * wave_a + wave_b * wave_b + wave_c * wave_c
    safe = jnp.where(norm > 0, norm, 1.0)
    living = jnp.where(norm > 0, 1.0, 0.0)
    kappa = (first0 + shear0) / (shear0 * (first0 + 2.0 * shear0))
    along_scale, factor = lax.optimization_barrier(
        (kappa / (safe * safe) * living, 0.5 / (shear0 * safe) * living)
    )
    force_a = part[0] * wave_a + part[5] * wave_b + part[4] * wave_c
    force_b = part[5] * wave_a + part[1] * wave_b + part[3] * wave_c
    force_c = part[4] * wave_a + part[3] * wave_b + part[2] * wave_c
    along = (wave_a * force_a + wave_b * force_b + wave_c * force_c) * along_scale
    waves = (wave_a, wave_b, wave_c)
    forces = (force_a, force_b, force_c)
    ndim = part.ndim

    def pick(table, axes):
        total = None
        for d in range(3):
            mask = lead([1.0 if axes[c] == d else 0.0 for c in range(6)], ndim)
            term = mask * table[d]
            total = term if total is None else total + term
        return total

    wave_one, wave_two = pick(waves, FIRST_AXIS), pick(waves, SECOND_AXIS)
    force_one, force_two = pick(forces, FIRST_AXIS), pick(forces, SECOND_AXIS)
    return factor * (wave_one * force_two + wave_two * force_one) - along * wave_one * wave_two


def signed_waves(index, edge):
    return jnp.where(index < edge // 2, index, index - edge).astype(jnp.float32)


def unit_columns():
    index = jnp.arange(6)
    values = jnp.where(
        index[:, None] == index[None, :], jnp.where(index[:, None] < 3, 1.0, 0.5), 0.0
    )
    return values.astype(jnp.float32)


def solve_slots(held_damage, held_strain, held_count, phase, moduli):
    edge = RES
    plane = edge * edge
    slots = held_damage.shape[0]
    first, shear = moduli_field(phase.reshape(edge, plane), moduli)
    first0 = jnp.mean(moduli[:, 0])
    shear0 = jnp.mean(moduli[:, 1])
    keep = (1.0 - held_damage).reshape(slots, 1, edge, plane)
    state_strain = jnp.transpose(held_strain.reshape(slots, 6, edge, plane), (1, 0, 2, 3))[
        :, :, None
    ]
    state = elastic_wide(state_strain, first, shear)
    gain = keep * shear / (1.0 + contract_wide(state, state))
    flat = jnp.arange(plane, dtype=jnp.int32)
    wave_a = signed_waves(jnp.arange(edge, dtype=jnp.int32), edge)[:, None]
    wave_b = signed_waves(flat // edge, edge)[None, :]
    wave_c = signed_waves(flat % edge, edge)[None, :]
    table = fourier_tables(edge)
    tables = tuple(jnp.asarray(table[k]) for k in ("both_one", "cos_two", "plus_two", "minus_two", "icos_one", "isin_one"))
    macro_field = unit_columns()[:, None, :, None, None]
    field = jnp.broadcast_to(macro_field, (6, slots, 6, edge, plane))
    count = held_count[:, None, None, None]
    for step in range(ITERS):
        polar = tangent_wide(field, first, shear, keep, state, gain) - elastic_wide(field, first0, shear0)
        polar = lax.optimization_barrier(polar)
        real_part, imag_part = forward(polar, tables)
        real_part = green_wide(real_part, first0, shear0, wave_a, wave_b, wave_c)
        imag_part = green_wide(imag_part, first0, shear0, wave_a, wave_b, wave_c)
        real_part, imag_part = lax.optimization_barrier((real_part, imag_part))
        back = inverse(real_part, imag_part, tables)
        field = jnp.where(step < count, macro_field - back, field)
    stress = tangent_wide(field, first, shear, keep, state, gain)
    means = jnp.sum(stress, axis=(3, 4)) / (edge * plane)
    return jnp.transpose(means, (1, 0, 2)).reshape(slots, 36)


def body(damage, strain, route, iters, phase, moduli, tangent_old):
    slots = ACT_DEV
    macro_count = lax.axis_size("macro")
    work_count = lax.axis_size("work")
    devices = macro_count * work_count
    my_macro = lax.axis_index("macro")
    my_work = lax.axis_index("work")
    points, voxels = damage.shape
    width = 7 * voxels
    active = route >= 0
    dest_macro = jnp.where(active, route // slots // work_count, -1)
    macro_ids = jnp.arange(macro_count, dtype=jnp.int32)
    to_macro = dest_macro[None, :] == macro_ids[:, None]
    point_ids = jnp.arange(points, dtype=jnp.int32)
    pick = jnp.max(jnp.where(to_macro, point_ids[None, :], -1), axis=1)
    sending = pick >= 0
    pick = jnp.maximum(pick, 0)
    meta = jnp.stack(
        [route.astype(jnp.float32) + 1.0, iters.astype(jnp.float32), point_ids.astype(jnp.float32) + 1.0]
        + [jnp.zeros((points,), jnp.float32)] * 125,
        axis=1,
    )
    outgoing = jnp.concatenate(
        [damage[pick], strain[pick].reshape(macro_count, 6 * voxels), meta[pick]], axis=1
    )
    outgoing = jnp.where(sending[:, None], outgoing, 0.0)
    arrived = lax.all_to_all(outgoing, "macro", 0, 0, tiled=True)
    valid = arrived[:, width] > 0.5
    rank = jnp.cumsum(valid.astype(jnp.int32)) - 1
    vol_ids = jnp.arange(slots, dtype=jnp.int32)
    select = (valid[None, :] & (rank[None, :] == vol_ids[:, None])).astype(jnp.float32)
    held = jnp.dot(select, arrived, precision=exact)
    held_valid = jnp.sum(select, axis=1) > 0.5
    held_route = (held[:, width] - 1.0).astype(jnp.int32)
    held_count = held[:, width + 1]
    held_row = held[:, width + 2]
    held_from = jnp.dot(select, macro_ids.astype(jnp.float32), precision=exact).astype(jnp.int32)
    tangents = solve_slots(
        held[:, :voxels], held[:, voxels:width].reshape(slots, 6, voxels), held_count, phase, moduli
    )
    dest_ids = jnp.arange(devices, dtype=jnp.int32)
    owner_dev = held_from * work_count + my_work
    to_owner = (held_valid[None, :] & (owner_dev[None, :] == dest_ids[:, None])).astype(jnp.float32)
    owner_part = jnp.dot(
        to_owner, jnp.concatenate([tangents, held_row[:, None]], axis=1), precision=exact
    )
    slot_parts = []
    for s in range(slots):
        hit = held_valid & (held_route == dest_ids[:, None] * slots + s)
        slot_parts.append(jnp.dot(hit.astype(jnp.float32), tangents, precision=exact))
    back = jnp.concatenate([owner_part] + slot_parts, axis=1)
    returned = lax.all_to_all(back, ("macro", "work"), 0, 0, tiled=True)
    row_ids = jnp.arange(points, dtype=jnp.float32) + 1.0
    mine = (returned[None, :, 36] == row_ids[:, None]).astype(jnp.float32)
    chosen = jnp.dot(mine, returned[:, :36], precision=exact)
    tangent = jnp.where(active[:, None], chosen, tangent_old)
    solved = jnp.stack(
        [jnp.sum(returned[:, 37 + 36 * s : 37 + 36 * (s + 1)], axis=0) for s in range(slots)]
    )
    return (tangent, solved)


def solution(mesh):
    return jax.shard_map(
        body,
        mesh=mesh,
        in_specs=(
            P(("macro", "work"), None),
            P(("macro", "work"), None, None),
            P(("macro", "work")),
            P(("macro", "work")),
            P(),
            P(),
            P(("macro", "work"), None),
        ),
        out_specs=(P(("macro", "work"), None), P(("macro", "work"), None)),
        check_vma=False,
    )
```

```python
import numpy as np
import jax
import jax.numpy as jnp
from jax import lax
from jax.sharding import PartitionSpec as P

RES = 16
ITERS = 2
ACT_DEV = 4

exact = lax.Precision.HIGHEST
fast = lax.Precision.HIGH


def moduli_field(phase, moduli):
    first = jnp.where(phase == 1, moduli[1, 0], moduli[0, 0])
    shear = jnp.where(phase == 1, moduli[1, 1], moduli[0, 1])
    return (first, shear)


def elastic(field, first, shear):
    trace = field[0] + field[1] + field[2]
    parts = [2.0 * shear * field[c] + first * trace for c in range(3)]
    parts = parts + [2.0 * shear * field[c] for c in range(3, 6)]
    return jnp.stack(parts)


def contract(left, right):
    diagonal = left[0] * right[0] + left[1] * right[1] + left[2] * right[2]
    return diagonal + 2.0 * (left[3] * right[3] + left[4] * right[4] + left[5] * right[5])


def green(part, first0, shear0, wave_a, wave_b, wave_c):
    norm = wave_a * wave_a + wave_b * wave_b + wave_c * wave_c
    safe = jnp.where(norm > 0, norm, 1.0)
    living = jnp.where(norm > 0, 1.0, 0.0)
    force_a = part[0] * wave_a + part[5] * wave_b + part[4] * wave_c
    force_b = part[5] * wave_a + part[1] * wave_b + part[3] * wave_c
    force_c = part[4] * wave_a + part[3] * wave_b + part[2] * wave_c
    kappa = (first0 + shear0) / (shear0 * (first0 + 2.0 * shear0))
    along = (wave_a * force_a + wave_b * force_b + wave_c * force_c) * kappa / (safe * safe)
    factor = 0.5 / (shear0 * safe)
    parts = [
        factor * 2.0 * wave_a * force_a - along * wave_a * wave_a,
        factor * 2.0 * wave_b * force_b - along * wave_b * wave_b,
        factor * 2.0 * wave_c * force_c - along * wave_c * wave_c,
        factor * (wave_c * force_b + wave_b * force_c) - along * wave_b * wave_c,
        factor * (wave_c * force_a + wave_a * force_c) - along * wave_a * wave_c,
        factor * (wave_b * force_a + wave_a * force_b) - along * wave_a * wave_b,
    ]
    return jnp.stack(parts) * living


def fourier_tables(edge):
    line = np.arange(edge)
    angle_one = (np.outer(line, line) % edge) * (2.0 * np.pi / edge)
    flat = np.arange(edge * edge)
    rows, cols = flat // edge, flat % edge
    angle_two = (np.outer(rows, rows) + np.outer(cols, cols)) % edge
    angle_two = angle_two * (2.0 * np.pi / edge)
    volume = float(edge ** 3)
    return dict(
        cos_one=np.cos(angle_one).astype(np.float32),
        sin_one=np.sin(angle_one).astype(np.float32),
        cos_two=np.cos(angle_two).astype(np.float32),
        nsin_two=(-np.sin(angle_two)).astype(np.float32),
        icos_two=(np.cos(angle_two) / volume).astype(np.float32),
        insin_two=(-np.sin(angle_two) / volume).astype(np.float32),
        plus_two=(np.cos(angle_two) - np.sin(angle_two)).astype(np.float32),
        both_one=np.concatenate([np.cos(angle_one), -np.sin(angle_one)]).astype(np.float32),
        icos_one=(np.cos(angle_one) / volume).astype(np.float32),
        isin_one=(np.sin(angle_one) / volume).astype(np.float32),
        minus_two=(-np.sin(angle_two) - np.cos(angle_two)).astype(np.float32),
    )


def forward(field, tables):
    both_one, cos_two, plus_two, minus_two, icos_one, isin_one = tables
    edge = icos_one.shape[0]
    stacked = jnp.einsum("ka,...al->...kl", both_one, field, precision=fast)
    real_one = stacked[..., :edge, :]
    imag_one = stacked[..., edge:, :]
    both = jnp.matmul(real_one + imag_one, cos_two, precision=fast)
    real_two = both - jnp.matmul(imag_one, plus_two, precision=fast)
    imag_two = both + jnp.matmul(real_one, minus_two, precision=fast)
    return (real_two, imag_two)


def inverse(real_two, imag_two, tables):
    both_one, cos_two, plus_two, minus_two, icos_one, isin_one = tables
    both = jnp.matmul(real_two + imag_two, cos_two, precision=fast)
    real_one = both + jnp.matmul(imag_two, minus_two, precision=fast)
    imag_one = both - jnp.matmul(real_two, plus_two, precision=fast)
    total = jnp.einsum("ka,...kl->...al", icos_one, real_one, precision=fast)
    return total - jnp.einsum("ka,...kl->...al", isin_one, imag_one, precision=fast)


DIAGONAL = np.array([1.0, 1.0, 1.0, 0.0, 0.0, 0.0], np.float32)
DOUBLED = np.array([1.0, 1.0, 1.0, 2.0, 2.0, 2.0], np.float32)
FIRST_AXIS = [0, 1, 2, 1, 0, 0]
SECOND_AXIS = [0, 1, 2, 2, 2, 1]


def lead(values, ndim):
    return jnp.asarray(np.asarray(values, np.float32).reshape((-1,) + (1,) * (ndim - 1)))


def elastic_wide(field, first, shear):
    trace = field[0] + field[1] + field[2]
    return 2.0 * shear * field + first * trace * lead(DIAGONAL, field.ndim)


def contract_wide(left, right):
    return jnp.sum(lead(DOUBLED, left.ndim) * left * right, axis=0)


def tangent_wide(field, first, shear, keep, state, gain):
    weight = gain * contract_wide(field, state)
    return keep * elastic_wide(field, first, shear) - weight * state


def green_wide(part, first0, shear0, wave_a, wave_b, wave_c):
    norm = wave_a * wave_a + wave_b * wave_b + wave_c * wave_c
    safe = jnp.where(norm > 0, norm, 1.0)
    living = jnp.where(norm > 0, 1.0, 0.0)
    kappa = (first0 + shear0) / (shear0 * (first0 + 2.0 * shear0))
    along_scale, factor = lax.optimization_barrier(
        (kappa / (safe * safe) * living, 0.5 / (shear0 * safe) * living)
    )
    force_a = part[0] * wave_a + part[5] * wave_b + part[4] * wave_c
    force_b = part[5] * wave_a + part[1] * wave_b + part[3] * wave_c
    force_c = part[4] * wave_a + part[3] * wave_b + part[2] * wave_c
    along = (wave_a * force_a + wave_b * force_b + wave_c * force_c) * along_scale
    waves = (wave_a, wave_b, wave_c)
    forces = (force_a, force_b, force_c)
    ndim = part.ndim

    def pick(table, axes):
        total = None
        for d in range(3):
            mask = lead([1.0 if axes[c] == d else 0.0 for c in range(6)], ndim)
            term = mask * table[d]
            total = term if total is None else total + term
        return total

    wave_one, wave_two = pick(waves, FIRST_AXIS), pick(waves, SECOND_AXIS)
    force_one, force_two = pick(forces, FIRST_AXIS), pick(forces, SECOND_AXIS)
    return factor * (wave_one * force_two + wave_two * force_one) - along * wave_one * wave_two


def signed_waves(index, edge):
    return jnp.where(index < edge // 2, index, index - edge).astype(jnp.float32)


def unit_columns():
    index = jnp.arange(6)
    values = jnp.where(
        index[:, None] == index[None, :], jnp.where(index[:, None] < 3, 1.0, 0.5), 0.0
    )
    return values.astype(jnp.float32)


def solve_slots(held_damage, held_strain, held_count, phase, moduli):
    edge = RES
    plane = edge * edge
    slots = held_damage.shape[0]
    first, shear = moduli_field(phase.reshape(edge, plane), moduli)
    first0 = jnp.mean(moduli[:, 0])
    shear0 = jnp.mean(moduli[:, 1])
    keep = (1.0 - held_damage).reshape(slots, 1, edge, plane)
    state_strain = jnp.transpose(held_strain.reshape(slots, 6, edge, plane), (1, 0, 2, 3))[
        :, :, None
    ]
    state = elastic_wide(state_strain, first, shear)
    gain = keep * shear / (1.0 + contract_wide(state, state))
    flat = jnp.arange(plane, dtype=jnp.int32)
    wave_a = signed_waves(jnp.arange(edge, dtype=jnp.int32), edge)[:, None]
    wave_b = signed_waves(flat // edge, edge)[None, :]
    wave_c = signed_waves(flat % edge, edge)[None, :]
    table = fourier_tables(edge)
    tables = tuple(jnp.asarray(table[k]) for k in ("both_one", "cos_two", "plus_two", "minus_two", "icos_one", "isin_one"))
    macro_field = unit_columns()[:, None, :, None, None]
    field = jnp.broadcast_to(macro_field, (6, slots, 6, edge, plane))
    count = held_count[:, None, None, None]
    for step in range(ITERS):
        polar = tangent_wide(field, first, shear, keep, state, gain) - elastic_wide(field, first0, shear0)
        if step == 0:
            polar = lax.optimization_barrier(polar)
        real_part, imag_part = forward(polar, tables)
        real_part = green_wide(real_part, first0, shear0, wave_a, wave_b, wave_c)
        imag_part = green_wide(imag_part, first0, shear0, wave_a, wave_b, wave_c)
        real_part, imag_part = lax.optimization_barrier((real_part, imag_part))
        back = inverse(real_part, imag_part, tables)
        field = jnp.where(step < count, macro_field - back, field)
    stress = tangent_wide(field, first, shear, keep, state, gain)
    means = jnp.sum(stress, axis=(3, 4)) / (edge * plane)
    return jnp.transpose(means, (1, 0, 2)).reshape(slots, 36)


def body(damage, strain, route, iters, phase, moduli, tangent_old):
    slots = ACT_DEV
    macro_count = lax.axis_size("macro")
    work_count = lax.axis_size("work")
    devices = macro_count * work_count
    my_macro = lax.axis_index("macro")
    my_work = lax.axis_index("work")
    points, voxels = damage.shape
    width = 7 * voxels
    active = route >= 0
    dest_macro = jnp.where(active, route // slots // work_count, -1)
    macro_ids = jnp.arange(macro_count, dtype=jnp.int32)
    to_macro = dest_macro[None, :] == macro_ids[:, None]
    point_ids = jnp.arange(points, dtype=jnp.int32)
    pick = jnp.max(jnp.where(to_macro, point_ids[None, :], -1), axis=1)
    sending = pick >= 0
    pick = jnp.maximum(pick, 0)
    meta = jnp.stack(
        [route.astype(jnp.float32) + 1.0, iters.astype(jnp.float32), point_ids.astype(jnp.float32) + 1.0]
        + [jnp.zeros((points,), jnp.float32)] * 125,
        axis=1,
    )
    outgoing = jnp.concatenate(
        [damage[pick], strain[pick].reshape(macro_count, 6 * voxels), meta[pick]], axis=1
    )
    outgoing = jnp.where(sending[:, None], outgoing, 0.0)
    arrived = lax.all_to_all(outgoing, "macro", 0, 0, tiled=True)
    valid = arrived[:, width] > 0.5
    rank = jnp.cumsum(valid.astype(jnp.int32)) - 1
    vol_ids = jnp.arange(slots, dtype=jnp.int32)
    select = (valid[None, :] & (rank[None, :] == vol_ids[:, None])).astype(jnp.float32)
    held = jnp.dot(select, arrived, precision=exact)
    held_valid = jnp.sum(select, axis=1) > 0.5
    held_route = (held[:, width] - 1.0).astype(jnp.int32)
    held_count = held[:, width + 1]
    held_row = held[:, width + 2]
    held_from = jnp.dot(select, macro_ids.astype(jnp.float32), precision=exact).astype(jnp.int32)
    tangents = solve_slots(
        held[:, :voxels], held[:, voxels:width].reshape(slots, 6, voxels), held_count, phase, moduli
    )
    dest_ids = jnp.arange(devices, dtype=jnp.int32)
    owner_dev = held_from * work_count + my_work
    to_owner = (held_valid[None, :] & (owner_dev[None, :] == dest_ids[:, None])).astype(jnp.float32)
    owner_part = jnp.dot(
        to_owner, jnp.concatenate([tangents, held_row[:, None]], axis=1), precision=exact
    )
    slot_parts = []
    for s in range(slots):
        hit = held_valid & (held_route == dest_ids[:, None] * slots + s)
        slot_parts.append(jnp.dot(hit.astype(jnp.float32), tangents, precision=exact))
    back = jnp.concatenate([owner_part] + slot_parts, axis=1)
    returned = lax.all_to_all(back, ("macro", "work"), 0, 0, tiled=True)
    row_ids = jnp.arange(points, dtype=jnp.float32) + 1.0
    mine = (returned[None, :, 36] == row_ids[:, None]).astype(jnp.float32)
    chosen = jnp.dot(mine, returned[:, :36], precision=exact)
    tangent = jnp.where(active[:, None], chosen, tangent_old)
    solved = jnp.stack(
        [jnp.sum(returned[:, 37 + 36 * s : 37 + 36 * (s + 1)], axis=0) for s in range(slots)]
    )
    return (tangent, solved)


def solution(mesh):
    return jax.shard_map(
        body,
        mesh=mesh,
        in_specs=(
            P(("macro", "work"), None),
            P(("macro", "work"), None, None),
            P(("macro", "work")),
            P(("macro", "work")),
            P(),
            P(),
            P(("macro", "work"), None),
        ),
        out_specs=(P(("macro", "work"), None), P(("macro", "work"), None)),
        check_vma=False,
    )
```

```python
import numpy as np
import jax
import jax.numpy as jnp
from jax import lax
from jax.sharding import PartitionSpec as P

RES = 16
ITERS = 2
ACT_DEV = 4

exact = lax.Precision.HIGHEST
fast = lax.Precision.HIGH


def moduli_field(phase, moduli):
    first = jnp.where(phase == 1, moduli[1, 0], moduli[0, 0])
    shear = jnp.where(phase == 1, moduli[1, 1], moduli[0, 1])
    return (first, shear)


def elastic(field, first, shear):
    trace = field[0] + field[1] + field[2]
    parts = [2.0 * shear * field[c] + first * trace for c in range(3)]
    parts = parts + [2.0 * shear * field[c] for c in range(3, 6)]
    return jnp.stack(parts)


def contract(left, right):
    diagonal = left[0] * right[0] + left[1] * right[1] + left[2] * right[2]
    return diagonal + 2.0 * (left[3] * right[3] + left[4] * right[4] + left[5] * right[5])


def green(part, first0, shear0, wave_a, wave_b, wave_c):
    norm = wave_a * wave_a + wave_b * wave_b + wave_c * wave_c
    safe = jnp.where(norm > 0, norm, 1.0)
    living = jnp.where(norm > 0, 1.0, 0.0)
    force_a = part[0] * wave_a + part[5] * wave_b + part[4] * wave_c
    force_b = part[5] * wave_a + part[1] * wave_b + part[3] * wave_c
    force_c = part[4] * wave_a + part[3] * wave_b + part[2] * wave_c
    kappa = (first0 + shear0) / (shear0 * (first0 + 2.0 * shear0))
    along = (wave_a * force_a + wave_b * force_b + wave_c * force_c) * kappa / (safe * safe)
    factor = 0.5 / (shear0 * safe)
    parts = [
        factor * 2.0 * wave_a * force_a - along * wave_a * wave_a,
        factor * 2.0 * wave_b * force_b - along * wave_b * wave_b,
        factor * 2.0 * wave_c * force_c - along * wave_c * wave_c,
        factor * (wave_c * force_b + wave_b * force_c) - along * wave_b * wave_c,
        factor * (wave_c * force_a + wave_a * force_c) - along * wave_a * wave_c,
        factor * (wave_b * force_a + wave_a * force_b) - along * wave_a * wave_b,
    ]
    return jnp.stack(parts) * living


def fourier_tables(edge):
    line = np.arange(edge)
    angle_one = (np.outer(line, line) % edge) * (2.0 * np.pi / edge)
    flat = np.arange(edge * edge)
    rows, cols = flat // edge, flat % edge
    angle_two = (np.outer(rows, rows) + np.outer(cols, cols)) % edge
    angle_two = angle_two * (2.0 * np.pi / edge)
    volume = float(edge ** 3)
    return dict(
        cos_one=np.cos(angle_one).astype(np.float32),
        sin_one=np.sin(angle_one).astype(np.float32),
        cos_two=np.cos(angle_two).astype(np.float32),
        nsin_two=(-np.sin(angle_two)).astype(np.float32),
        icos_two=(np.cos(angle_two) / volume).astype(np.float32),
        insin_two=(-np.sin(angle_two) / volume).astype(np.float32),
        plus_two=(np.cos(angle_two) - np.sin(angle_two)).astype(np.float32),
        both_one=np.concatenate([np.cos(angle_one), -np.sin(angle_one)]).astype(np.float32),
        icos_one=(np.cos(angle_one) / volume).astype(np.float32),
        isin_one=(np.sin(angle_one) / volume).astype(np.float32),
        minus_two=(-np.sin(angle_two) - np.cos(angle_two)).astype(np.float32),
    )


def forward(field, tables):
    both_one, cos_two, plus_two, minus_two, icos_one, isin_one = tables
    edge = icos_one.shape[0]
    stacked = jnp.einsum("ka,...al->...kl", both_one, field, precision=fast)
    real_one = stacked[..., :edge, :]
    imag_one = stacked[..., edge:, :]
    both = jnp.matmul(real_one + imag_one, cos_two, precision=fast)
    real_two = both - jnp.matmul(imag_one, plus_two, precision=fast)
    imag_two = both + jnp.matmul(real_one, minus_two, precision=fast)
    return (real_two, imag_two)


def inverse(real_two, imag_two, tables):
    both_one, cos_two, plus_two, minus_two, icos_one, isin_one = tables
    both = jnp.matmul(real_two + imag_two, cos_two, precision=fast)
    real_one = both + jnp.matmul(imag_two, minus_two, precision=fast)
    imag_one = both - jnp.matmul(real_two, plus_two, precision=fast)
    total = jnp.einsum("ka,...kl->...al", icos_one, real_one, precision=fast)
    return total - jnp.einsum("ka,...kl->...al", isin_one, imag_one, precision=fast)


DIAGONAL = np.array([1.0, 1.0, 1.0, 0.0, 0.0, 0.0], np.float32)
DOUBLED = np.array([1.0, 1.0, 1.0, 2.0, 2.0, 2.0], np.float32)
FIRST_AXIS = [0, 1, 2, 1, 0, 0]
SECOND_AXIS = [0, 1, 2, 2, 2, 1]


def lead(values, ndim):
    return jnp.asarray(np.asarray(values, np.float32).reshape((-1,) + (1,) * (ndim - 1)))


def elastic_wide(field, first, shear):
    trace = field[0] + field[1] + field[2]
    return 2.0 * shear * field + first * trace * lead(DIAGONAL, field.ndim)


def contract_wide(left, right):
    return jnp.sum(lead(DOUBLED, left.ndim) * left * right, axis=0)


def tangent_wide(field, first, shear, keep, state, gain):
    weight = gain * contract_wide(field, state)
    return keep * elastic_wide(field, first, shear) - weight * state


def green_wide(part, first0, shear0, wave_a, wave_b, wave_c):
    norm = wave_a * wave_a + wave_b * wave_b + wave_c * wave_c
    safe = jnp.where(norm > 0, norm, 1.0)
    living = jnp.where(norm > 0, 1.0, 0.0)
    kappa = (first0 + shear0) / (shear0 * (first0 + 2.0 * shear0))
    along_scale, factor = lax.optimization_barrier(
        (kappa / (safe * safe) * living, 0.5 / (shear0 * safe) * living)
    )
    force_a = part[0] * wave_a + part[5] * wave_b + part[4] * wave_c
    force_b = part[5] * wave_a + part[1] * wave_b + part[3] * wave_c
    force_c = part[4] * wave_a + part[3] * wave_b + part[2] * wave_c
    along = (wave_a * force_a + wave_b * force_b + wave_c * force_c) * along_scale
    waves = (wave_a, wave_b, wave_c)
    forces = (force_a, force_b, force_c)
    ndim = part.ndim

    def pick(table, axes):
        total = None
        for d in range(3):
            mask = lead([1.0 if axes[c] == d else 0.0 for c in range(6)], ndim)
            term = mask * table[d]
            total = term if total is None else total + term
        return total

    wave_one, wave_two = pick(waves, FIRST_AXIS), pick(waves, SECOND_AXIS)
    force_one, force_two = pick(forces, FIRST_AXIS), pick(forces, SECOND_AXIS)
    return factor * (wave_one * force_two + wave_two * force_one) - along * wave_one * wave_two


def signed_waves(index, edge):
    return jnp.where(index < edge // 2, index, index - edge).astype(jnp.float32)


def unit_columns():
    index = jnp.arange(6)
    values = jnp.where(
        index[:, None] == index[None, :], jnp.where(index[:, None] < 3, 1.0, 0.5), 0.0
    )
    return values.astype(jnp.float32)


def solve_slots(held_damage, held_strain, held_count, phase, moduli):
    edge = RES
    plane = edge * edge
    slots = held_damage.shape[0]
    first, shear = moduli_field(phase.reshape(edge, plane), moduli)
    first0 = jnp.mean(moduli[:, 0])
    shear0 = jnp.mean(moduli[:, 1])
    keep = (1.0 - held_damage).reshape(slots, 1, edge, plane)
    state_strain = jnp.transpose(held_strain.reshape(slots, 6, edge, plane), (1, 0, 2, 3))[
        :, :, None
    ]
    state = elastic_wide(state_strain, first, shear)
    gain = keep * shear / (1.0 + contract_wide(state, state))
    flat = jnp.arange(plane, dtype=jnp.int32)
    wave_a = signed_waves(jnp.arange(edge, dtype=jnp.int32), edge)[:, None]
    wave_b = signed_waves(flat // edge, edge)[None, :]
    wave_c = signed_waves(flat % edge, edge)[None, :]
    table = fourier_tables(edge)
    tables = tuple(jnp.asarray(table[k]) for k in ("both_one", "cos_two", "plus_two", "minus_two", "icos_one", "isin_one"))
    macro_field = unit_columns()[:, None, :, None, None]
    field = jnp.broadcast_to(macro_field, (6, slots, 6, edge, plane))
    count = held_count[:, None, None, None]
    first_gap = keep * first - first0
    shear_gap = keep * shear - shear0
    for step in range(ITERS):
        polar = elastic_wide(field, first_gap, shear_gap) - gain * contract_wide(field, state) * state
        polar = lax.optimization_barrier(polar)
        real_part, imag_part = forward(polar, tables)
        real_part = green_wide(real_part, first0, shear0, wave_a, wave_b, wave_c)
        imag_part = green_wide(imag_part, first0, shear0, wave_a, wave_b, wave_c)
        real_part, imag_part = lax.optimization_barrier((real_part, imag_part))
        back = inverse(real_part, imag_part, tables)
        field = jnp.where(step < count, macro_field - back, field)
    stress = tangent_wide(field, first, shear, keep, state, gain)
    means = jnp.sum(stress, axis=(3, 4)) / (edge * plane)
    return jnp.transpose(means, (1, 0, 2)).reshape(slots, 36)


def body(damage, strain, route, iters, phase, moduli, tangent_old):
    slots = ACT_DEV
    macro_count = lax.axis_size("macro")
    work_count = lax.axis_size("work")
    devices = macro_count * work_count
    my_macro = lax.axis_index("macro")
    my_work = lax.axis_index("work")
    points, voxels = damage.shape
    width = 7 * voxels
    active = route >= 0
    dest_macro = jnp.where(active, route // slots // work_count, -1)
    macro_ids = jnp.arange(macro_count, dtype=jnp.int32)
    to_macro = dest_macro[None, :] == macro_ids[:, None]
    point_ids = jnp.arange(points, dtype=jnp.int32)
    pick = jnp.max(jnp.where(to_macro, point_ids[None, :], -1), axis=1)
    sending = pick >= 0
    pick = jnp.maximum(pick, 0)
    meta = jnp.stack(
        [route.astype(jnp.float32) + 1.0, iters.astype(jnp.float32), point_ids.astype(jnp.float32) + 1.0]
        + [jnp.zeros((points,), jnp.float32)] * 125,
        axis=1,
    )
    outgoing = jnp.concatenate(
        [damage[pick], strain[pick].reshape(macro_count, 6 * voxels), meta[pick]], axis=1
    )
    outgoing = jnp.where(sending[:, None], outgoing, 0.0)
    arrived = lax.all_to_all(outgoing, "macro", 0, 0, tiled=True)
    valid = arrived[:, width] > 0.5
    rank = jnp.cumsum(valid.astype(jnp.int32)) - 1
    vol_ids = jnp.arange(slots, dtype=jnp.int32)
    select = (valid[None, :] & (rank[None, :] == vol_ids[:, None])).astype(jnp.float32)
    held = jnp.dot(select, arrived, precision=exact)
    held_valid = jnp.sum(select, axis=1) > 0.5
    held_route = (held[:, width] - 1.0).astype(jnp.int32)
    held_count = held[:, width + 1]
    held_row = held[:, width + 2]
    held_from = jnp.dot(select, macro_ids.astype(jnp.float32), precision=exact).astype(jnp.int32)
    tangents = solve_slots(
        held[:, :voxels], held[:, voxels:width].reshape(slots, 6, voxels), held_count, phase, moduli
    )
    dest_ids = jnp.arange(devices, dtype=jnp.int32)
    owner_dev = held_from * work_count + my_work
    to_owner = (held_valid[None, :] & (owner_dev[None, :] == dest_ids[:, None])).astype(jnp.float32)
    owner_part = jnp.dot(
        to_owner, jnp.concatenate([tangents, held_row[:, None]], axis=1), precision=exact
    )
    slot_parts = []
    for s in range(slots):
        hit = held_valid & (held_route == dest_ids[:, None] * slots + s)
        slot_parts.append(jnp.dot(hit.astype(jnp.float32), tangents, precision=exact))
    back = jnp.concatenate([owner_part] + slot_parts, axis=1)
    returned = lax.all_to_all(back, ("macro", "work"), 0, 0, tiled=True)
    row_ids = jnp.arange(points, dtype=jnp.float32) + 1.0
    mine = (returned[None, :, 36] == row_ids[:, None]).astype(jnp.float32)
    chosen = jnp.dot(mine, returned[:, :36], precision=exact)
    tangent = jnp.where(active[:, None], chosen, tangent_old)
    solved = jnp.stack(
        [jnp.sum(returned[:, 37 + 36 * s : 37 + 36 * (s + 1)], axis=0) for s in range(slots)]
    )
    return (tangent, solved)


def solution(mesh):
    return jax.shard_map(
        body,
        mesh=mesh,
        in_specs=(
            P(("macro", "work"), None),
            P(("macro", "work"), None, None),
            P(("macro", "work")),
            P(("macro", "work")),
            P(),
            P(),
            P(("macro", "work"), None),
        ),
        out_specs=(P(("macro", "work"), None), P(("macro", "work"), None)),
        check_vma=False,
    )
```

```python
import numpy as np
import jax
import jax.numpy as jnp
from jax import lax
from jax.sharding import PartitionSpec as P

RES = 16
ITERS = 2
ACT_DEV = 4

exact = lax.Precision.HIGHEST
fast = lax.Precision.HIGH


def moduli_field(phase, moduli):
    first = jnp.where(phase == 1, moduli[1, 0], moduli[0, 0])
    shear = jnp.where(phase == 1, moduli[1, 1], moduli[0, 1])
    return (first, shear)


def elastic(field, first, shear):
    trace = field[0] + field[1] + field[2]
    parts = [2.0 * shear * field[c] + first * trace for c in range(3)]
    parts = parts + [2.0 * shear * field[c] for c in range(3, 6)]
    return jnp.stack(parts)


def contract(left, right):
    diagonal = left[0] * right[0] + left[1] * right[1] + left[2] * right[2]
    return diagonal + 2.0 * (left[3] * right[3] + left[4] * right[4] + left[5] * right[5])


def green(part, first0, shear0, wave_a, wave_b, wave_c):
    norm = wave_a * wave_a + wave_b * wave_b + wave_c * wave_c
    safe = jnp.where(norm > 0, norm, 1.0)
    living = jnp.where(norm > 0, 1.0, 0.0)
    force_a = part[0] * wave_a + part[5] * wave_b + part[4] * wave_c
    force_b = part[5] * wave_a + part[1] * wave_b + part[3] * wave_c
    force_c = part[4] * wave_a + part[3] * wave_b + part[2] * wave_c
    kappa = (first0 + shear0) / (shear0 * (first0 + 2.0 * shear0))
    along = (wave_a * force_a + wave_b * force_b + wave_c * force_c) * kappa / (safe * safe)
    factor = 0.5 / (shear0 * safe)
    parts = [
        factor * 2.0 * wave_a * force_a - along * wave_a * wave_a,
        factor * 2.0 * wave_b * force_b - along * wave_b * wave_b,
        factor * 2.0 * wave_c * force_c - along * wave_c * wave_c,
        factor * (wave_c * force_b + wave_b * force_c) - along * wave_b * wave_c,
        factor * (wave_c * force_a + wave_a * force_c) - along * wave_a * wave_c,
        factor * (wave_b * force_a + wave_a * force_b) - along * wave_a * wave_b,
    ]
    return jnp.stack(parts) * living


def fourier_tables(edge):
    line = np.arange(edge)
    angle_one = (np.outer(line, line) % edge) * (2.0 * np.pi / edge)
    flat = np.arange(edge * edge)
    rows, cols = flat // edge, flat % edge
    angle_two = (np.outer(rows, rows) + np.outer(cols, cols)) % edge
    angle_two = angle_two * (2.0 * np.pi / edge)
    volume = float(edge ** 3)
    return dict(
        cos_one=np.cos(angle_one).astype(np.float32),
        sin_one=np.sin(angle_one).astype(np.float32),
        cos_two=np.cos(angle_two).astype(np.float32),
        nsin_two=(-np.sin(angle_two)).astype(np.float32),
        icos_two=(np.cos(angle_two) / volume).astype(np.float32),
        insin_two=(-np.sin(angle_two) / volume).astype(np.float32),
        plus_two=(np.cos(angle_two) - np.sin(angle_two)).astype(np.float32),
        both_one=np.concatenate([np.cos(angle_one), -np.sin(angle_one)]).astype(np.float32),
        icos_one=(np.cos(angle_one) / volume).astype(np.float32),
        isin_one=(np.sin(angle_one) / volume).astype(np.float32),
        minus_two=(-np.sin(angle_two) - np.cos(angle_two)).astype(np.float32),
    )


def forward(field, tables):
    both_one, cos_two, plus_two, minus_two, icos_one, isin_one = tables
    edge = icos_one.shape[0]
    stacked = jnp.einsum("ka,...al->...kl", both_one, field, precision=fast)
    real_one = stacked[..., :edge, :]
    imag_one = stacked[..., edge:, :]
    both = jnp.matmul(real_one + imag_one, cos_two, precision=fast)
    real_two = both - jnp.matmul(imag_one, plus_two, precision=fast)
    imag_two = both + jnp.matmul(real_one, minus_two, precision=fast)
    return (real_two, imag_two)


def inverse(real_two, imag_two, tables):
    both_one, cos_two, plus_two, minus_two, icos_one, isin_one = tables
    both = jnp.matmul(real_two + imag_two, cos_two, precision=fast)
    real_one = both + jnp.matmul(imag_two, minus_two, precision=fast)
    imag_one = both - jnp.matmul(real_two, plus_two, precision=fast)
    total = jnp.einsum("ka,...kl->...al", icos_one, real_one, precision=fast)
    return total - jnp.einsum("ka,...kl->...al", isin_one, imag_one, precision=fast)


DIAGONAL = np.array([1.0, 1.0, 1.0, 0.0, 0.0, 0.0], np.float32)
DOUBLED = np.array([1.0, 1.0, 1.0, 2.0, 2.0, 2.0], np.float32)
FIRST_AXIS = [0, 1, 2, 1, 0, 0]
SECOND_AXIS = [0, 1, 2, 2, 2, 1]


def lead(values, ndim):
    return jnp.asarray(np.asarray(values, np.float32).reshape((-1,) + (1,) * (ndim - 1)))


def elastic_wide(field, first, shear):
    trace = field[0] + field[1] + field[2]
    return 2.0 * shear * field + first * trace * lead(DIAGONAL, field.ndim)


def contract_wide(left, right):
    return jnp.sum(lead(DOUBLED, left.ndim) * left * right, axis=0)


def tangent_wide(field, first, shear, keep, state, gain):
    weight = gain * contract_wide(field, state)
    return keep * elastic_wide(field, first, shear) - weight * state


def green_wide(part, first0, shear0, wave_a, wave_b, wave_c):
    norm = wave_a * wave_a + wave_b * wave_b + wave_c * wave_c
    safe = jnp.where(norm > 0, norm, 1.0)
    living = jnp.where(norm > 0, 1.0, 0.0)
    kappa = (first0 + shear0) / (shear0 * (first0 + 2.0 * shear0))
    along_scale, factor = lax.optimization_barrier(
        (kappa / (safe * safe) * living, 0.5 / (shear0 * safe) * living)
    )
    force_a = part[0] * wave_a + part[5] * wave_b + part[4] * wave_c
    force_b = part[5] * wave_a + part[1] * wave_b + part[3] * wave_c
    force_c = part[4] * wave_a + part[3] * wave_b + part[2] * wave_c
    along = (wave_a * force_a + wave_b * force_b + wave_c * force_c) * along_scale
    waves = (wave_a, wave_b, wave_c)
    forces = (force_a, force_b, force_c)
    ndim = part.ndim

    def pick(table, axes):
        total = None
        for d in range(3):
            mask = lead([1.0 if axes[c] == d else 0.0 for c in range(6)], ndim)
            term = mask * table[d]
            total = term if total is None else total + term
        return total

    wave_one, wave_two = pick(waves, FIRST_AXIS), pick(waves, SECOND_AXIS)
    force_one, force_two = pick(forces, FIRST_AXIS), pick(forces, SECOND_AXIS)
    return factor * (wave_one * force_two + wave_two * force_one) - along * wave_one * wave_two


def signed_waves(index, edge):
    return jnp.where(index < edge // 2, index, index - edge).astype(jnp.float32)


def unit_columns():
    index = jnp.arange(6)
    values = jnp.where(
        index[:, None] == index[None, :], jnp.where(index[:, None] < 3, 1.0, 0.5), 0.0
    )
    return values.astype(jnp.float32)


def solve_slots(held_damage, held_strain, held_count, phase, moduli):
    edge = RES
    plane = edge * edge
    slots = held_damage.shape[0]
    first, shear = moduli_field(phase.reshape(edge, plane), moduli)
    first0 = jnp.mean(moduli[:, 0])
    shear0 = jnp.mean(moduli[:, 1])
    keep = (1.0 - held_damage).reshape(slots, 1, edge, plane)
    state_strain = jnp.transpose(held_strain.reshape(slots, 6, edge, plane), (1, 0, 2, 3))[
        :, :, None
    ]
    state = elastic_wide(state_strain, first, shear)
    gain = keep * shear / (1.0 + contract_wide(state, state))
    flat = jnp.arange(plane, dtype=jnp.int32)
    wave_a = signed_waves(jnp.arange(edge, dtype=jnp.int32), edge)[:, None]
    wave_b = signed_waves(flat // edge, edge)[None, :]
    wave_c = signed_waves(flat % edge, edge)[None, :]
    table = fourier_tables(edge)
    tables = tuple(jnp.asarray(table[k]) for k in ("both_one", "cos_two", "plus_two", "minus_two", "icos_one", "isin_one"))
    macro_field = unit_columns()[:, None, :, None, None]
    field = jnp.broadcast_to(macro_field, (6, slots, 6, edge, plane))
    count = held_count[:, None, None, None]
    first_gap = keep * first - first0
    shear_gap = keep * shear - shear0
    for step in range(ITERS):
        polar = elastic_wide(field, first_gap, shear_gap) - gain * contract_wide(field, state) * state
        polar = lax.optimization_barrier(polar)
        real_part, imag_part = forward(polar, tables)
        real_part = green_wide(real_part, first0, shear0, wave_a, wave_b, wave_c)
        imag_part = green_wide(imag_part, first0, shear0, wave_a, wave_b, wave_c)
        real_part, imag_part = lax.optimization_barrier((real_part, imag_part))
        back = inverse(real_part, imag_part, tables)
        field = jnp.where(step < count, macro_field - back, field)
    stress = elastic_wide(field, keep * first, keep * shear) - gain * contract_wide(field, state) * state
    means = jnp.sum(stress, axis=(3, 4)) / (edge * plane)
    return jnp.transpose(means, (1, 0, 2)).reshape(slots, 36)


def body(damage, strain, route, iters, phase, moduli, tangent_old):
    slots = ACT_DEV
    macro_count = lax.axis_size("macro")
    work_count = lax.axis_size("work")
    devices = macro_count * work_count
    my_macro = lax.axis_index("macro")
    my_work = lax.axis_index("work")
    points, voxels = damage.shape
    width = 7 * voxels
    active = route >= 0
    dest_macro = jnp.where(active, route // slots // work_count, -1)
    macro_ids = jnp.arange(macro_count, dtype=jnp.int32)
    to_macro = dest_macro[None, :] == macro_ids[:, None]
    point_ids = jnp.arange(points, dtype=jnp.int32)
    pick = jnp.max(jnp.where(to_macro, point_ids[None, :], -1), axis=1)
    sending = pick >= 0
    pick = jnp.maximum(pick, 0)
    meta = jnp.stack(
        [route.astype(jnp.float32) + 1.0, iters.astype(jnp.float32), point_ids.astype(jnp.float32) + 1.0]
        + [jnp.zeros((points,), jnp.float32)] * 125,
        axis=1,
    )
    outgoing = jnp.concatenate(
        [damage[pick], strain[pick].reshape(macro_count, 6 * voxels), meta[pick]], axis=1
    )
    outgoing = jnp.where(sending[:, None], outgoing, 0.0)
    arrived = lax.all_to_all(outgoing, "macro", 0, 0, tiled=True)
    valid = arrived[:, width] > 0.5
    rank = jnp.cumsum(valid.astype(jnp.int32)) - 1
    vol_ids = jnp.arange(slots, dtype=jnp.int32)
    select = (valid[None, :] & (rank[None, :] == vol_ids[:, None])).astype(jnp.float32)
    held = jnp.dot(select, arrived, precision=exact)
    held_valid = jnp.sum(select, axis=1) > 0.5
    held_route = (held[:, width] - 1.0).astype(jnp.int32)
    held_count = held[:, width + 1]
    held_row = held[:, width + 2]
    held_from = jnp.dot(select, macro_ids.astype(jnp.float32), precision=exact).astype(jnp.int32)
    tangents = solve_slots(
        held[:, :voxels], held[:, voxels:width].reshape(slots, 6, voxels), held_count, phase, moduli
    )
    dest_ids = jnp.arange(devices, dtype=jnp.int32)
    owner_dev = held_from * work_count + my_work
    to_owner = (held_valid[None, :] & (owner_dev[None, :] == dest_ids[:, None])).astype(jnp.float32)
    owner_part = jnp.dot(
        to_owner, jnp.concatenate([tangents, held_row[:, None]], axis=1), precision=exact
    )
    slot_parts = []
    for s in range(slots):
        hit = held_valid & (held_route == dest_ids[:, None] * slots + s)
        slot_parts.append(jnp.dot(hit.astype(jnp.float32), tangents, precision=exact))
    back = jnp.concatenate([owner_part] + slot_parts, axis=1)
    returned = lax.all_to_all(back, ("macro", "work"), 0, 0, tiled=True)
    row_ids = jnp.arange(points, dtype=jnp.float32) + 1.0
    mine = (returned[None, :, 36] == row_ids[:, None]).astype(jnp.float32)
    chosen = jnp.dot(mine, returned[:, :36], precision=exact)
    tangent = jnp.where(active[:, None], chosen, tangent_old)
    solved = jnp.stack(
        [jnp.sum(returned[:, 37 + 36 * s : 37 + 36 * (s + 1)], axis=0) for s in range(slots)]
    )
    return (tangent, solved)


def solution(mesh):
    return jax.shard_map(
        body,
        mesh=mesh,
        in_specs=(
            P(("macro", "work"), None),
            P(("macro", "work"), None, None),
            P(("macro", "work")),
            P(("macro", "work")),
            P(),
            P(),
            P(("macro", "work"), None),
        ),
        out_specs=(P(("macro", "work"), None), P(("macro", "work"), None)),
        check_vma=False,
    )
```

```python
import numpy as np
import jax
import jax.numpy as jnp
from jax import lax
from jax.sharding import PartitionSpec as P

RES = 16
ITERS = 2
ACT_DEV = 4

exact = lax.Precision.HIGHEST
fast = lax.Precision.HIGH


def moduli_field(phase, moduli):
    first = jnp.where(phase == 1, moduli[1, 0], moduli[0, 0])
    shear = jnp.where(phase == 1, moduli[1, 1], moduli[0, 1])
    return (first, shear)


def elastic(field, first, shear):
    trace = field[0] + field[1] + field[2]
    parts = [2.0 * shear * field[c] + first * trace for c in range(3)]
    parts = parts + [2.0 * shear * field[c] for c in range(3, 6)]
    return jnp.stack(parts)


def contract(left, right):
    diagonal = left[0] * right[0] + left[1] * right[1] + left[2] * right[2]
    return diagonal + 2.0 * (left[3] * right[3] + left[4] * right[4] + left[5] * right[5])


def green(part, first0, shear0, wave_a, wave_b, wave_c):
    norm = wave_a * wave_a + wave_b * wave_b + wave_c * wave_c
    safe = jnp.where(norm > 0, norm, 1.0)
    living = jnp.where(norm > 0, 1.0, 0.0)
    force_a = part[0] * wave_a + part[5] * wave_b + part[4] * wave_c
    force_b = part[5] * wave_a + part[1] * wave_b + part[3] * wave_c
    force_c = part[4] * wave_a + part[3] * wave_b + part[2] * wave_c
    kappa = (first0 + shear0) / (shear0 * (first0 + 2.0 * shear0))
    along = (wave_a * force_a + wave_b * force_b + wave_c * force_c) * kappa / (safe * safe)
    factor = 0.5 / (shear0 * safe)
    parts = [
        factor * 2.0 * wave_a * force_a - along * wave_a * wave_a,
        factor * 2.0 * wave_b * force_b - along * wave_b * wave_b,
        factor * 2.0 * wave_c * force_c - along * wave_c * wave_c,
        factor * (wave_c * force_b + wave_b * force_c) - along * wave_b * wave_c,
        factor * (wave_c * force_a + wave_a * force_c) - along * wave_a * wave_c,
        factor * (wave_b * force_a + wave_a * force_b) - along * wave_a * wave_b,
    ]
    return jnp.stack(parts) * living


def fourier_tables(edge):
    line = np.arange(edge)
    angle_one = (np.outer(line, line) % edge) * (2.0 * np.pi / edge)
    flat = np.arange(edge * edge)
    rows, cols = flat // edge, flat % edge
    angle_two = (np.outer(rows, rows) + np.outer(cols, cols)) % edge
    angle_two = angle_two * (2.0 * np.pi / edge)
    volume = float(edge ** 3)
    return dict(
        cos_one=np.cos(angle_one).astype(np.float32),
        sin_one=np.sin(angle_one).astype(np.float32),
        cos_two=np.cos(angle_two).astype(np.float32),
        nsin_two=(-np.sin(angle_two)).astype(np.float32),
        icos_two=(np.cos(angle_two) / volume).astype(np.float32),
        insin_two=(-np.sin(angle_two) / volume).astype(np.float32),
        plus_two=(np.cos(angle_two) - np.sin(angle_two)).astype(np.float32),
        both_one=np.concatenate([np.cos(angle_one), -np.sin(angle_one)]).astype(np.float32),
        icos_one=(np.cos(angle_one) / volume).astype(np.float32),
        isin_one=(np.sin(angle_one) / volume).astype(np.float32),
        minus_two=(-np.sin(angle_two) - np.cos(angle_two)).astype(np.float32),
    )


def forward(field, tables):
    both_one, cos_two, plus_two, minus_two, icos_one, isin_one = tables
    edge = icos_one.shape[0]
    stacked = jnp.einsum("ka,...al->...kl", both_one, field, precision=fast)
    real_one = stacked[..., :edge, :]
    imag_one = stacked[..., edge:, :]
    both = jnp.matmul(real_one + imag_one, cos_two, precision=fast)
    real_two = both - jnp.matmul(imag_one, plus_two, precision=fast)
    imag_two = both + jnp.matmul(real_one, minus_two, precision=fast)
    return (real_two, imag_two)


def inverse(real_two, imag_two, tables):
    both_one, cos_two, plus_two, minus_two, icos_one, isin_one = tables
    both = jnp.matmul(real_two + imag_two, cos_two, precision=fast)
    real_one = both + jnp.matmul(imag_two, minus_two, precision=fast)
    imag_one = both - jnp.matmul(real_two, plus_two, precision=fast)
    total = jnp.einsum("ka,...kl->...al", icos_one, real_one, precision=fast)
    return total - jnp.einsum("ka,...kl->...al", isin_one, imag_one, precision=fast)


DIAGONAL = np.array([1.0, 1.0, 1.0, 0.0, 0.0, 0.0], np.float32)
DOUBLED = np.array([1.0, 1.0, 1.0, 2.0, 2.0, 2.0], np.float32)
FIRST_AXIS = [0, 1, 2, 1, 0, 0]
SECOND_AXIS = [0, 1, 2, 2, 2, 1]


def lead(values, ndim):
    return jnp.asarray(np.asarray(values, np.float32).reshape((-1,) + (1,) * (ndim - 1)))


def elastic_wide(field, first, shear):
    trace = field[0] + field[1] + field[2]
    return 2.0 * shear * field + first * trace * lead(DIAGONAL, field.ndim)


def contract_wide(left, right):
    return jnp.sum(lead(DOUBLED, left.ndim) * left * right, axis=0)


def tangent_wide(field, first, shear, keep, state, gain):
    weight = gain * contract_wide(field, state)
    return keep * elastic_wide(field, first, shear) - weight * state


def green_wide(part, first0, shear0, wave_a, wave_b, wave_c):
    norm = wave_a * wave_a + wave_b * wave_b + wave_c * wave_c
    safe = jnp.where(norm > 0, norm, 1.0)
    living = jnp.where(norm > 0, 1.0, 0.0)
    kappa = (first0 + shear0) / (shear0 * (first0 + 2.0 * shear0))
    along_scale, factor = lax.optimization_barrier(
        (kappa / (safe * safe) * living, 0.5 / (shear0 * safe) * living)
    )
    force_a = part[0] * wave_a + part[5] * wave_b + part[4] * wave_c
    force_b = part[5] * wave_a + part[1] * wave_b + part[3] * wave_c
    force_c = part[4] * wave_a + part[3] * wave_b + part[2] * wave_c
    along = (wave_a * force_a + wave_b * force_b + wave_c * force_c) * along_scale
    waves = (wave_a, wave_b, wave_c)
    forces = (force_a, force_b, force_c)
    ndim = part.ndim

    def pick(table, axes):
        total = None
        for d in range(3):
            mask = lead([1.0 if axes[c] == d else 0.0 for c in range(6)], ndim)
            term = mask * table[d]
            total = term if total is None else total + term
        return total

    wave_one, wave_two = pick(waves, FIRST_AXIS), pick(waves, SECOND_AXIS)
    force_one, force_two = pick(forces, FIRST_AXIS), pick(forces, SECOND_AXIS)
    return factor * (wave_one * force_two + wave_two * force_one) - along * wave_one * wave_two


def signed_waves(index, edge):
    return jnp.where(index < edge // 2, index, index - edge).astype(jnp.float32)


def unit_columns():
    index = jnp.arange(6)
    values = jnp.where(
        index[:, None] == index[None, :], jnp.where(index[:, None] < 3, 1.0, 0.5), 0.0
    )
    return values.astype(jnp.float32)


def solve_slots(held_damage, held_strain, held_count, phase, moduli):
    edge = RES
    plane = edge * edge
    slots = held_damage.shape[0]
    first, shear = moduli_field(phase.reshape(edge, plane), moduli)
    first0 = jnp.mean(moduli[:, 0])
    shear0 = jnp.mean(moduli[:, 1])
    keep = (1.0 - held_damage).reshape(slots, 1, edge, plane)
    state_strain = jnp.transpose(held_strain.reshape(slots, 6, edge, plane), (1, 0, 2, 3))[
        :, :, None
    ]
    state = elastic_wide(state_strain, first, shear)
    gain = keep * shear / (1.0 + contract_wide(state, state))
    flat = jnp.arange(plane, dtype=jnp.int32)
    wave_a = signed_waves(jnp.arange(edge, dtype=jnp.int32), edge)[:, None]
    wave_b = signed_waves(flat // edge, edge)[None, :]
    wave_c = signed_waves(flat % edge, edge)[None, :]
    table = fourier_tables(edge)
    tables = tuple(jnp.asarray(table[k]) for k in ("both_one", "cos_two", "plus_two", "minus_two", "icos_one", "isin_one"))
    macro_field = unit_columns()[:, None, :, None, None]
    field = jnp.broadcast_to(macro_field, (6, slots, 6, edge, plane))
    count = held_count[:, None, None, None]
    first_gap = keep * first - first0
    double_gap = 2.0 * (keep * shear - shear0)
    weighted_state = lead(DOUBLED, state.ndim) * state
    gained_state = gain * state
    diagonal = lead(DIAGONAL, state.ndim)
    for step in range(ITERS):
        trace = field[0] + field[1] + field[2]
        coupling = jnp.sum(weighted_state * field, axis=0)
        polar = double_gap * field + first_gap * trace * diagonal - coupling * gained_state
        polar = lax.optimization_barrier(polar)
        real_part, imag_part = forward(polar, tables)
        real_part = green_wide(real_part, first0, shear0, wave_a, wave_b, wave_c)
        imag_part = green_wide(imag_part, first0, shear0, wave_a, wave_b, wave_c)
        real_part, imag_part = lax.optimization_barrier((real_part, imag_part))
        back = inverse(real_part, imag_part, tables)
        field = jnp.where(step < count, macro_field - back, field)
    stress = tangent_wide(field, first, shear, keep, state, gain)
    means = jnp.sum(stress, axis=(3, 4)) / (edge * plane)
    return jnp.transpose(means, (1, 0, 2)).reshape(slots, 36)


def body(damage, strain, route, iters, phase, moduli, tangent_old):
    slots = ACT_DEV
    macro_count = lax.axis_size("macro")
    work_count = lax.axis_size("work")
    devices = macro_count * work_count
    my_macro = lax.axis_index("macro")
    my_work = lax.axis_index("work")
    points, voxels = damage.shape
    width = 7 * voxels
    active = route >= 0
    dest_macro = jnp.where(active, route // slots // work_count, -1)
    macro_ids = jnp.arange(macro_count, dtype=jnp.int32)
    to_macro = dest_macro[None, :] == macro_ids[:, None]
    point_ids = jnp.arange(points, dtype=jnp.int32)
    pick = jnp.max(jnp.where(to_macro, point_ids[None, :], -1), axis=1)
    sending = pick >= 0
    pick = jnp.maximum(pick, 0)
    meta = jnp.stack(
        [route.astype(jnp.float32) + 1.0, iters.astype(jnp.float32), point_ids.astype(jnp.float32) + 1.0]
        + [jnp.zeros((points,), jnp.float32)] * 125,
        axis=1,
    )
    outgoing = jnp.concatenate(
        [damage[pick], strain[pick].reshape(macro_count, 6 * voxels), meta[pick]], axis=1
    )
    outgoing = jnp.where(sending[:, None], outgoing, 0.0)
    arrived = lax.all_to_all(outgoing, "macro", 0, 0, tiled=True)
    valid = arrived[:, width] > 0.5
    rank = jnp.cumsum(valid.astype(jnp.int32)) - 1
    vol_ids = jnp.arange(slots, dtype=jnp.int32)
    select = (valid[None, :] & (rank[None, :] == vol_ids[:, None])).astype(jnp.float32)
    held = jnp.dot(select, arrived, precision=exact)
    held_valid = jnp.sum(select, axis=1) > 0.5
    held_route = (held[:, width] - 1.0).astype(jnp.int32)
    held_count = held[:, width + 1]
    held_row = held[:, width + 2]
    held_from = jnp.dot(select, macro_ids.astype(jnp.float32), precision=exact).astype(jnp.int32)
    tangents = solve_slots(
        held[:, :voxels], held[:, voxels:width].reshape(slots, 6, voxels), held_count, phase, moduli
    )
    dest_ids = jnp.arange(devices, dtype=jnp.int32)
    owner_dev = held_from * work_count + my_work
    to_owner = (held_valid[None, :] & (owner_dev[None, :] == dest_ids[:, None])).astype(jnp.float32)
    owner_part = jnp.dot(
        to_owner, jnp.concatenate([tangents, held_row[:, None]], axis=1), precision=exact
    )
    slot_parts = []
    for s in range(slots):
        hit = held_valid & (held_route == dest_ids[:, None] * slots + s)
        slot_parts.append(jnp.dot(hit.astype(jnp.float32), tangents, precision=exact))
    back = jnp.concatenate([owner_part] + slot_parts, axis=1)
    returned = lax.all_to_all(back, ("macro", "work"), 0, 0, tiled=True)
    row_ids = jnp.arange(points, dtype=jnp.float32) + 1.0
    mine = (returned[None, :, 36] == row_ids[:, None]).astype(jnp.float32)
    chosen = jnp.dot(mine, returned[:, :36], precision=exact)
    tangent = jnp.where(active[:, None], chosen, tangent_old)
    solved = jnp.stack(
        [jnp.sum(returned[:, 37 + 36 * s : 37 + 36 * (s + 1)], axis=0) for s in range(slots)]
    )
    return (tangent, solved)


def solution(mesh):
    return jax.shard_map(
        body,
        mesh=mesh,
        in_specs=(
            P(("macro", "work"), None),
            P(("macro", "work"), None, None),
            P(("macro", "work")),
            P(("macro", "work")),
            P(),
            P(),
            P(("macro", "work"), None),
        ),
        out_specs=(P(("macro", "work"), None), P(("macro", "work"), None)),
        check_vma=False,
    )
```

```python
import numpy as np
import jax
import jax.numpy as jnp
from jax import lax
from jax.sharding import PartitionSpec as P

RES = 16
ITERS = 2
ACT_DEV = 4

exact = lax.Precision.HIGHEST
fast = lax.Precision.HIGH


def moduli_field(phase, moduli):
    first = jnp.where(phase == 1, moduli[1, 0], moduli[0, 0])
    shear = jnp.where(phase == 1, moduli[1, 1], moduli[0, 1])
    return (first, shear)


def elastic(field, first, shear):
    trace = field[0] + field[1] + field[2]
    parts = [2.0 * shear * field[c] + first * trace for c in range(3)]
    parts = parts + [2.0 * shear * field[c] for c in range(3, 6)]
    return jnp.stack(parts)


def contract(left, right):
    diagonal = left[0] * right[0] + left[1] * right[1] + left[2] * right[2]
    return diagonal + 2.0 * (left[3] * right[3] + left[4] * right[4] + left[5] * right[5])


def green(part, first0, shear0, wave_a, wave_b, wave_c):
    norm = wave_a * wave_a + wave_b * wave_b + wave_c * wave_c
    safe = jnp.where(norm > 0, norm, 1.0)
    living = jnp.where(norm > 0, 1.0, 0.0)
    force_a = part[0] * wave_a + part[5] * wave_b + part[4] * wave_c
    force_b = part[5] * wave_a + part[1] * wave_b + part[3] * wave_c
    force_c = part[4] * wave_a + part[3] * wave_b + part[2] * wave_c
    kappa = (first0 + shear0) / (shear0 * (first0 + 2.0 * shear0))
    along = (wave_a * force_a + wave_b * force_b + wave_c * force_c) * kappa / (safe * safe)
    factor = 0.5 / (shear0 * safe)
    parts = [
        factor * 2.0 * wave_a * force_a - along * wave_a * wave_a,
        factor * 2.0 * wave_b * force_b - along * wave_b * wave_b,
        factor * 2.0 * wave_c * force_c - along * wave_c * wave_c,
        factor * (wave_c * force_b + wave_b * force_c) - along * wave_b * wave_c,
        factor * (wave_c * force_a + wave_a * force_c) - along * wave_a * wave_c,
        factor * (wave_b * force_a + wave_a * force_b) - along * wave_a * wave_b,
    ]
    return jnp.stack(parts) * living


def fourier_tables(edge):
    line = np.arange(edge)
    angle_one = (np.outer(line, line) % edge) * (2.0 * np.pi / edge)
    flat = np.arange(edge * edge)
    rows, cols = flat // edge, flat % edge
    angle_two = (np.outer(rows, rows) + np.outer(cols, cols)) % edge
    angle_two = angle_two * (2.0 * np.pi / edge)
    volume = float(edge ** 3)
    return dict(
        cos_one=np.cos(angle_one).astype(np.float32),
        sin_one=np.sin(angle_one).astype(np.float32),
        cos_two=np.cos(angle_two).astype(np.float32),
        nsin_two=(-np.sin(angle_two)).astype(np.float32),
        icos_two=(np.cos(angle_two) / volume).astype(np.float32),
        insin_two=(-np.sin(angle_two) / volume).astype(np.float32),
        plus_two=(np.cos(angle_two) - np.sin(angle_two)).astype(np.float32),
        both_one=np.concatenate([np.cos(angle_one), -np.sin(angle_one)]).astype(np.float32),
        icos_one=(np.cos(angle_one) / volume).astype(np.float32),
        isin_one=(np.sin(angle_one) / volume).astype(np.float32),
        minus_two=(-np.sin(angle_two) - np.cos(angle_two)).astype(np.float32),
    )


def forward(field, tables):
    both_one, cos_two, plus_two, minus_two, icos_one, isin_one = tables
    edge = icos_one.shape[0]
    stacked = jnp.einsum("ka,...al->...kl", both_one, field, precision=fast)
    real_one = stacked[..., :edge, :]
    imag_one = stacked[..., edge:, :]
    both = jnp.matmul(real_one + imag_one, cos_two, precision=fast)
    real_two = both - jnp.matmul(imag_one, plus_two, precision=fast)
    imag_two = both + jnp.matmul(real_one, minus_two, precision=fast)
    return (real_two, imag_two)


def inverse(real_two, imag_two, tables):
    both_one, cos_two, plus_two, minus_two, icos_one, isin_one = tables
    both = jnp.matmul(real_two + imag_two, cos_two, precision=fast)
    real_one = both + jnp.matmul(imag_two, minus_two, precision=fast)
    imag_one = both - jnp.matmul(real_two, plus_two, precision=fast)
    total = jnp.einsum("ka,...kl->...al", icos_one, real_one, precision=fast)
    return total - jnp.einsum("ka,...kl->...al", isin_one, imag_one, precision=fast)


DIAGONAL = np.array([1.0, 1.0, 1.0, 0.0, 0.0, 0.0], np.float32)
DOUBLED = np.array([1.0, 1.0, 1.0, 2.0, 2.0, 2.0], np.float32)
FIRST_AXIS = [0, 1, 2, 1, 0, 0]
SECOND_AXIS = [0, 1, 2, 2, 2, 1]


def lead(values, ndim):
    return jnp.asarray(np.asarray(values, np.float32).reshape((-1,) + (1,) * (ndim - 1)))


def elastic_wide(field, first, shear):
    trace = field[0] + field[1] + field[2]
    return 2.0 * shear * field + first * trace * lead(DIAGONAL, field.ndim)


def contract_wide(left, right):
    return jnp.sum(lead(DOUBLED, left.ndim) * left * right, axis=0)


def tangent_wide(field, first, shear, keep, state, gain):
    weight = gain * contract_wide(field, state)
    return keep * elastic_wide(field, first, shear) - weight * state


def green_wide(part, first0, shear0, wave_a, wave_b, wave_c):
    norm = wave_a * wave_a + wave_b * wave_b + wave_c * wave_c
    safe = jnp.where(norm > 0, norm, 1.0)
    living = jnp.where(norm > 0, 1.0, 0.0)
    kappa = (first0 + shear0) / (shear0 * (first0 + 2.0 * shear0))
    along_scale, factor = lax.optimization_barrier(
        (kappa / (safe * safe) * living, 0.5 / (shear0 * safe) * living)
    )
    force_a = part[0] * wave_a + part[5] * wave_b + part[4] * wave_c
    force_b = part[5] * wave_a + part[1] * wave_b + part[3] * wave_c
    force_c = part[4] * wave_a + part[3] * wave_b + part[2] * wave_c
    along = wave_a * force_a + wave_b * force_b + wave_c * force_c
    waves = (wave_a, wave_b, wave_c)
    forces = (force_a, force_b, force_c)
    ndim = part.ndim

    def pick(table, axes, width):
        total = None
        for d in range(3):
            mask = lead([1.0 if axes[c] == d else 0.0 for c in range(6)], width)
            term = mask * table[d]
            total = term if total is None else total + term
        return total

    wave_one, wave_two = pick(waves, FIRST_AXIS, 3), pick(waves, SECOND_AXIS, 3)
    factor_one, factor_two, along_pair = lax.optimization_barrier(
        (factor * wave_one, factor * wave_two, along_scale * wave_one * wave_two)
    )
    shape = (6,) + (1,) * (ndim - 3) + factor_one.shape[1:]
    factor_one, factor_two, along_pair = (
        factor_one.reshape(shape), factor_two.reshape(shape), along_pair.reshape(shape)
    )
    force_one, force_two = pick(forces, FIRST_AXIS, ndim), pick(forces, SECOND_AXIS, ndim)
    return factor_one * force_two + factor_two * force_one - along * along_pair


def signed_waves(index, edge):
    return jnp.where(index < edge // 2, index, index - edge).astype(jnp.float32)


def unit_columns():
    index = jnp.arange(6)
    values = jnp.where(
        index[:, None] == index[None, :], jnp.where(index[:, None] < 3, 1.0, 0.5), 0.0
    )
    return values.astype(jnp.float32)


def solve_slots(held_damage, held_strain, held_count, phase, moduli):
    edge = RES
    plane = edge * edge
    slots = held_damage.shape[0]
    first, shear = moduli_field(phase.reshape(edge, plane), moduli)
    first0 = jnp.mean(moduli[:, 0])
    shear0 = jnp.mean(moduli[:, 1])
    keep = (1.0 - held_damage).reshape(slots, 1, edge, plane)
    state_strain = jnp.transpose(held_strain.reshape(slots, 6, edge, plane), (1, 0, 2, 3))[
        :, :, None
    ]
    state = elastic_wide(state_strain, first, shear)
    gain = keep * shear / (1.0 + contract_wide(state, state))
    flat = jnp.arange(plane, dtype=jnp.int32)
    wave_a = signed_waves(jnp.arange(edge, dtype=jnp.int32), edge)[:, None]
    wave_b = signed_waves(flat // edge, edge)[None, :]
    wave_c = signed_waves(flat % edge, edge)[None, :]
    table = fourier_tables(edge)
    tables = tuple(jnp.asarray(table[k]) for k in ("both_one", "cos_two", "plus_two", "minus_two", "icos_one", "isin_one"))
    macro_field = unit_columns()[:, None, :, None, None]
    field = jnp.broadcast_to(macro_field, (6, slots, 6, edge, plane))
    count = held_count[:, None, None, None]
    first_gap = keep * first - first0
    shear_gap = keep * shear - shear0
    for step in range(ITERS):
        polar = elastic_wide(field, first_gap, shear_gap) - gain * contract_wide(field, state) * state
        polar = lax.optimization_barrier(polar)
        real_part, imag_part = forward(polar, tables)
        real_part = green_wide(real_part, first0, shear0, wave_a, wave_b, wave_c)
        imag_part = green_wide(imag_part, first0, shear0, wave_a, wave_b, wave_c)
        real_part, imag_part = lax.optimization_barrier((real_part, imag_part))
        back = inverse(real_part, imag_part, tables)
        field = jnp.where(step < count, macro_field - back, field)
    stress = tangent_wide(field, first, shear, keep, state, gain)
    means = jnp.sum(stress, axis=(3, 4)) / (edge * plane)
    return jnp.transpose(means, (1, 0, 2)).reshape(slots, 36)


def body(damage, strain, route, iters, phase, moduli, tangent_old):
    slots = ACT_DEV
    macro_count = lax.axis_size("macro")
    work_count = lax.axis_size("work")
    devices = macro_count * work_count
    my_macro = lax.axis_index("macro")
    my_work = lax.axis_index("work")
    points, voxels = damage.shape
    width = 7 * voxels
    active = route >= 0
    dest_macro = jnp.where(active, route // slots // work_count, -1)
    macro_ids = jnp.arange(macro_count, dtype=jnp.int32)
    to_macro = dest_macro[None, :] == macro_ids[:, None]
    point_ids = jnp.arange(points, dtype=jnp.int32)
    pick = jnp.max(jnp.where(to_macro, point_ids[None, :], -1), axis=1)
    sending = pick >= 0
    pick = jnp.maximum(pick, 0)
    meta = jnp.stack(
        [route.astype(jnp.float32) + 1.0, iters.astype(jnp.float32), point_ids.astype(jnp.float32) + 1.0]
        + [jnp.zeros((points,), jnp.float32)] * 125,
        axis=1,
    )
    outgoing = jnp.concatenate(
        [damage[pick], strain[pick].reshape(macro_count, 6 * voxels), meta[pick]], axis=1
    )
    outgoing = jnp.where(sending[:, None], outgoing, 0.0)
    arrived = lax.all_to_all(outgoing, "macro", 0, 0, tiled=True)
    valid = arrived[:, width] > 0.5
    rank = jnp.cumsum(valid.astype(jnp.int32)) - 1
    vol_ids = jnp.arange(slots, dtype=jnp.int32)
    select = (valid[None, :] & (rank[None, :] == vol_ids[:, None])).astype(jnp.float32)
    held = jnp.dot(select, arrived, precision=exact)
    held_valid = jnp.sum(select, axis=1) > 0.5
    held_route = (held[:, width] - 1.0).astype(jnp.int32)
    held_count = held[:, width + 1]
    held_row = held[:, width + 2]
    held_from = jnp.dot(select, macro_ids.astype(jnp.float32), precision=exact).astype(jnp.int32)
    tangents = solve_slots(
        held[:, :voxels], held[:, voxels:width].reshape(slots, 6, voxels), held_count, phase, moduli
    )
    dest_ids = jnp.arange(devices, dtype=jnp.int32)
    owner_dev = held_from * work_count + my_work
    to_owner = (held_valid[None, :] & (owner_dev[None, :] == dest_ids[:, None])).astype(jnp.float32)
    owner_part = jnp.dot(
        to_owner, jnp.concatenate([tangents, held_row[:, None]], axis=1), precision=exact
    )
    slot_parts = []
    for s in range(slots):
        hit = held_valid & (held_route == dest_ids[:, None] * slots + s)
        slot_parts.append(jnp.dot(hit.astype(jnp.float32), tangents, precision=exact))
    back = jnp.concatenate([owner_part] + slot_parts, axis=1)
    returned = lax.all_to_all(back, ("macro", "work"), 0, 0, tiled=True)
    row_ids = jnp.arange(points, dtype=jnp.float32) + 1.0
    mine = (returned[None, :, 36] == row_ids[:, None]).astype(jnp.float32)
    chosen = jnp.dot(mine, returned[:, :36], precision=exact)
    tangent = jnp.where(active[:, None], chosen, tangent_old)
    solved = jnp.stack(
        [jnp.sum(returned[:, 37 + 36 * s : 37 + 36 * (s + 1)], axis=0) for s in range(slots)]
    )
    return (tangent, solved)


def solution(mesh):
    return jax.shard_map(
        body,
        mesh=mesh,
        in_specs=(
            P(("macro", "work"), None),
            P(("macro", "work"), None, None),
            P(("macro", "work")),
            P(("macro", "work")),
            P(),
            P(),
            P(("macro", "work"), None),
        ),
        out_specs=(P(("macro", "work"), None), P(("macro", "work"), None)),
        check_vma=False,
    )
```

```python
import numpy as np
import jax
import jax.numpy as jnp
from jax import lax
from jax.sharding import PartitionSpec as P

RES = 16
ITERS = 2
ACT_DEV = 4

exact = lax.Precision.HIGHEST
fast = lax.Precision.HIGH


def moduli_field(phase, moduli):
    first = jnp.where(phase == 1, moduli[1, 0], moduli[0, 0])
    shear = jnp.where(phase == 1, moduli[1, 1], moduli[0, 1])
    return (first, shear)


def elastic(field, first, shear):
    trace = field[0] + field[1] + field[2]
    parts = [2.0 * shear * field[c] + first * trace for c in range(3)]
    parts = parts + [2.0 * shear * field[c] for c in range(3, 6)]
    return jnp.stack(parts)


def contract(left, right):
    diagonal = left[0] * right[0] + left[1] * right[1] + left[2] * right[2]
    return diagonal + 2.0 * (left[3] * right[3] + left[4] * right[4] + left[5] * right[5])


def green(part, first0, shear0, wave_a, wave_b, wave_c):
    norm = wave_a * wave_a + wave_b * wave_b + wave_c * wave_c
    safe = jnp.where(norm > 0, norm, 1.0)
    living = jnp.where(norm > 0, 1.0, 0.0)
    force_a = part[0] * wave_a + part[5] * wave_b + part[4] * wave_c
    force_b = part[5] * wave_a + part[1] * wave_b + part[3] * wave_c
    force_c = part[4] * wave_a + part[3] * wave_b + part[2] * wave_c
    kappa = (first0 + shear0) / (shear0 * (first0 + 2.0 * shear0))
    along = (wave_a * force_a + wave_b * force_b + wave_c * force_c) * kappa / (safe * safe)
    factor = 0.5 / (shear0 * safe)
    parts = [
        factor * 2.0 * wave_a * force_a - along * wave_a * wave_a,
        factor * 2.0 * wave_b * force_b - along * wave_b * wave_b,
        factor * 2.0 * wave_c * force_c - along * wave_c * wave_c,
        factor * (wave_c * force_b + wave_b * force_c) - along * wave_b * wave_c,
        factor * (wave_c * force_a + wave_a * force_c) - along * wave_a * wave_c,
        factor * (wave_b * force_a + wave_a * force_b) - along * wave_a * wave_b,
    ]
    return jnp.stack(parts) * living


def fourier_tables(edge):
    line = np.arange(edge)
    angle_one = (np.outer(line, line) % edge) * (2.0 * np.pi / edge)
    flat = np.arange(edge * edge)
    rows, cols = flat // edge, flat % edge
    angle_two = (np.outer(rows, rows) + np.outer(cols, cols)) % edge
    angle_two = angle_two * (2.0 * np.pi / edge)
    volume = float(edge ** 3)
    return dict(
        cos_one=np.cos(angle_one).astype(np.float32),
        sin_one=np.sin(angle_one).astype(np.float32),
        cos_two=np.cos(angle_two).astype(np.float32),
        nsin_two=(-np.sin(angle_two)).astype(np.float32),
        icos_two=(np.cos(angle_two) / volume).astype(np.float32),
        insin_two=(-np.sin(angle_two) / volume).astype(np.float32),
        plus_two=(np.cos(angle_two) - np.sin(angle_two)).astype(np.float32),
        both_one=np.concatenate([np.cos(angle_one), -np.sin(angle_one)]).astype(np.float32),
        icos_one=(np.cos(angle_one) / volume).astype(np.float32),
        isin_one=(np.sin(angle_one) / volume).astype(np.float32),
        minus_two=(-np.sin(angle_two) - np.cos(angle_two)).astype(np.float32),
    )


def forward(field, tables):
    both_one, cos_two, plus_two, minus_two, icos_one, isin_one = tables
    edge = icos_one.shape[0]
    stacked = jnp.einsum("ka,...al->...kl", both_one, field, precision=fast)
    real_one = stacked[..., :edge, :]
    imag_one = stacked[..., edge:, :]
    both = jnp.matmul(real_one + imag_one, cos_two, precision=fast)
    real_two = both - jnp.matmul(imag_one, plus_two, precision=fast)
    imag_two = both + jnp.matmul(real_one, minus_two, precision=fast)
    return (real_two, imag_two)


def inverse(real_two, imag_two, tables):
    both_one, cos_two, plus_two, minus_two, icos_one, isin_one = tables
    both = jnp.matmul(real_two + imag_two, cos_two, precision=fast)
    real_one = both + jnp.matmul(imag_two, minus_two, precision=fast)
    imag_one = both - jnp.matmul(real_two, plus_two, precision=fast)
    total = jnp.einsum("ka,...kl->...al", icos_one, real_one, precision=fast)
    return total - jnp.einsum("ka,...kl->...al", isin_one, imag_one, precision=fast)


DIAGONAL = np.array([1.0, 1.0, 1.0, 0.0, 0.0, 0.0], np.float32)
DOUBLED = np.array([1.0, 1.0, 1.0, 2.0, 2.0, 2.0], np.float32)
FIRST_AXIS = [0, 1, 2, 1, 0, 0]
SECOND_AXIS = [0, 1, 2, 2, 2, 1]


def lead(values, ndim):
    return jnp.asarray(np.asarray(values, np.float32).reshape((-1,) + (1,) * (ndim - 1)))


def elastic_wide(field, first, shear):
    trace = field[0] + field[1] + field[2]
    return 2.0 * shear * field + first * trace * lead(DIAGONAL, field.ndim)


def contract_wide(left, right):
    return jnp.sum(lead(DOUBLED, left.ndim) * left * right, axis=0)


def tangent_wide(field, first, shear, keep, state, gain):
    weight = gain * contract_wide(field, state)
    return keep * elastic_wide(field, first, shear) - weight * state


def green_wide(part, first0, shear0, wave_a, wave_b, wave_c):
    norm = wave_a * wave_a + wave_b * wave_b + wave_c * wave_c
    safe = jnp.where(norm > 0, norm, 1.0)
    living = jnp.where(norm > 0, 1.0, 0.0)
    kappa = (first0 + shear0) / (shear0 * (first0 + 2.0 * shear0))
    along_scale, factor = lax.optimization_barrier(
        (kappa / (safe * safe) * living, 0.5 / (shear0 * safe) * living)
    )
    force_a = part[0] * wave_a + part[5] * wave_b + part[4] * wave_c
    force_b = part[5] * wave_a + part[1] * wave_b + part[3] * wave_c
    force_c = part[4] * wave_a + part[3] * wave_b + part[2] * wave_c
    along = wave_a * force_a + wave_b * force_b + wave_c * force_c
    waves = (wave_a, wave_b, wave_c)
    forces = (force_a, force_b, force_c)
    ndim = part.ndim

    def pick(table, axes, width):
        total = None
        for d in range(3):
            mask = lead([1.0 if axes[c] == d else 0.0 for c in range(6)], width)
            term = mask * table[d]
            total = term if total is None else total + term
        return total

    wave_one, wave_two = pick(waves, FIRST_AXIS, 3), pick(waves, SECOND_AXIS, 3)
    factor_one, factor_two, along_pair = lax.optimization_barrier(
        (factor * wave_one, factor * wave_two, along_scale * wave_one * wave_two)
    )
    shape = (6,) + (1,) * (ndim - 3) + factor_one.shape[1:]
    factor_one, factor_two, along_pair = (
        factor_one.reshape(shape), factor_two.reshape(shape), along_pair.reshape(shape)
    )
    force_one, force_two = pick(forces, FIRST_AXIS, ndim), pick(forces, SECOND_AXIS, ndim)
    return factor_one * force_two + factor_two * force_one - along * along_pair


def signed_waves(index, edge):
    return jnp.where(index < edge // 2, index, index - edge).astype(jnp.float32)


def unit_columns():
    index = jnp.arange(6)
    values = jnp.where(
        index[:, None] == index[None, :], jnp.where(index[:, None] < 3, 1.0, 0.5), 0.0
    )
    return values.astype(jnp.float32)


def solve_slots(held_damage, held_strain, held_count, phase, moduli):
    edge = RES
    plane = edge * edge
    slots = held_damage.shape[0]
    first, shear = moduli_field(phase.reshape(edge, plane), moduli)
    first0 = jnp.mean(moduli[:, 0])
    shear0 = jnp.mean(moduli[:, 1])
    keep = (1.0 - held_damage).reshape(slots, 1, edge, plane)
    state_strain = jnp.transpose(held_strain.reshape(slots, 6, edge, plane), (1, 0, 2, 3))[
        :, :, None
    ]
    state = elastic_wide(state_strain, first, shear)
    gain = keep * shear / (1.0 + contract_wide(state, state))
    flat = jnp.arange(plane, dtype=jnp.int32)
    wave_a = signed_waves(jnp.arange(edge, dtype=jnp.int32), edge)[:, None]
    wave_b = signed_waves(flat // edge, edge)[None, :]
    wave_c = signed_waves(flat % edge, edge)[None, :]
    table = fourier_tables(edge)
    tables = tuple(jnp.asarray(table[k]) for k in ("both_one", "cos_two", "plus_two", "minus_two", "icos_one", "isin_one"))
    macro_field = unit_columns()[:, None, :, None, None]
    field = jnp.broadcast_to(macro_field, (6, slots, 6, edge, plane))
    count = held_count[:, None, None, None]
    first_gap = keep * first - first0
    shear_gap = keep * shear - shear0
    for step in range(ITERS):
        polar = elastic_wide(field, first_gap, shear_gap) - gain * contract_wide(field, state) * state
        if step == 0:
            polar = lax.optimization_barrier(polar)
        real_part, imag_part = forward(polar, tables)
        real_part = green_wide(real_part, first0, shear0, wave_a, wave_b, wave_c)
        imag_part = green_wide(imag_part, first0, shear0, wave_a, wave_b, wave_c)
        real_part, imag_part = lax.optimization_barrier((real_part, imag_part))
        back = inverse(real_part, imag_part, tables)
        field = jnp.where(step < count, macro_field - back, field)
    stress = tangent_wide(field, first, shear, keep, state, gain)
    means = jnp.sum(stress, axis=(3, 4)) / (edge * plane)
    return jnp.transpose(means, (1, 0, 2)).reshape(slots, 36)


def body(damage, strain, route, iters, phase, moduli, tangent_old):
    slots = ACT_DEV
    macro_count = lax.axis_size("macro")
    work_count = lax.axis_size("work")
    devices = macro_count * work_count
    my_macro = lax.axis_index("macro")
    my_work = lax.axis_index("work")
    points, voxels = damage.shape
    width = 7 * voxels
    active = route >= 0
    dest_macro = jnp.where(active, route // slots // work_count, -1)
    macro_ids = jnp.arange(macro_count, dtype=jnp.int32)
    to_macro = dest_macro[None, :] == macro_ids[:, None]
    point_ids = jnp.arange(points, dtype=jnp.int32)
    pick = jnp.max(jnp.where(to_macro, point_ids[None, :], -1), axis=1)
    sending = pick >= 0
    pick = jnp.maximum(pick, 0)
    meta = jnp.stack(
        [route.astype(jnp.float32) + 1.0, iters.astype(jnp.float32), point_ids.astype(jnp.float32) + 1.0]
        + [jnp.zeros((points,), jnp.float32)] * 125,
        axis=1,
    )
    outgoing = jnp.concatenate(
        [damage[pick], strain[pick].reshape(macro_count, 6 * voxels), meta[pick]], axis=1
    )
    outgoing = jnp.where(sending[:, None], outgoing, 0.0)
    arrived = lax.all_to_all(outgoing, "macro", 0, 0, tiled=True)
    valid = arrived[:, width] > 0.5
    rank = jnp.cumsum(valid.astype(jnp.int32)) - 1
    vol_ids = jnp.arange(slots, dtype=jnp.int32)
    select = (valid[None, :] & (rank[None, :] == vol_ids[:, None])).astype(jnp.float32)
    held = jnp.dot(select, arrived, precision=exact)
    held_valid = jnp.sum(select, axis=1) > 0.5
    held_route = (held[:, width] - 1.0).astype(jnp.int32)
    held_count = held[:, width + 1]
    held_row = held[:, width + 2]
    held_from = jnp.dot(select, macro_ids.astype(jnp.float32), precision=exact).astype(jnp.int32)
    tangents = solve_slots(
        held[:, :voxels], held[:, voxels:width].reshape(slots, 6, voxels), held_count, phase, moduli
    )
    dest_ids = jnp.arange(devices, dtype=jnp.int32)
    owner_dev = held_from * work_count + my_work
    to_owner = (held_valid[None, :] & (owner_dev[None, :] == dest_ids[:, None])).astype(jnp.float32)
    owner_part = jnp.dot(
        to_owner, jnp.concatenate([tangents, held_row[:, None]], axis=1), precision=exact
    )
    slot_parts = []
    for s in range(slots):
        hit = held_valid & (held_route == dest_ids[:, None] * slots + s)
        slot_parts.append(jnp.dot(hit.astype(jnp.float32), tangents, precision=exact))
    back = jnp.concatenate([owner_part] + slot_parts, axis=1)
    returned = lax.all_to_all(back, ("macro", "work"), 0, 0, tiled=True)
    row_ids = jnp.arange(points, dtype=jnp.float32) + 1.0
    mine = (returned[None, :, 36] == row_ids[:, None]).astype(jnp.float32)
    chosen = jnp.dot(mine, returned[:, :36], precision=exact)
    tangent = jnp.where(active[:, None], chosen, tangent_old)
    solved = jnp.stack(
        [jnp.sum(returned[:, 37 + 36 * s : 37 + 36 * (s + 1)], axis=0) for s in range(slots)]
    )
    return (tangent, solved)


def solution(mesh):
    return jax.shard_map(
        body,
        mesh=mesh,
        in_specs=(
            P(("macro", "work"), None),
            P(("macro", "work"), None, None),
            P(("macro", "work")),
            P(("macro", "work")),
            P(),
            P(),
            P(("macro", "work"), None),
        ),
        out_specs=(P(("macro", "work"), None), P(("macro", "work"), None)),
        check_vma=False,
    )
```
